32 devices in a mesh: region: 8 (over z, x), sub: 4 (over y, core).
Axes of the slice: x: 2, y: 2, z: 4, core: 2. Of those that a mesh axis runs over, the one named last changes fastest.
Arguments:
- waves: bfloat16 [128, 3, 400, 128], P(('region', 'sub')), may hold values from -170 to 170
- local_event: int32 [512, 2], P(('region', 'sub')), may hold values from 0 to 3
- partner_event: int32 [512, 2], P(('region', 'sub')), may hold values from 0 to 15
- station_mask: int32 [512, 2, 128], P(('region', 'sub')), may hold values 0 or 1
Outputs:
- correlation: float32 [512, 2, 101, 128], P(('region', 'sub'))
The draws below stay inside these ranges and needn't reach their ends.
All inputs are finite; a program needn't handle non-finite values. No bound on the sum of `station_mask` on one device may be relied on, other than what follows from the above.
Results may differ from the reference program's by a relative error of at most 0.0028.
Values may be sent and summed in bfloat16 or wider, within the bound.
No kernel may reach another device: no remote copies, remote signals or barrier semaphores. Data moves between devices by JAX's collectives and lax.ppermute only.
A program may use at most 128 MiB of HBM per device.

```python
import math
import jax
import jax.numpy as jnp
from jax import lax

S = 128
SAMPLES = 400
LAG = 50
ROUNDS = 2
E_DEV = 4
PAIRS_DEV = 16
EVENTS = 128
PAIRS = 512
REGION_EVENTS = 16
N_REGION = 8
N_SUB = 4


def draw_waves(key, part):
    keys = jax.random.split(key, 4)
    reach = LAG // 2
    template = jnp.clip(jax.random.normal(keys[0], (3, SAMPLES + 2 * reach, S), jnp.float32), -4.0, 4.0)
    delays = jax.random.randint(keys[1], (EVENTS,), 0, 2 * reach + 1)
    positions = jnp.arange(SAMPLES, dtype=jnp.int32)[None, :] + delays[:, None]
    moved = jnp.transpose(template[:, positions, :], (1, 0, 2, 3))
    noise = jnp.clip(jax.random.normal(keys[2], (EVENTS, 3, SAMPLES, S), jnp.float32), -4.0, 4.0)
    spread = math.log(10.0)
    amplitude = jnp.exp(jax.random.uniform(keys[3], (EVENTS, 1, 1, S), jnp.float32, 0.0, spread))
    return (amplitude * (0.8 * moved + 0.6 * noise)).astype(jnp.bfloat16)


def set_ends(array, rng, smallest, high):
    longest = array.shape.index(max(array.shape))
    spots = []
    for shift in (0, 1):
        where = [jax.random.randint(jax.random.fold_in(rng, axis), (), 0, length) for axis, length in enumerate(array.shape)]
        where[longest] = (where[longest] + shift) % array.shape[longest]
        spots.append(tuple(where))
    return array.at[spots[0]].set(smallest).at[spots[1]].set(high)


def setup_inputs(seed: int = 0) -> dict:
    seeds = jax.random.split(jax.random.key(seed), 5)
    return {
        "waves": draw_waves(jax.random.fold_in(seeds[4], 71), 0),
        "local_event": set_ends(jax.random.randint(seeds[1], (PAIRS, ROUNDS), 0, E_DEV), jax.random.fold_in(seeds[1], 1), 0, E_DEV - 1).astype(jnp.int32),
        "partner_event": set_ends(jax.random.randint(seeds[2], (PAIRS, ROUNDS), 0, REGION_EVENTS), jax.random.fold_in(seeds[2], 1), 0, REGION_EVENTS - 1).astype(jnp.int32),
        "station_mask": set_ends((jax.random.randint(seeds[3], (PAIRS, ROUNDS, S), 0, 4) < 3).astype(jnp.int32), jax.random.fold_in(seeds[3], 1), 0, 1),
    }


def cross_lags(own_spec, far_spec):
    product = lax.optimization_barrier(jnp.sum(jnp.conj(own_spec) * far_spec, axis=1))
    series = jnp.fft.irfft(product, n=SAMPLES, axis=1)
    return jnp.concatenate([series[:, SAMPLES - LAG:], series[:, :LAG + 1]], axis=1)

def rounded_spectrum(partners):
    spec = jnp.fft.rfft(partners, axis=2)
    real_part = lax.optimization_barrier(jnp.real(spec).astype(jnp.bfloat16)).astype(jnp.float32)
    imag_part = lax.optimization_barrier(jnp.imag(spec).astype(jnp.bfloat16)).astype(jnp.float32)
    return real_part + 1j * imag_part

def reference(waves, local_event, partner_event, station_mask):
    devices = N_REGION * N_SUB
    grouped = waves.reshape(N_REGION, E_DEV * N_SUB, 3, SAMPLES, S)
    own_rows = local_event.reshape(devices, PAIRS_DEV, ROUNDS)
    far_rows = partner_event.reshape(devices, PAIRS_DEV, ROUNDS)
    station_masks = station_mask.reshape(devices, PAIRS_DEV, ROUNDS, S)
    sample_index = jnp.arange(SAMPLES)
    window = ((sample_index >= LAG) & (sample_index < SAMPLES - LAG)).astype(jnp.float32)

    def device_pairs(device):
        region = device // N_SUB
        sub_index = device % N_SUB
        region_block = lax.dynamic_index_in_dim(grouped, region, 0, keepdims=False).astype(jnp.float32)
        before = lax.dynamic_index_in_dim(grouped, (region + N_REGION - 1) % N_REGION, 0, keepdims=False).astype(jnp.float32)
        own_window = lax.dynamic_slice_in_dim(region_block, (sub_index * E_DEV).astype(jnp.int32), E_DEV, 0)
        own_window = own_window * window[None, None, :, None]
        own_energy = lax.optimization_barrier(jnp.sum(own_window * own_window, axis=(1, 2)))
        own_spec = jnp.fft.rfft(own_window, axis=2)
        results = []
        for current, partners in enumerate((region_block, before)):
            partner_energy = lax.optimization_barrier(jnp.sum(partners * partners, axis=(1, 2)))
            partner_spec = rounded_spectrum(partners)
            own_pick = own_rows[device, :, current]
            far_pick = far_rows[device, :, current]
            shifted = cross_lags(own_spec[own_pick], partner_spec[far_pick])
            denominator = jnp.sqrt(own_energy[own_pick] * partner_energy[far_pick] + 1e-06)
            gate_rows = station_masks[device, :, current].astype(jnp.float32)
            results.append(shifted / denominator[:, None, :] * gate_rows[:, None, :])
        return jnp.stack(results, axis=1)
    stacked = lax.map(device_pairs, jnp.arange(devices, dtype=jnp.int32))
    return stacked.reshape(devices * PAIRS_DEV, ROUNDS, 2 * LAG + 1, S)
```

```python
import math

import jax
import jax.numpy as jnp
from jax import lax
from jax.experimental import pallas as pl
from jax.experimental.pallas import tpu as pltpu
from jax.sharding import PartitionSpec as P

LAG = 50


def forward_table(samples):
    half = samples // 2
    sample_index = jnp.arange(samples, dtype=jnp.int32)
    orders = jnp.arange(half, dtype=jnp.int32)
    turn = 2.0 * math.pi / samples
    phase = (orders[:, None] * sample_index[None, :] % samples).astype(jnp.float32) * turn
    top = (half * sample_index % samples).astype(jnp.float32) * turn
    lower = jnp.concatenate([jnp.cos(top)[None, :], -jnp.sin(phase[1:])], axis=0)
    return jnp.concatenate([jnp.cos(phase), lower], axis=0)


def inverse_table(samples, reach):
    half = samples // 2
    orders = jnp.arange(half, dtype=jnp.int32)
    offsets = (jnp.arange(2 * reach + 1, dtype=jnp.int32) - reach + samples) % samples
    phase = (offsets[:, None] * orders[None, :] % samples).astype(jnp.float32) * (
        2.0 * math.pi / samples
    )
    parity = jnp.where(offsets % 2 == 0, 1.0, -1.0).astype(jnp.float32)
    scale = 2.0 / samples
    even = ((1.0 + parity) / (2.0 * samples))[:, None]
    odd = ((1.0 - parity) / (2.0 * samples))[:, None]
    cos_part = jnp.concatenate([even, scale * jnp.cos(phase[:, 1:])], axis=1)
    sin_part = jnp.concatenate([odd, -scale * jnp.sin(phase[:, 1:])], axis=1)
    table = jnp.concatenate([cos_part, sin_part], axis=1)
    rows = -(-table.shape[0] // 8) * 8
    return jnp.pad(table, ((0, rows - table.shape[0]), (0, 0)))


def split_exact(value):
    hi = lax.reduce_precision(value, exponent_bits=8, mantissa_bits=7)
    rest = value - hi
    mid = lax.reduce_precision(rest, exponent_bits=8, mantissa_bits=7)
    low = rest - mid
    return jnp.stack([hi, mid, low], axis=1).astype(jnp.bfloat16)


def correlate_kernel(a_ref, b_ref, own_ref, part_ref, inv_ref, den_ref, mask_ref, *rest):
    out_ref = rest[-2]
    x_ref = rest[-1]
    q = pl.program_id(0)
    ai = a_ref[q]
    comps = own_ref.shape[1]
    samples = own_ref.shape[2]
    half = samples // 2
    lags = out_ref.shape[2]
    u = None
    v = None
    w = None
    for c in range(comps):
        own = own_ref[ai, c]
        far = part_ref[0, c * samples:(c + 1) * samples, :].astype(jnp.float32)
        oa = own[:half]
        ob = own[half:]
        fa = far[:half]
        fb = far[half:]
        uc = oa * fa + ob * fb
        vc = oa * fb - ob * fa
        wc = oa[:8] * fa[:8] - ob[:8] * fb[:8]
        u = uc if u is None else u + uc
        v = vc if v is None else v + vc
        w = wc if w is None else w + wc
    first = lax.broadcasted_iota(jnp.int32, w.shape, 0) == 0
    x_ref[:half, :] = u
    x_ref[half:, :] = v
    x_ref[half:half + 8, :] = jnp.where(first, w, v[:8])
    raw = jnp.dot(
        inv_ref[...], x_ref[...], precision=lax.Precision.HIGHEST,
        preferred_element_type=jnp.float32,
    )
    out_ref[0, 0] = raw[:lags] / den_ref[0] * mask_ref[0]


def correlate_round(own_spec, partners, inverse, denom, mask, own_pick, far_pick, rnd, rounds, prior):
    count = own_pick.shape[0]
    events, comps, samples, stations = own_spec.shape
    rows = partners.shape[1]
    lags = 2 * LAG + 1
    in_specs = [
        pl.BlockSpec((events, comps, samples, stations), lambda q, a, b: (0, 0, 0, 0)),
        pl.BlockSpec((1, rows, stations), lambda q, a, b: (b[q], 0, 0)),
        pl.BlockSpec(inverse.shape, lambda q, a, b: (0, 0)),
        pl.BlockSpec((1, 1, stations), lambda q, a, b: (q, 0, 0)),
        pl.BlockSpec((1, 1, stations), lambda q, a, b: (q, 0, 0)),
    ]
    operands = [own_spec, partners, inverse, denom, mask]
    aliases = {}
    if prior is not None:
        in_specs.append(pl.BlockSpec(memory_space=pl.ANY))
        operands.append(prior)
        aliases = {2 + len(operands) - 1: 0}
    grid_spec = pltpu.PrefetchScalarGridSpec(
        num_scalar_prefetch=2,
        grid=(count,),
        in_specs=in_specs,
        out_specs=pl.BlockSpec((1, 1, lags, stations), lambda q, a, b: (q, rnd, 0, 0)),
        scratch_shapes=[pltpu.VMEM((samples, stations), jnp.float32)],
    )
    return pl.pallas_call(
        correlate_kernel,
        grid_spec=grid_spec,
        out_shape=jax.ShapeDtypeStruct((count, rounds, lags, stations), jnp.float32),
        input_output_aliases=aliases,
        compiler_params=pltpu.CompilerParams(dimension_semantics=("arbitrary",)),
    )(own_pick, far_pick, *operands)


def shards(waves, local_event, partner_event, station_mask):
    events, comps, samples, stations = waves.shape
    rounds = local_event.shape[1]
    forward = forward_table(samples)
    inverse = inverse_table(samples, LAG)

    wide = waves.astype(jnp.float32)
    spec = jnp.einsum("jt,ects->ecjs", forward, wide, precision=lax.Precision.HIGH)
    full_energy = jnp.sum(wide * wide, axis=(1, 2))
    sample_index = jnp.arange(samples, dtype=jnp.int32)
    window = ((sample_index >= LAG) & (sample_index < samples - LAG)).astype(jnp.float32)
    own_window = wide * window[None, None, :, None]
    own_energy = jnp.sum(own_window * own_window, axis=(1, 2))
    own_spec = jnp.einsum(
        "jt,ects->ecjs", forward[:, LAG:samples - LAG], wide[:, :, LAG:samples - LAG, :],
        precision=lax.Precision.HIGH,
    )

    body = spec.astype(jnp.bfloat16).reshape(events, comps * samples, stations)
    pieces = split_exact(full_energy)
    pad = 16 - pieces.shape[1]
    tail = jnp.pad(pieces, ((0, 0), (0, pad), (0, 0)))
    packed = jnp.concatenate([body, tail], axis=1)

    region_len = lax.axis_size("region")
    home = lax.all_gather(packed, "sub", axis=0, tiled=True)
    far_part = lax.ppermute(
        packed, "region", [(i, (i + 1) % region_len) for i in range(region_len)]
    )
    far = lax.all_gather(far_part, "sub", axis=0, tiled=True)

    out = None
    body_rows = comps * samples
    for rnd, partners in enumerate((home, far)):
        energy = jnp.sum(partners[:, body_rows:body_rows + 3, :].astype(jnp.float32), axis=1)
        own_pick = jnp.clip(local_event[:, rnd], 0, events - 1)
        far_pick = jnp.clip(partner_event[:, rnd], 0, partners.shape[0] - 1)
        denom = jnp.sqrt(
            jnp.take(own_energy, own_pick, axis=0) * jnp.take(energy, far_pick, axis=0) + 1e-06
        )
        mask = station_mask[:, rnd].astype(jnp.float32)
        out = correlate_round(
            own_spec, partners, inverse, denom[:, None, :], mask[:, None, :],
            own_pick, far_pick, rnd, rounds, out,
        )
    return out


def solution(mesh):
    placed = (
        P(("region", "sub"), None, None, None),
        P(("region", "sub"), None),
        P(("region", "sub"), None),
        P(("region", "sub"), None, None),
    )
    return jax.shard_map(
        shards,
        mesh=mesh,
        in_specs=placed,
        out_specs=P(("region", "sub"), None, None, None),
        check_vma=False,
    )
```

```python
import math

import jax
import jax.numpy as jnp
from jax import lax
from jax.experimental import pallas as pl
from jax.experimental.pallas import tpu as pltpu
from jax.sharding import PartitionSpec as P

LAG = 50


def forward_table(samples):
    half = samples // 2
    sample_index = jnp.arange(samples, dtype=jnp.int32)
    orders = jnp.arange(half, dtype=jnp.int32)
    turn = 2.0 * math.pi / samples
    phase = (orders[:, None] * sample_index[None, :] % samples).astype(jnp.float32) * turn
    top = (half * sample_index % samples).astype(jnp.float32) * turn
    lower = jnp.concatenate([jnp.cos(top)[None, :], -jnp.sin(phase[1:])], axis=0)
    return jnp.concatenate([jnp.cos(phase), lower], axis=0)


def inverse_table(samples, reach):
    half = samples // 2
    orders = jnp.arange(half, dtype=jnp.int32)
    offsets = (jnp.arange(2 * reach + 1, dtype=jnp.int32) - reach + samples) % samples
    phase = (offsets[:, None] * orders[None, :] % samples).astype(jnp.float32) * (
        2.0 * math.pi / samples
    )
    parity = jnp.where(offsets % 2 == 0, 1.0, -1.0).astype(jnp.float32)
    scale = 2.0 / samples
    even = ((1.0 + parity) / (2.0 * samples))[:, None]
    odd = ((1.0 - parity) / (2.0 * samples))[:, None]
    cos_part = jnp.concatenate([even, scale * jnp.cos(phase[:, 1:])], axis=1)
    sin_part = jnp.concatenate([odd, -scale * jnp.sin(phase[:, 1:])], axis=1)
    table = jnp.concatenate([cos_part, sin_part], axis=1)
    rows = -(-table.shape[0] // 8) * 8
    return jnp.pad(table, ((0, rows - table.shape[0]), (0, 0)))


def split_exact(value):
    hi = lax.reduce_precision(value, exponent_bits=8, mantissa_bits=7)
    rest = value - hi
    mid = lax.reduce_precision(rest, exponent_bits=8, mantissa_bits=7)
    low = rest - mid
    return jnp.stack([hi, mid, low], axis=1).astype(jnp.bfloat16)


def correlate_kernel(a_ref, b_ref, own_ref, part_ref, inv_ref, den_ref, mask_ref, *rest):
    out_ref = rest[-2]
    x_ref = rest[-1]
    q = pl.program_id(0)
    ai = a_ref[q]
    comps = own_ref.shape[1]
    samples = own_ref.shape[2]
    half = samples // 2
    lags = out_ref.shape[2]
    u = None
    v = None
    w = None
    for c in range(comps):
        own = own_ref[ai, c]
        far = part_ref[0, c * samples:(c + 1) * samples, :].astype(jnp.float32)
        oa = own[:half]
        ob = own[half:]
        fa = far[:half]
        fb = far[half:]
        uc = oa * fa + ob * fb
        vc = oa * fb - ob * fa
        wc = oa[:8] * fa[:8] - ob[:8] * fb[:8]
        u = uc if u is None else u + uc
        v = vc if v is None else v + vc
        w = wc if w is None else w + wc
    first = lax.broadcasted_iota(jnp.int32, w.shape, 0) == 0
    x_ref[:half, :] = u
    x_ref[half:, :] = v
    x_ref[half:half + 8, :] = jnp.where(first, w, v[:8])
    raw = jnp.dot(
        inv_ref[...], x_ref[...], precision=lax.Precision.HIGHEST,
        preferred_element_type=jnp.float32,
    )
    out_ref[0, 0] = raw[:lags] / den_ref[0] * mask_ref[0]


def correlate_round(own_spec, partners, inverse, denom, mask, own_pick, far_pick):
    count = own_pick.shape[0]
    events, comps, samples, stations = own_spec.shape
    rows = partners.shape[1]
    lags = 2 * LAG + 1
    in_specs = [
        pl.BlockSpec((events, comps, samples, stations), lambda q, a, b: (0, 0, 0, 0)),
        pl.BlockSpec((1, rows, stations), lambda q, a, b: (b[q], 0, 0)),
        pl.BlockSpec(inverse.shape, lambda q, a, b: (0, 0)),
        pl.BlockSpec((1, 1, stations), lambda q, a, b: (q, 0, 0)),
        pl.BlockSpec((1, 1, stations), lambda q, a, b: (q, 0, 0)),
    ]
    grid_spec = pltpu.PrefetchScalarGridSpec(
        num_scalar_prefetch=2,
        grid=(count,),
        in_specs=in_specs,
        out_specs=pl.BlockSpec((1, 1, lags, stations), lambda q, a, b: (q, 0, 0, 0)),
        scratch_shapes=[pltpu.VMEM((samples, stations), jnp.float32)],
    )
    return pl.pallas_call(
        correlate_kernel,
        grid_spec=grid_spec,
        out_shape=jax.ShapeDtypeStruct((count, 1, lags, stations), jnp.float32),
        compiler_params=pltpu.CompilerParams(dimension_semantics=("arbitrary",)),
    )(own_pick, far_pick, own_spec, partners, inverse, denom, mask)


def spectra(forward, wide):
    samples = forward.shape[1]
    return jnp.einsum(
        "jt,ects->ecjs", forward[:, LAG:samples - LAG], wide, precision=lax.Precision.HIGH
    )


def by_xor(value, axis, flip):
    length = lax.axis_size(axis)
    return lax.ppermute(value, axis, [(i, i ^ flip) for i in range(length)])


def shards(waves, local_event, partner_event, station_mask):
    events, comps, samples, stations = waves.shape
    forward = forward_table(samples)
    inverse = inverse_table(samples, LAG)
    region_len = lax.axis_size("region")
    sub_at = lax.axis_index("sub")

    inner = waves[:, :, LAG:samples - LAG, :]
    meta = jnp.concatenate(
        [station_mask[:, 1], local_event[:, 1:2], partner_event[:, 1:2]], axis=1
    )
    sent_inner, sent_meta = lax.ppermute(
        (inner, meta), "region", [(i, (i - 1) % region_len) for i in range(region_len)]
    )

    wide = waves.astype(jnp.float32)
    spec = jnp.einsum("jt,ects->ecjs", forward, wide, precision=lax.Precision.HIGH)
    full_energy = jnp.sum(wide * wide, axis=(1, 2))
    body = spec.astype(jnp.bfloat16).reshape(events, comps * samples, stations)
    pieces = split_exact(full_energy)
    tail = jnp.pad(pieces, ((0, 0), (0, 16 - pieces.shape[1]), (0, 0)))
    packed = jnp.concatenate([body, tail], axis=1)

    near = by_xor(packed, "sub", 1)
    across = by_xor(packed, "sub", 2)
    corner = by_xor(across, "sub", 1)
    home = jnp.concatenate([packed, near, across, corner], axis=0)
    body_rows = comps * samples
    home_energy = jnp.sum(home[:, body_rows:body_rows + 3, :].astype(jnp.float32), axis=1)

    def local_index(pick):
        pick = jnp.clip(pick, 0, home.shape[0] - 1)
        return jnp.bitwise_xor(pick // events, sub_at) * events + pick % events

    def run(own_inner, own_pick, far_pick, mask):
        own_wide = own_inner.astype(jnp.float32)
        own_spec = spectra(forward, own_wide)
        own_energy = jnp.sum(own_wide * own_wide, axis=(1, 2))
        own_pick = jnp.clip(own_pick, 0, events - 1)
        far_pick = local_index(far_pick)
        denom = jnp.sqrt(
            jnp.take(own_energy, own_pick, axis=0) * jnp.take(home_energy, far_pick, axis=0)
            + 1e-06
        )
        return correlate_round(
            own_spec, home, inverse, denom[:, None, :],
            mask.astype(jnp.float32)[:, None, :], own_pick, far_pick,
        )

    ahead = run(sent_inner, sent_meta[:, stations], sent_meta[:, stations + 1],
                sent_meta[:, :stations])
    back = lax.ppermute(ahead, "region", [(i, (i + 1) % region_len) for i in range(region_len)])
    mine = run(inner, local_event[:, 0], partner_event[:, 0], station_mask[:, 0])
    return jnp.concatenate([mine, back], axis=1)


def solution(mesh):
    placed = (
        P(("region", "sub"), None, None, None),
        P(("region", "sub"), None),
        P(("region", "sub"), None),
        P(("region", "sub"), None, None),
    )
    return jax.shard_map(
        shards,
        mesh=mesh,
        in_specs=placed,
        out_specs=P(("region", "sub"), None, None, None),
        check_vma=False,
    )
```

```python
import math

import jax
import jax.numpy as jnp
from jax import lax
from jax.experimental import pallas as pl
from jax.experimental.pallas import tpu as pltpu
from jax.sharding import PartitionSpec as P

LAG = 50


def forward_table(samples):
    half = samples // 2
    sample_index = jnp.arange(samples, dtype=jnp.int32)
    orders = jnp.arange(half, dtype=jnp.int32)
    turn = 2.0 * math.pi / samples
    phase = (orders[:, None] * sample_index[None, :] % samples).astype(jnp.float32) * turn
    top = (half * sample_index % samples).astype(jnp.float32) * turn
    lower = jnp.concatenate([jnp.cos(top)[None, :], -jnp.sin(phase[1:])], axis=0)
    return jnp.concatenate([jnp.cos(phase), lower], axis=0)


def inverse_table(samples, reach):
    half = samples // 2
    orders = jnp.arange(half, dtype=jnp.int32)
    offsets = (jnp.arange(2 * reach + 1, dtype=jnp.int32) - reach + samples) % samples
    phase = (offsets[:, None] * orders[None, :] % samples).astype(jnp.float32) * (
        2.0 * math.pi / samples
    )
    parity = jnp.where(offsets % 2 == 0, 1.0, -1.0).astype(jnp.float32)
    scale = 2.0 / samples
    even = ((1.0 + parity) / (2.0 * samples))[:, None]
    odd = ((1.0 - parity) / (2.0 * samples))[:, None]
    cos_part = jnp.concatenate([even, scale * jnp.cos(phase[:, 1:])], axis=1)
    sin_part = jnp.concatenate([odd, -scale * jnp.sin(phase[:, 1:])], axis=1)
    table = jnp.concatenate([cos_part, sin_part], axis=1)
    rows = -(-table.shape[0] // 8) * 8
    return jnp.pad(table, ((0, rows - table.shape[0]), (0, 0)))


def split_exact(value):
    hi = lax.reduce_precision(value, exponent_bits=8, mantissa_bits=7)
    rest = value - hi
    mid = lax.reduce_precision(rest, exponent_bits=8, mantissa_bits=7)
    low = rest - mid
    return jnp.stack([hi, mid, low], axis=1).astype(jnp.bfloat16)


def product_kernel(a_ref, k_ref, sel_ref, own_ref, *rest):
    part_refs = rest[:-1]
    out_ref = rest[-1]
    q = pl.program_id(0)
    ai = a_ref[q]
    ki = k_ref[q]
    comps = own_ref.shape[1]
    samples = own_ref.shape[2]
    half = samples // 2

    def product(part_ref):
        u = None
        v = None
        w = None
        for c in range(comps):
            own = own_ref[ai, c]
            far = part_ref[0, c * samples:(c + 1) * samples, :].astype(jnp.float32)
            oa = own[:half]
            ob = own[half:]
            fa = far[:half]
            fb = far[half:]
            uc = oa * fa + ob * fb
            vc = oa * fb - ob * fa
            wc = oa[:8] * fa[:8] - ob[:8] * fb[:8]
            u = uc if u is None else u + uc
            v = vc if v is None else v + vc
            w = wc if w is None else w + wc
        first = lax.broadcasted_iota(jnp.int32, w.shape, 0) == 0
        out_ref[0, :half, :] = u
        out_ref[0, half:, :] = v
        out_ref[0, half:half + 8, :] = jnp.where(first, w, v[:8])

    for j, part_ref in enumerate(part_refs):
        pl.when(ki == j)(lambda part_ref=part_ref: product(part_ref))


def last_use(piece, event, which):
    count = piece.shape[0]
    order = jnp.arange(count, dtype=jnp.int32)
    hits = piece == which
    latest = lax.cummax(jnp.where(hits, order, -1), axis=0)
    first = jnp.min(jnp.where(hits, order, count - 1))
    at = jnp.where(latest >= 0, latest, first)
    return jnp.take(event, at, axis=0)


def correlate_round(own_spec, pieces, inverse, denom, mask, own_pick, piece_pick, event_pick):
    count = own_pick.shape[0]
    events, comps, samples, stations = own_spec.shape
    rows = pieces[0].shape[1]
    lags = 2 * LAG + 1
    select = jnp.concatenate(
        [last_use(piece_pick, event_pick, j) for j in range(len(pieces))], axis=0
    )
    in_specs = [pl.BlockSpec((events, comps, samples, stations), lambda q, a, k, s: (0, 0, 0, 0))]
    for j in range(len(pieces)):
        in_specs.append(
            pl.BlockSpec((1, rows, stations), lambda q, a, k, s, j=j: (s[j * count + q], 0, 0))
        )
    grid_spec = pltpu.PrefetchScalarGridSpec(
        num_scalar_prefetch=3,
        grid=(count,),
        in_specs=in_specs,
        out_specs=pl.BlockSpec((1, samples, stations), lambda q, a, k, s: (q, 0, 0)),
    )
    packed = pl.pallas_call(
        product_kernel,
        grid_spec=grid_spec,
        out_shape=jax.ShapeDtypeStruct((count, samples, stations), jnp.float32),
        compiler_params=pltpu.CompilerParams(dimension_semantics=("arbitrary",)),
    )(own_pick, piece_pick, select, own_spec, *pieces)
    raw = jnp.einsum("jk,qks->qjs", inverse[:lags], packed, precision=lax.Precision.HIGH)
    return raw / denom[:, None, :] * mask[:, None, :]


def spectra(forward, wide):
    samples = forward.shape[1]
    return jnp.einsum(
        "jt,ects->ecjs", forward[:, LAG:samples - LAG], wide, precision=lax.Precision.HIGH
    )


def by_xor(value, axis, flip):
    length = lax.axis_size(axis)
    return lax.ppermute(value, axis, [(i, i ^ flip) for i in range(length)])


def shards(waves, local_event, partner_event, station_mask):
    events, comps, samples, stations = waves.shape
    forward = forward_table(samples)
    inverse = inverse_table(samples, LAG)
    region_len = lax.axis_size("region")
    sub_at = lax.axis_index("sub")

    inner = waves[:, :, LAG:samples - LAG, :]
    meta = jnp.concatenate(
        [station_mask[:, 1], local_event[:, 1:2], partner_event[:, 1:2]], axis=1
    )
    sent_inner, sent_meta = lax.ppermute(
        (inner, meta), "region", [(i, (i - 1) % region_len) for i in range(region_len)]
    )

    wide = waves.astype(jnp.float32)
    spec = jnp.einsum("jt,ects->ecjs", forward, wide, precision=lax.Precision.HIGH)
    full_energy = jnp.sum(wide * wide, axis=(1, 2))
    body = spec.astype(jnp.bfloat16).reshape(events, comps * samples, stations)
    pieces = split_exact(full_energy)
    tail = jnp.pad(pieces, ((0, 0), (0, 16 - pieces.shape[1]), (0, 0)))
    packed = jnp.concatenate([body, tail], axis=1)

    near = by_xor(packed, "sub", 1)
    across = by_xor(packed, "sub", 2)
    corner = by_xor(across, "sub", 1)
    pieces = (packed, near, across, corner)
    body_rows = comps * samples
    home_energy = jnp.concatenate(
        [jnp.sum(p[:, body_rows:body_rows + 3, :].astype(jnp.float32), axis=1) for p in pieces],
        axis=0,
    )

    def run(own_inner, own_pick, far_pick, mask):
        own_wide = own_inner.astype(jnp.float32)
        own_spec = spectra(forward, own_wide)
        own_energy = jnp.sum(own_wide * own_wide, axis=(1, 2))
        own_pick = jnp.clip(own_pick, 0, events - 1)
        far_pick = jnp.clip(far_pick, 0, len(pieces) * events - 1)
        piece_pick = jnp.bitwise_xor(far_pick // events, sub_at)
        event_pick = far_pick % events
        denom = jnp.sqrt(
            jnp.take(own_energy, own_pick, axis=0)
            * jnp.take(home_energy, piece_pick * events + event_pick, axis=0)
            + 1e-06
        )
        return correlate_round(
            own_spec, pieces, inverse, denom, mask.astype(jnp.float32), own_pick,
            piece_pick, event_pick,
        )

    ahead = run(sent_inner, sent_meta[:, stations], sent_meta[:, stations + 1],
                sent_meta[:, :stations])
    back = lax.ppermute(ahead, "region", [(i, (i + 1) % region_len) for i in range(region_len)])
    mine = run(inner, local_event[:, 0], partner_event[:, 0], station_mask[:, 0])
    return jnp.stack([mine, back], axis=1)


def solution(mesh):
    placed = (
        P(("region", "sub"), None, None, None),
        P(("region", "sub"), None),
        P(("region", "sub"), None),
        P(("region", "sub"), None, None),
    )
    return jax.shard_map(
        shards,
        mesh=mesh,
        in_specs=placed,
        out_specs=P(("region", "sub"), None, None, None),
        check_vma=False,
    )
```

```python
import math

import jax
import jax.numpy as jnp
from jax import lax
from jax.experimental import pallas as pl
from jax.experimental.pallas import tpu as pltpu
from jax.sharding import PartitionSpec as P

LAG = 50


def forward_table(samples):
    half = samples // 2
    sample_index = jnp.arange(samples, dtype=jnp.int32)
    orders = jnp.arange(half, dtype=jnp.int32)
    turn = 2.0 * math.pi / samples
    phase = (orders[:, None] * sample_index[None, :] % samples).astype(jnp.float32) * turn
    top = (half * sample_index % samples).astype(jnp.float32) * turn
    lower = jnp.concatenate([jnp.cos(top)[None, :], -jnp.sin(phase[1:])], axis=0)
    return jnp.concatenate([jnp.cos(phase), lower], axis=0)


def inverse_table(samples, reach):
    half = samples // 2
    orders = jnp.arange(half, dtype=jnp.int32)
    offsets = (jnp.arange(2 * reach + 1, dtype=jnp.int32) - reach + samples) % samples
    phase = (offsets[:, None] * orders[None, :] % samples).astype(jnp.float32) * (
        2.0 * math.pi / samples
    )
    parity = jnp.where(offsets % 2 == 0, 1.0, -1.0).astype(jnp.float32)
    scale = 2.0 / samples
    even = ((1.0 + parity) / (2.0 * samples))[:, None]
    odd = ((1.0 - parity) / (2.0 * samples))[:, None]
    cos_part = jnp.concatenate([even, scale * jnp.cos(phase[:, 1:])], axis=1)
    sin_part = jnp.concatenate([odd, -scale * jnp.sin(phase[:, 1:])], axis=1)
    table = jnp.concatenate([cos_part, sin_part], axis=1)
    rows = -(-table.shape[0] // 8) * 8
    return jnp.pad(table, ((0, rows - table.shape[0]), (0, 0)))


def split_exact(value):
    hi = lax.reduce_precision(value, exponent_bits=8, mantissa_bits=7)
    rest = value - hi
    mid = lax.reduce_precision(rest, exponent_bits=8, mantissa_bits=7)
    low = rest - mid
    return jnp.stack([hi, mid, low], axis=1).astype(jnp.bfloat16)


def round_kernel(a_ref, b_ref, u_ref, own_ref, oen_ref, mask_ref, inv_ref, *rest):
    pieces = rest[:-4]
    out_ref, buf, sem, x_ref = rest[-4:]
    events, comps, samples, stations = own_ref.shape
    half = samples // 2
    body_rows = comps * samples
    count, lags = out_ref.shape[0], out_ref.shape[1]
    sub_at = u_ref[0]

    def start(q, slot):
        b = b_ref[q]
        piece = jnp.bitwise_xor(b // events, sub_at)
        event = b % events
        for j, source in enumerate(pieces):
            @pl.when(piece == j)
            def _():
                pltpu.make_async_copy(source.at[event], buf.at[slot], sem.at[slot]).start()

    start(0, 0)

    def step(q, carry):
        slot = q % 2

        @pl.when(q + 1 < count)
        def _():
            start(q + 1, 1 - slot)

        pltpu.make_async_copy(pieces[0].at[0], buf.at[slot], sem.at[slot]).wait()
        ai = a_ref[q]
        u = None
        v = None
        w = None
        for c in range(comps):
            own = own_ref[ai, c]
            far = buf[slot, c * samples:(c + 1) * samples, :].astype(jnp.float32)
            oa = own[:half]
            ob = own[half:]
            fa = far[:half]
            fb = far[half:]
            uc = oa * fa + ob * fb
            vc = oa * fb - ob * fa
            wc = oa[:8] * fa[:8] - ob[:8] * fb[:8]
            u = uc if u is None else u + uc
            v = vc if v is None else v + vc
            w = wc if w is None else w + wc
        first = lax.broadcasted_iota(jnp.int32, w.shape, 0) == 0
        x_ref[:half, :] = u
        x_ref[half:, :] = v
        x_ref[half:half + 8, :] = jnp.where(first, w, v[:8])
        raw = jnp.dot(
            inv_ref[...], x_ref[...], precision=lax.Precision.HIGHEST,
            preferred_element_type=jnp.float32,
        )
        energy = jnp.sum(buf[slot, body_rows:body_rows + 16, :].astype(jnp.float32), axis=0,
                         keepdims=True)
        denom = jnp.sqrt(oen_ref[ai] * energy + 1e-06)
        out_ref[q] = raw[:lags] / denom * mask_ref[q]
        return carry

    lax.fori_loop(0, count, step, 0)


def correlate_round(own_spec, own_energy, pieces, inverse, mask, own_pick, far_pick, sub_at):
    count = own_pick.shape[0]
    events, comps, samples, stations = own_spec.shape
    rows = pieces[0].shape[1]
    lags = 2 * LAG + 1
    smem = pl.BlockSpec(memory_space=pltpu.SMEM)
    vmem = pl.BlockSpec(memory_space=pltpu.VMEM)
    hbm = pl.BlockSpec(memory_space=pl.ANY)
    return pl.pallas_call(
        round_kernel,
        in_specs=[smem, smem, smem, vmem, vmem, vmem, vmem] + [hbm] * len(pieces),
        out_specs=vmem,
        out_shape=jax.ShapeDtypeStruct((count, lags, stations), jnp.float32),
        scratch_shapes=[
            pltpu.VMEM((2, rows, stations), pieces[0].dtype),
            pltpu.SemaphoreType.DMA((2,)),
            pltpu.VMEM((samples, stations), jnp.float32),
        ],
    )(own_pick, far_pick, sub_at, own_spec, own_energy[:, None, :], mask[:, None, :], inverse,
      *pieces)


def spectra(forward, wide):
    samples = forward.shape[1]
    return jnp.einsum(
        "jt,ects->ecjs", forward[:, LAG:samples - LAG], wide, precision=lax.Precision.HIGH
    )


def by_xor(value, axis, flip):
    length = lax.axis_size(axis)
    return lax.ppermute(value, axis, [(i, i ^ flip) for i in range(length)])


def shards(waves, local_event, partner_event, station_mask):
    events, comps, samples, stations = waves.shape
    forward = forward_table(samples)
    inverse = inverse_table(samples, LAG)
    region_len = lax.axis_size("region")
    sub_at = lax.axis_index("sub")

    inner = waves[:, :, LAG:samples - LAG, :]
    meta = jnp.concatenate(
        [station_mask[:, 1], local_event[:, 1:2], partner_event[:, 1:2]], axis=1
    )
    sent_inner, sent_meta = lax.ppermute(
        (inner, meta), "region", [(i, (i - 1) % region_len) for i in range(region_len)]
    )

    wide = waves.astype(jnp.float32)
    spec = jnp.einsum("jt,ects->ecjs", forward, wide, precision=lax.Precision.HIGH)
    full_energy = jnp.sum(wide * wide, axis=(1, 2))
    body = spec.astype(jnp.bfloat16).reshape(events, comps * samples, stations)
    pieces = split_exact(full_energy)
    tail = jnp.pad(pieces, ((0, 0), (0, 16 - pieces.shape[1]), (0, 0)))
    packed = jnp.concatenate([body, tail], axis=1)

    near = by_xor(packed, "sub", 1)
    across = by_xor(packed, "sub", 2)
    corner = by_xor(across, "sub", 1)
    pieces = (packed, near, across, corner)
    sub_vec = jnp.full((1,), sub_at, jnp.int32)

    def run(own_inner, own_pick, far_pick, mask):
        own_wide = own_inner.astype(jnp.float32)
        own_spec = spectra(forward, own_wide)
        own_energy = jnp.sum(own_wide * own_wide, axis=(1, 2))
        own_pick = jnp.clip(own_pick, 0, events - 1)
        far_pick = jnp.clip(far_pick, 0, len(pieces) * events - 1)
        return correlate_round(
            own_spec, own_energy, pieces, inverse, mask.astype(jnp.float32), own_pick,
            far_pick, sub_vec,
        )

    ahead_pick = sent_meta[:, stations]
    ahead_far = sent_meta[:, stations + 1]
    ahead_mask = sent_meta[:, :stations]
    count = ahead_pick.shape[0]
    split = count // 2
    back = []
    for lo, hi in ((0, split), (split, count)):
        part = run(sent_inner, ahead_pick[lo:hi], ahead_far[lo:hi], ahead_mask[lo:hi])
        back.append(
            lax.ppermute(part, "region", [(i, (i + 1) % region_len) for i in range(region_len)])
        )
    mine = run(inner, local_event[:, 0], partner_event[:, 0], station_mask[:, 0])
    return jnp.stack([mine, jnp.concatenate(back, axis=0)], axis=1)


def solution(mesh):
    placed = (
        P(("region", "sub"), None, None, None),
        P(("region", "sub"), None),
        P(("region", "sub"), None),
        P(("region", "sub"), None, None),
    )
    return jax.shard_map(
        shards,
        mesh=mesh,
        in_specs=placed,
        out_specs=P(("region", "sub"), None, None, None),
        check_vma=False,
    )
```

```python
import functools
import math

import jax
import jax.numpy as jnp
from jax import lax
from jax.experimental import pallas as pl
from jax.experimental.pallas import tpu as pltpu
from jax.sharding import PartitionSpec as P

LAG = 50


def forward_table(samples):
    half = samples // 2
    sample_index = jnp.arange(samples, dtype=jnp.int32)
    orders = jnp.arange(half, dtype=jnp.int32)
    turn = 2.0 * math.pi / samples
    phase = (orders[:, None] * sample_index[None, :] % samples).astype(jnp.float32) * turn
    top = (half * sample_index % samples).astype(jnp.float32) * turn
    lower = jnp.concatenate([jnp.cos(top)[None, :], -jnp.sin(phase[1:])], axis=0)
    return jnp.concatenate([jnp.cos(phase), lower], axis=0)


def inverse_table(samples, reach):
    half = samples // 2
    orders = jnp.arange(half, dtype=jnp.int32)
    offsets = (jnp.arange(2 * reach + 1, dtype=jnp.int32) - reach + samples) % samples
    phase = (offsets[:, None] * orders[None, :] % samples).astype(jnp.float32) * (
        2.0 * math.pi / samples
    )
    parity = jnp.where(offsets % 2 == 0, 1.0, -1.0).astype(jnp.float32)
    scale = 2.0 / samples
    even = ((1.0 + parity) / (2.0 * samples))[:, None]
    odd = ((1.0 - parity) / (2.0 * samples))[:, None]
    cos_part = jnp.concatenate([even, scale * jnp.cos(phase[:, 1:])], axis=1)
    sin_part = jnp.concatenate([odd, -scale * jnp.sin(phase[:, 1:])], axis=1)
    table = jnp.concatenate([cos_part, sin_part], axis=1)
    rows = -(-table.shape[0] // 8) * 8
    return jnp.pad(table, ((0, rows - table.shape[0]), (0, 0)))


def split_exact(value):
    hi = lax.reduce_precision(value, exponent_bits=8, mantissa_bits=7)
    rest = value - hi
    mid = lax.reduce_precision(rest, exponent_bits=8, mantissa_bits=7)
    low = rest - mid
    return jnp.stack([hi, mid, low], axis=1).astype(jnp.bfloat16)


def round_kernel(allowed, a_ref, b_ref, u_ref, own_ref, oen_ref, mask_ref, inv_ref, *rest):
    pieces = rest[:-4]
    out_ref, buf, sem, x_ref = rest[-4:]
    events, comps, samples, stations = own_ref.shape
    half = samples // 2
    body_rows = comps * samples
    count, lags = out_ref.shape[0], out_ref.shape[1]
    sub_at = u_ref[0]

    def piece_of(q):
        return jnp.bitwise_xor(b_ref[q] // events, sub_at)

    def wanted(q):
        piece = piece_of(q)
        hit = piece == allowed[0]
        for j in allowed[1:]:
            hit = hit | (piece == j)
        return hit

    def start(q, slot):
        piece = piece_of(q)
        event = b_ref[q] % events
        for j, source in zip(allowed, pieces):
            @pl.when(piece == j)
            def _():
                pltpu.make_async_copy(source.at[event], buf.at[slot], sem.at[slot]).start()

    start(0, 0)

    def step(q, carry):
        slot = q % 2

        @pl.when(q + 1 < count)
        def _():
            start(q + 1, 1 - slot)

        @pl.when(wanted(q))
        def _():
            work(q, slot)

        @pl.when(jnp.logical_not(wanted(q)))
        def _():
            out_ref[q] = jnp.zeros((lags, stations), jnp.float32)

        return carry

    def work(q, slot):
        pltpu.make_async_copy(pieces[0].at[0], buf.at[slot], sem.at[slot]).wait()
        ai = a_ref[q]
        u = None
        v = None
        w = None
        for c in range(comps):
            own = own_ref[ai, c]
            far = buf[slot, c * samples:(c + 1) * samples, :].astype(jnp.float32)
            oa = own[:half]
            ob = own[half:]
            fa = far[:half]
            fb = far[half:]
            uc = oa * fa + ob * fb
            vc = oa * fb - ob * fa
            wc = oa[:8] * fa[:8] - ob[:8] * fb[:8]
            u = uc if u is None else u + uc
            v = vc if v is None else v + vc
            w = wc if w is None else w + wc
        first = lax.broadcasted_iota(jnp.int32, w.shape, 0) == 0
        x_ref[:half, :] = u
        x_ref[half:, :] = v
        x_ref[half:half + 8, :] = jnp.where(first, w, v[:8])
        raw = jnp.dot(
            inv_ref[...], x_ref[...], precision=lax.Precision.HIGHEST,
            preferred_element_type=jnp.float32,
        )
        energy = jnp.sum(buf[slot, body_rows:body_rows + 16, :].astype(jnp.float32), axis=0,
                         keepdims=True)
        denom = jnp.sqrt(oen_ref[ai] * energy + 1e-06)
        out_ref[q] = raw[:lags] / denom * mask_ref[q]

    lax.fori_loop(0, count, step, 0)


def correlate_round(own_spec, own_energy, pieces, allowed, inverse, mask, own_pick, far_pick,
                    sub_at):
    count = own_pick.shape[0]
    events, comps, samples, stations = own_spec.shape
    rows = pieces[0].shape[1]
    lags = 2 * LAG + 1
    smem = pl.BlockSpec(memory_space=pltpu.SMEM)
    vmem = pl.BlockSpec(memory_space=pltpu.VMEM)
    hbm = pl.BlockSpec(memory_space=pl.ANY)
    return pl.pallas_call(
        functools.partial(round_kernel, allowed),
        in_specs=[smem, smem, smem, vmem, vmem, vmem, vmem] + [hbm] * len(pieces),
        out_specs=vmem,
        out_shape=jax.ShapeDtypeStruct((count, lags, stations), jnp.float32),
        cost_estimate=pl.CostEstimate(
            flops=count * 6 * 2 * 104 * samples * stations,
            transcendentals=count * stations,
            bytes_accessed=count * 8 * (rows + comps * samples) * stations,
        ),
        scratch_shapes=[
            pltpu.VMEM((2, rows, stations), pieces[0].dtype),
            pltpu.SemaphoreType.DMA((2,)),
            pltpu.VMEM((samples, stations), jnp.float32),
        ],
    )(own_pick, far_pick, sub_at, own_spec, own_energy[:, None, :], mask[:, None, :], inverse,
      *pieces)


def spectra(forward, wide):
    samples = forward.shape[1]
    return jnp.einsum(
        "jt,ects->ecjs", forward[:, LAG:samples - LAG], wide, precision=lax.Precision.HIGH
    )


def by_xor(value, axis, flip):
    length = lax.axis_size(axis)
    return lax.ppermute(value, axis, [(i, i ^ flip) for i in range(length)])


def shards(waves, local_event, partner_event, station_mask):
    events, comps, samples, stations = waves.shape
    forward = forward_table(samples)
    inverse = inverse_table(samples, LAG)
    region_len = lax.axis_size("region")
    sub_at = lax.axis_index("sub")

    inner = waves[:, :, LAG:samples - LAG, :]
    meta = jnp.concatenate(
        [station_mask[:, 1], local_event[:, 1:2], partner_event[:, 1:2]], axis=1
    )
    sent_inner, sent_meta = lax.ppermute(
        (inner, meta), "region", [(i, (i - 1) % region_len) for i in range(region_len)]
    )

    wide = waves.astype(jnp.float32)
    spec = jnp.einsum("jt,ects->ecjs", forward, wide, precision=lax.Precision.HIGH)
    full_energy = jnp.sum(wide * wide, axis=(1, 2))
    body = spec.astype(jnp.bfloat16).reshape(events, comps * samples, stations)
    pieces = split_exact(full_energy)
    tail = jnp.pad(pieces, ((0, 0), (0, 16 - pieces.shape[1]), (0, 0)))
    packed = jnp.concatenate([body, tail], axis=1)

    near = by_xor(packed, "sub", 1)
    across = by_xor(packed, "sub", 2)
    pieces = [packed, near, across, None]
    sub_vec = jnp.full((1,), sub_at, jnp.int32)

    def run(own_inner, own_pick, far_pick, mask, allowed=(0, 1, 2, 3)):
        own_wide = own_inner.astype(jnp.float32)
        own_spec = spectra(forward, own_wide)
        own_energy = jnp.sum(own_wide * own_wide, axis=(1, 2))
        own_pick = jnp.clip(own_pick, 0, events - 1)
        far_pick = jnp.clip(far_pick, 0, len(pieces) * events - 1)
        return correlate_round(
            own_spec, own_energy, tuple(pieces[j] for j in allowed), allowed, inverse,
            mask.astype(jnp.float32), own_pick, far_pick, sub_vec,
        )

    own_args = (inner, local_event[:, 0], partner_event[:, 0], station_mask[:, 0])
    mine = run(*own_args, allowed=(0, 1))
    across, mine = lax.optimization_barrier((across, mine))
    pieces[2] = across
    pieces[3] = by_xor(across, "sub", 1)
    mine = mine + run(*own_args, allowed=(2,))
    pieces[3], mine = lax.optimization_barrier((pieces[3], mine))

    ahead_pick = sent_meta[:, stations]
    ahead_far = sent_meta[:, stations + 1]
    ahead_mask = sent_meta[:, :stations]
    count = ahead_pick.shape[0]
    split = count // 2
    back = []
    for lo, hi in ((0, split), (split, count)):
        part = run(sent_inner, ahead_pick[lo:hi], ahead_far[lo:hi], ahead_mask[lo:hi])
        back.append(
            lax.ppermute(part, "region", [(i, (i + 1) % region_len) for i in range(region_len)])
        )
    mine = mine + run(*own_args, allowed=(3,))
    return jnp.stack([mine, jnp.concatenate(back, axis=0)], axis=1)


def solution(mesh):
    placed = (
        P(("region", "sub"), None, None, None),
        P(("region", "sub"), None),
        P(("region", "sub"), None),
        P(("region", "sub"), None, None),
    )
    return jax.shard_map(
        shards,
        mesh=mesh,
        in_specs=placed,
        out_specs=P(("region", "sub"), None, None, None),
        check_vma=False,
    )
```

```python
import functools
import math

import jax
import jax.numpy as jnp
from jax import lax
from jax.experimental import pallas as pl
from jax.experimental.pallas import tpu as pltpu
from jax.sharding import PartitionSpec as P

LAG = 50


def forward_table(samples):
    half = samples // 2
    sample_index = jnp.arange(samples, dtype=jnp.int32)
    orders = jnp.arange(half, dtype=jnp.int32)
    turn = 2.0 * math.pi / samples
    phase = (orders[:, None] * sample_index[None, :] % samples).astype(jnp.float32) * turn
    top = (half * sample_index % samples).astype(jnp.float32) * turn
    lower = jnp.concatenate([jnp.cos(top)[None, :], -jnp.sin(phase[1:])], axis=0)
    return jnp.concatenate([jnp.cos(phase), lower], axis=0)


def inverse_table(samples, reach):
    half = samples // 2
    orders = jnp.arange(half, dtype=jnp.int32)
    offsets = (jnp.arange(2 * reach + 1, dtype=jnp.int32) - reach + samples) % samples
    phase = (offsets[:, None] * orders[None, :] % samples).astype(jnp.float32) * (
        2.0 * math.pi / samples
    )
    parity = jnp.where(offsets % 2 == 0, 1.0, -1.0).astype(jnp.float32)
    scale = 2.0 / samples
    even = ((1.0 + parity) / (2.0 * samples))[:, None]
    odd = ((1.0 - parity) / (2.0 * samples))[:, None]
    cos_part = jnp.concatenate([even, scale * jnp.cos(phase[:, 1:])], axis=1)
    sin_part = jnp.concatenate([odd, -scale * jnp.sin(phase[:, 1:])], axis=1)
    table = jnp.concatenate([cos_part, sin_part], axis=1)
    rows = -(-table.shape[0] // 8) * 8
    return jnp.pad(table, ((0, rows - table.shape[0]), (0, 0)))


def split_exact(value):
    hi = lax.reduce_precision(value, exponent_bits=8, mantissa_bits=7)
    rest = value - hi
    mid = lax.reduce_precision(rest, exponent_bits=8, mantissa_bits=7)
    low = rest - mid
    return jnp.stack([hi, mid, low], axis=1).astype(jnp.bfloat16)


def round_kernel(allowed, keep, a_ref, b_ref, u_ref, own_ref, oen_ref, mask_ref, inv_ref, *rest):
    pieces = rest[:len(allowed)]
    out_ref, buf, sem, x_ref = rest[-4:]
    events, comps, samples, stations = own_ref.shape
    half = samples // 2
    body_rows = comps * samples
    count, lags = out_ref.shape[0], out_ref.shape[1]
    sub_at = u_ref[0]

    def piece_of(q):
        return jnp.bitwise_xor(b_ref[q] // events, sub_at)

    def wanted(q):
        piece = piece_of(q)
        hit = piece == allowed[0]
        for j in allowed[1:]:
            hit = hit | (piece == j)
        return hit

    def start(q, slot):
        piece = piece_of(q)
        event = b_ref[q] % events
        for j, source in zip(allowed, pieces):
            @pl.when(piece == j)
            def _():
                pltpu.make_async_copy(source.at[event], buf.at[slot], sem.at[slot]).start()

    start(0, 0)

    def step(q, carry):
        slot = q % 2

        @pl.when(q + 1 < count)
        def _():
            start(q + 1, 1 - slot)

        @pl.when(wanted(q))
        def _():
            work(q, slot)

        @pl.when(jnp.logical_not(wanted(q)))
        def _():
            if keep:
                out_ref[q] = rest[len(allowed)][q]
            else:
                out_ref[q] = jnp.zeros((lags, stations), jnp.float32)

        return carry

    def work(q, slot):
        pltpu.make_async_copy(pieces[0].at[0], buf.at[slot], sem.at[slot]).wait()
        ai = a_ref[q]
        u = None
        v = None
        w = None
        for c in range(comps):
            own = own_ref[ai, c]
            far = buf[slot, c * samples:(c + 1) * samples, :].astype(jnp.float32)
            oa = own[:half]
            ob = own[half:]
            fa = far[:half]
            fb = far[half:]
            uc = oa * fa + ob * fb
            vc = oa * fb - ob * fa
            wc = oa[:8] * fa[:8] - ob[:8] * fb[:8]
            u = uc if u is None else u + uc
            v = vc if v is None else v + vc
            w = wc if w is None else w + wc
        first = lax.broadcasted_iota(jnp.int32, w.shape, 0) == 0
        x_ref[:half, :] = u
        x_ref[half:, :] = v
        x_ref[half:half + 8, :] = jnp.where(first, w, v[:8])
        raw = jnp.dot(
            inv_ref[...], x_ref[...], precision=lax.Precision.HIGHEST,
            preferred_element_type=jnp.float32,
        )
        energy = jnp.sum(buf[slot, body_rows:body_rows + 16, :].astype(jnp.float32), axis=0,
                         keepdims=True)
        denom = jnp.sqrt(oen_ref[ai] * energy + 1e-06)
        out_ref[q] = raw[:lags] / denom * mask_ref[q]

    lax.fori_loop(0, count, step, 0)


def correlate_round(own_spec, own_energy, pieces, allowed, inverse, mask, own_pick, far_pick,
                    sub_at, prior):
    count = own_pick.shape[0]
    events, comps, samples, stations = own_spec.shape
    rows = pieces[0].shape[1]
    lags = 2 * LAG + 1
    smem = pl.BlockSpec(memory_space=pltpu.SMEM)
    vmem = pl.BlockSpec(memory_space=pltpu.VMEM)
    hbm = pl.BlockSpec(memory_space=pl.ANY)
    return pl.pallas_call(
        functools.partial(round_kernel, allowed, prior is not None),
        in_specs=[smem, smem, smem, vmem, vmem, vmem, vmem] + [hbm] * len(pieces)
        + ([vmem] if prior is not None else []),
        out_specs=vmem,
        out_shape=jax.ShapeDtypeStruct((count, lags, stations), jnp.float32),
        cost_estimate=pl.CostEstimate(
            flops=count * 6 * 2 * 104 * samples * stations,
            transcendentals=count * stations,
            bytes_accessed=count * 8 * (rows + comps * samples) * stations,
        ),
        scratch_shapes=[
            pltpu.VMEM((2, rows, stations), pieces[0].dtype),
            pltpu.SemaphoreType.DMA((2,)),
            pltpu.VMEM((samples, stations), jnp.float32),
        ],
    )(own_pick, far_pick, sub_at, own_spec, own_energy[:, None, :], mask[:, None, :], inverse,
      *pieces, *([prior] if prior is not None else []))


def spectra(forward, wide):
    samples = forward.shape[1]
    return jnp.einsum(
        "jt,ects->ecjs", forward[:, LAG:samples - LAG], wide, precision=lax.Precision.HIGH
    )


def by_xor(value, axis, flip):
    length = lax.axis_size(axis)
    return lax.ppermute(value, axis, [(i, i ^ flip) for i in range(length)])


def shards(waves, local_event, partner_event, station_mask):
    events, comps, samples, stations = waves.shape
    forward = forward_table(samples)
    inverse = inverse_table(samples, LAG)
    region_len = lax.axis_size("region")
    sub_at = lax.axis_index("sub")

    inner = waves[:, :, LAG:samples - LAG, :]
    slots = local_event.shape[0]
    inner_rows = comps * (samples - 2 * LAG)
    picks = jnp.zeros((2, stations), jnp.int32)
    picks = picks.at[0, :slots].set(local_event[:, 1]).at[1, :slots].set(partner_event[:, 1])
    meta = jnp.concatenate([station_mask[:, 1], picks], axis=0).astype(jnp.bfloat16)
    meta_rows = -(-meta.shape[0] // 16) * 16
    meta = jnp.pad(meta, ((0, meta_rows - meta.shape[0]), (0, 0)))
    carried = jnp.concatenate([inner.reshape(events * inner_rows, stations), meta], axis=0)
    sent = lax.ppermute(
        carried, "region", [(i, (i - 1) % region_len) for i in range(region_len)]
    )
    sent_inner = sent[:events * inner_rows].reshape(inner.shape)
    sent_meta = sent[events * inner_rows:].astype(jnp.int32)

    wide = waves.astype(jnp.float32)
    spec = jnp.einsum("jt,ects->ecjs", forward, wide, precision=lax.Precision.HIGH)
    full_energy = jnp.sum(wide * wide, axis=(1, 2))
    body = spec.astype(jnp.bfloat16).reshape(events, comps * samples, stations)
    pieces = split_exact(full_energy)
    tail = jnp.pad(pieces, ((0, 0), (0, 16 - pieces.shape[1]), (0, 0)))
    packed = jnp.concatenate([body, tail], axis=1)

    near = by_xor(packed, "sub", 1)
    across = by_xor(packed, "sub", 2)
    pieces = [packed, near, across, None]
    sub_vec = jnp.full((1,), sub_at, jnp.int32)

    def run(own_inner, own_pick, far_pick, mask, allowed=(0, 1, 2, 3), prior=None):
        own_wide = own_inner.astype(jnp.float32)
        own_spec = spectra(forward, own_wide)
        own_energy = jnp.sum(own_wide * own_wide, axis=(1, 2))
        own_pick = jnp.clip(own_pick, 0, events - 1)
        far_pick = jnp.clip(far_pick, 0, len(pieces) * events - 1)
        return correlate_round(
            own_spec, own_energy, tuple(pieces[j] for j in allowed), allowed, inverse,
            mask.astype(jnp.float32), own_pick, far_pick, sub_vec, prior,
        )

    own_args = (inner, local_event[:, 0], partner_event[:, 0], station_mask[:, 0])
    mine = run(*own_args, allowed=(0, 1))
    across, mine = lax.optimization_barrier((across, mine))
    pieces[2] = across
    pieces[3] = by_xor(across, "sub", 1)

    ahead_pick = sent_meta[slots, :slots]
    ahead_far = sent_meta[slots + 1, :slots]
    ahead_mask = sent_meta[:slots]
    split = slots // 2
    back = []
    for lo, hi in ((0, split), (split, slots)):
        part = run(sent_inner, ahead_pick[lo:hi], ahead_far[lo:hi], ahead_mask[lo:hi])
        part, mine = lax.optimization_barrier((part, mine))
        back.append(
            lax.ppermute(part, "region", [(i, (i + 1) % region_len) for i in range(region_len)])
        )
    late = mine
    mine = run(*own_args, allowed=(2, 3), prior=late)
    return jnp.stack([mine, jnp.concatenate(back, axis=0)], axis=1)


def solution(mesh):
    placed = (
        P(("region", "sub"), None, None, None),
        P(("region", "sub"), None),
        P(("region", "sub"), None),
        P(("region", "sub"), None, None),
    )
    return jax.shard_map(
        shards,
        mesh=mesh,
        in_specs=placed,
        out_specs=P(("region", "sub"), None, None, None),
        check_vma=False,
    )
```

```python
import functools
import math

import jax
import jax.numpy as jnp
from jax import lax
from jax.experimental import pallas as pl
from jax.experimental.pallas import tpu as pltpu
from jax.sharding import PartitionSpec as P

LAG = 50


def forward_table(samples):
    half = samples // 2
    sample_index = jnp.arange(samples, dtype=jnp.int32)
    orders = jnp.arange(half, dtype=jnp.int32)
    turn = 2.0 * math.pi / samples
    phase = (orders[:, None] * sample_index[None, :] % samples).astype(jnp.float32) * turn
    top = (half * sample_index % samples).astype(jnp.float32) * turn
    lower = jnp.concatenate([jnp.cos(top)[None, :], -jnp.sin(phase[1:])], axis=0)
    return jnp.concatenate([jnp.cos(phase), lower], axis=0)


def inverse_table(samples, reach):
    half = samples // 2
    orders = jnp.arange(half, dtype=jnp.int32)
    offsets = (jnp.arange(2 * reach + 1, dtype=jnp.int32) - reach + samples) % samples
    phase = (offsets[:, None] * orders[None, :] % samples).astype(jnp.float32) * (
        2.0 * math.pi / samples
    )
    parity = jnp.where(offsets % 2 == 0, 1.0, -1.0).astype(jnp.float32)
    scale = 2.0 / samples
    even = ((1.0 + parity) / (2.0 * samples))[:, None]
    odd = ((1.0 - parity) / (2.0 * samples))[:, None]
    cos_part = jnp.concatenate([even, scale * jnp.cos(phase[:, 1:])], axis=1)
    sin_part = jnp.concatenate([odd, -scale * jnp.sin(phase[:, 1:])], axis=1)
    table = jnp.concatenate([cos_part, sin_part], axis=1)
    rows = -(-table.shape[0] // 8) * 8
    return jnp.pad(table, ((0, rows - table.shape[0]), (0, 0)))


def split_exact(value):
    hi = lax.reduce_precision(value, exponent_bits=8, mantissa_bits=7)
    rest = value - hi
    mid = lax.reduce_precision(rest, exponent_bits=8, mantissa_bits=7)
    low = rest - mid
    return jnp.stack([hi, mid, low], axis=1).astype(jnp.bfloat16)


def round_kernel(allowed, a_ref, b_ref, u_ref, own_ref, oen_ref, mask_ref, inv_ref, *rest):
    pieces = rest[:-4]
    out_ref, buf, sem, x_ref = rest[-4:]
    events, comps, samples, stations = own_ref.shape
    half = samples // 2
    body_rows = comps * samples
    count, lags = out_ref.shape[0], out_ref.shape[1]
    sub_at = u_ref[0]

    def piece_of(q):
        return jnp.bitwise_xor(b_ref[q] // events, sub_at)

    def wanted(q):
        piece = piece_of(q)
        hit = piece == allowed[0]
        for j in allowed[1:]:
            hit = hit | (piece == j)
        return hit

    def start(q, slot):
        piece = piece_of(q)
        event = b_ref[q] % events
        for j, source in zip(allowed, pieces):
            @pl.when(piece == j)
            def _():
                pltpu.make_async_copy(source.at[event], buf.at[slot], sem.at[slot]).start()

    start(0, 0)

    def step(q, carry):
        slot = q % 2

        @pl.when(q + 1 < count)
        def _():
            start(q + 1, 1 - slot)

        @pl.when(wanted(q))
        def _():
            work(q, slot)

        @pl.when(jnp.logical_not(wanted(q)))
        def _():
            out_ref[q] = jnp.zeros((lags, stations), jnp.float32)

        return carry

    def work(q, slot):
        pltpu.make_async_copy(pieces[0].at[0], buf.at[slot], sem.at[slot]).wait()
        ai = a_ref[q]
        u = None
        v = None
        w = None
        for c in range(comps):
            own = own_ref[ai, c]
            far = buf[slot, c * samples:(c + 1) * samples, :].astype(jnp.float32)
            oa = own[:half]
            ob = own[half:]
            fa = far[:half]
            fb = far[half:]
            uc = oa * fa + ob * fb
            vc = oa * fb - ob * fa
            wc = oa[:8] * fa[:8] - ob[:8] * fb[:8]
            u = uc if u is None else u + uc
            v = vc if v is None else v + vc
            w = wc if w is None else w + wc
        first = lax.broadcasted_iota(jnp.int32, w.shape, 0) == 0
        x_ref[:half, :] = u
        x_ref[half:, :] = v
        x_ref[half:half + 8, :] = jnp.where(first, w, v[:8])
        raw = jnp.dot(
            inv_ref[...], x_ref[...], precision=lax.Precision.HIGHEST,
            preferred_element_type=jnp.float32,
        )
        energy = jnp.sum(buf[slot, body_rows:body_rows + 16, :].astype(jnp.float32), axis=0,
                         keepdims=True)
        denom = jnp.sqrt(oen_ref[ai] * energy + 1e-06)
        out_ref[q] = raw[:lags] / denom * mask_ref[q]

    lax.fori_loop(0, count, step, 0)


def correlate_round(own_spec, own_energy, pieces, allowed, inverse, mask, own_pick, far_pick,
                    sub_at):
    count = own_pick.shape[0]
    events, comps, samples, stations = own_spec.shape
    rows = pieces[0].shape[1]
    lags = 2 * LAG + 1
    smem = pl.BlockSpec(memory_space=pltpu.SMEM)
    vmem = pl.BlockSpec(memory_space=pltpu.VMEM)
    hbm = pl.BlockSpec(memory_space=pl.ANY)
    return pl.pallas_call(
        functools.partial(round_kernel, allowed),
        in_specs=[smem, smem, smem, vmem, vmem, vmem, vmem] + [hbm] * len(pieces),
        out_specs=vmem,
        out_shape=jax.ShapeDtypeStruct((count, lags, stations), jnp.float32),
        cost_estimate=pl.CostEstimate(
            flops=count * 6 * 2 * 104 * samples * stations,
            transcendentals=count * stations,
            bytes_accessed=count * 8 * (rows + comps * samples) * stations,
        ),
        scratch_shapes=[
            pltpu.VMEM((2, rows, stations), pieces[0].dtype),
            pltpu.SemaphoreType.DMA((2,)),
            pltpu.VMEM((samples, stations), jnp.float32),
        ],
    )(own_pick, far_pick, sub_at, own_spec, own_energy[:, None, :], mask[:, None, :], inverse,
      *pieces)


def spectra(forward, wide):
    samples = forward.shape[1]
    return jnp.einsum(
        "jt,ects->ecjs", forward[:, LAG:samples - LAG], wide, precision=lax.Precision.HIGH
    )


def by_xor(value, axis, flip):
    length = lax.axis_size(axis)
    return lax.ppermute(value, axis, [(i, i ^ flip) for i in range(length)])


def shards(waves, local_event, partner_event, station_mask):
    events, comps, samples, stations = waves.shape
    forward = forward_table(samples)
    inverse = inverse_table(samples, LAG)
    region_len = lax.axis_size("region")
    sub_at = lax.axis_index("sub")

    inner = waves[:, :, LAG:samples - LAG, :]
    meta = jnp.concatenate(
        [station_mask[:, 1], local_event[:, 1:2], partner_event[:, 1:2]], axis=1
    )
    sent_inner, sent_meta = lax.ppermute(
        (inner, meta), "region", [(i, (i - 1) % region_len) for i in range(region_len)]
    )

    wide = waves.astype(jnp.float32)
    spec = jnp.einsum("jt,ects->ecjs", forward, wide, precision=lax.Precision.HIGH)
    full_energy = jnp.sum(wide * wide, axis=(1, 2))
    body = spec.astype(jnp.bfloat16).reshape(events, comps * samples, stations)
    pieces = split_exact(full_energy)
    tail = jnp.pad(pieces, ((0, 0), (0, 16 - pieces.shape[1]), (0, 0)))
    packed = jnp.concatenate([body, tail], axis=1)

    near = by_xor(packed, "sub", 1)
    across = by_xor(packed, "sub", 2)
    pieces = [packed, near, across, None]
    sub_vec = jnp.full((1,), sub_at, jnp.int32)

    def run(own_inner, own_pick, far_pick, mask, allowed=(0, 1, 2, 3)):
        own_wide = own_inner.astype(jnp.float32)
        own_spec = spectra(forward, own_wide)
        own_energy = jnp.sum(own_wide * own_wide, axis=(1, 2))
        own_pick = jnp.clip(own_pick, 0, events - 1)
        far_pick = jnp.clip(far_pick, 0, len(pieces) * events - 1)
        return correlate_round(
            own_spec, own_energy, tuple(pieces[j] for j in allowed), allowed, inverse,
            mask.astype(jnp.float32), own_pick, far_pick, sub_vec,
        )

    own_args = (inner, local_event[:, 0], partner_event[:, 0])
    own_mask = station_mask[:, 0]
    mine = run(*own_args, own_mask, allowed=(0, 1))
    across, mine = lax.optimization_barrier((across, mine))
    pieces[2] = across
    pieces[3] = by_xor(across, "sub", 1)

    ahead_pick = sent_meta[:, stations]
    ahead_far = sent_meta[:, stations + 1]
    ahead_mask = sent_meta[:, :stations]
    count = ahead_pick.shape[0]
    split = count // 2
    back = []
    for lo, hi in ((0, split), (split, count)):
        part = run(sent_inner, ahead_pick[lo:hi], ahead_far[lo:hi], ahead_mask[lo:hi])
        back.append(part)
    back[-1], own_mask = lax.optimization_barrier((back[-1], own_mask))
    back = [
        lax.ppermute(part, "region", [(i, (i + 1) % region_len) for i in range(region_len)])
        for part in back
    ]
    late = run(*own_args, own_mask, allowed=(2, 3))
    return jnp.stack([mine + late, jnp.concatenate(back, axis=0)], axis=1)


def solution(mesh):
    placed = (
        P(("region", "sub"), None, None, None),
        P(("region", "sub"), None),
        P(("region", "sub"), None),
        P(("region", "sub"), None, None),
    )
    return jax.shard_map(
        shards,
        mesh=mesh,
        in_specs=placed,
        out_specs=P(("region", "sub"), None, None, None),
        check_vma=False,
    )
```

```python
import math

import jax
import jax.numpy as jnp
from jax import lax
from jax.experimental import pallas as pl
from jax.experimental.pallas import tpu as pltpu
from jax.sharding import PartitionSpec as P

LAG = 50


def forward_table(samples):
    half = samples // 2
    sample_index = jnp.arange(samples, dtype=jnp.int32)
    orders = jnp.arange(half, dtype=jnp.int32)
    turn = 2.0 * math.pi / samples
    phase = (orders[:, None] * sample_index[None, :] % samples).astype(jnp.float32) * turn
    top = (half * sample_index % samples).astype(jnp.float32) * turn
    lower = jnp.concatenate([jnp.cos(top)[None, :], -jnp.sin(phase[1:])], axis=0)
    return jnp.concatenate([jnp.cos(phase), lower], axis=0)


def inverse_table(samples, reach):
    half = samples // 2
    orders = jnp.arange(half, dtype=jnp.int32)
    offsets = (jnp.arange(2 * reach + 1, dtype=jnp.int32) - reach + samples) % samples
    phase = (offsets[:, None] * orders[None, :] % samples).astype(jnp.float32) * (
        2.0 * math.pi / samples
    )
    parity = jnp.where(offsets % 2 == 0, 1.0, -1.0).astype(jnp.float32)
    scale = 2.0 / samples
    even = ((1.0 + parity) / (2.0 * samples))[:, None]
    odd = ((1.0 - parity) / (2.0 * samples))[:, None]
    cos_part = jnp.concatenate([even, scale * jnp.cos(phase[:, 1:])], axis=1)
    sin_part = jnp.concatenate([odd, -scale * jnp.sin(phase[:, 1:])], axis=1)
    table = jnp.concatenate([cos_part, sin_part], axis=1)
    rows = -(-table.shape[0] // 8) * 8
    return jnp.pad(table, ((0, rows - table.shape[0]), (0, 0)))


def split_exact(value):
    hi = lax.reduce_precision(value, exponent_bits=8, mantissa_bits=7)
    rest = value - hi
    mid = lax.reduce_precision(rest, exponent_bits=8, mantissa_bits=7)
    low = rest - mid
    return jnp.stack([hi, mid, low], axis=1).astype(jnp.bfloat16)


def round_kernel(a_ref, b_ref, u_ref, own_ref, oen_ref, mask_ref, inv_ref, inv_low_ref, *rest):
    pieces = rest[:-4]
    out_ref, buf, sem, x_ref = rest[-4:]
    events, comps, samples, stations = own_ref.shape
    half = samples // 2
    body_rows = comps * samples
    count, lags = out_ref.shape[0], out_ref.shape[1]
    sub_at = u_ref[0]

    def start(q, slot):
        b = b_ref[q]
        piece = jnp.bitwise_xor(b // events, sub_at)
        event = b % events
        for j, source in enumerate(pieces):
            @pl.when(piece == j)
            def _():
                pltpu.make_async_copy(source.at[event], buf.at[slot], sem.at[slot]).start()

    start(0, 0)

    def step(q, carry):
        slot = q % 2

        @pl.when(q + 1 < count)
        def _():
            start(q + 1, 1 - slot)

        pltpu.make_async_copy(pieces[0].at[0], buf.at[slot], sem.at[slot]).wait()
        ai = a_ref[q]
        u = None
        v = None
        w = None
        for c in range(comps):
            own = own_ref[ai, c]
            far = buf[slot, c * samples:(c + 1) * samples, :].astype(jnp.float32)
            oa = own[:half]
            ob = own[half:]
            fa = far[:half]
            fb = far[half:]
            uc = oa * fa + ob * fb
            vc = oa * fb - ob * fa
            wc = oa[:8] * fa[:8] - ob[:8] * fb[:8]
            u = uc if u is None else u + uc
            v = vc if v is None else v + vc
            w = wc if w is None else w + wc
        first = lax.broadcasted_iota(jnp.int32, w.shape, 0) == 0
        x_ref[:half, :] = u
        x_ref[half:, :] = v
        x_ref[half:half + 8, :] = jnp.where(first, w, v[:8])
        x = x_ref[...]
        x_high = x.astype(jnp.bfloat16)
        x_low = (x - x_high.astype(jnp.float32)).astype(jnp.bfloat16)
        inv_high = inv_ref[...]
        raw = jnp.dot(inv_high, x_high, preferred_element_type=jnp.float32)
        raw = raw + jnp.dot(inv_high, x_low, preferred_element_type=jnp.float32)
        raw = raw + jnp.dot(inv_low_ref[...], x_high, preferred_element_type=jnp.float32)
        energy = jnp.sum(buf[slot, body_rows:body_rows + 16, :].astype(jnp.float32), axis=0,
                         keepdims=True)
        denom = jnp.sqrt(oen_ref[ai] * energy + 1e-06)
        out_ref[q] = raw[:lags] / denom * mask_ref[q]
        return carry

    lax.fori_loop(0, count, step, 0)


def correlate_round(own_spec, own_energy, pieces, inverse, mask, own_pick, far_pick, sub_at):
    count = own_pick.shape[0]
    events, comps, samples, stations = own_spec.shape
    rows = pieces[0].shape[1]
    lags = 2 * LAG + 1
    smem = pl.BlockSpec(memory_space=pltpu.SMEM)
    vmem = pl.BlockSpec(memory_space=pltpu.VMEM)
    hbm = pl.BlockSpec(memory_space=pl.ANY)
    return pl.pallas_call(
        round_kernel,
        in_specs=[smem, smem, smem, vmem, vmem, vmem, vmem, vmem] + [hbm] * len(pieces),
        out_specs=vmem,
        out_shape=jax.ShapeDtypeStruct((count, lags, stations), jnp.float32),
        scratch_shapes=[
            pltpu.VMEM((2, rows, stations), pieces[0].dtype),
            pltpu.SemaphoreType.DMA((2,)),
            pltpu.VMEM((samples, stations), jnp.float32),
        ],
    )(own_pick, far_pick, sub_at, own_spec, own_energy[:, None, :], mask[:, None, :], *inverse,
      *pieces)


def spectra(forward, wide):
    samples = forward.shape[1]
    return jnp.einsum(
        "jt,ects->ecjs", forward[:, LAG:samples - LAG], wide, precision=lax.Precision.HIGH
    )


def by_xor(value, axis, flip):
    length = lax.axis_size(axis)
    return lax.ppermute(value, axis, [(i, i ^ flip) for i in range(length)])


def shards(waves, local_event, partner_event, station_mask):
    events, comps, samples, stations = waves.shape
    forward = forward_table(samples)
    table = inverse_table(samples, LAG)
    table_high = lax.reduce_precision(table, exponent_bits=8, mantissa_bits=7)
    inverse = (table_high.astype(jnp.bfloat16), (table - table_high).astype(jnp.bfloat16))
    region_len = lax.axis_size("region")
    sub_at = lax.axis_index("sub")

    inner = waves[:, :, LAG:samples - LAG, :]
    meta = jnp.concatenate(
        [station_mask[:, 1], local_event[:, 1:2], partner_event[:, 1:2]], axis=1
    )
    sent_inner, sent_meta = lax.ppermute(
        (inner, meta), "region", [(i, (i - 1) % region_len) for i in range(region_len)]
    )

    wide = waves.astype(jnp.float32)
    spec = jnp.einsum("jt,ects->ecjs", forward, wide, precision=lax.Precision.HIGH)
    full_energy = jnp.sum(wide * wide, axis=(1, 2))
    body = spec.astype(jnp.bfloat16).reshape(events, comps * samples, stations)
    pieces = split_exact(full_energy)
    tail = jnp.pad(pieces, ((0, 0), (0, 16 - pieces.shape[1]), (0, 0)))
    packed = jnp.concatenate([body, tail], axis=1)

    near = by_xor(packed, "sub", 1)
    across = by_xor(packed, "sub", 2)
    corner = by_xor(across, "sub", 1)
    pieces = (packed, near, across, corner)
    sub_vec = jnp.full((1,), sub_at, jnp.int32)

    def run(own_inner, own_pick, far_pick, mask):
        own_wide = own_inner.astype(jnp.float32)
        own_spec = spectra(forward, own_wide)
        own_energy = jnp.sum(own_wide * own_wide, axis=(1, 2))
        own_pick = jnp.clip(own_pick, 0, events - 1)
        far_pick = jnp.clip(far_pick, 0, len(pieces) * events - 1)
        return correlate_round(
            own_spec, own_energy, pieces, inverse, mask.astype(jnp.float32), own_pick,
            far_pick, sub_vec,
        )

    ahead_pick = sent_meta[:, stations]
    ahead_far = sent_meta[:, stations + 1]
    ahead_mask = sent_meta[:, :stations]
    count = ahead_pick.shape[0]
    split = count // 2
    back = []
    for lo, hi in ((0, split), (split, count)):
        part = run(sent_inner, ahead_pick[lo:hi], ahead_far[lo:hi], ahead_mask[lo:hi])
        back.append(
            lax.ppermute(part, "region", [(i, (i + 1) % region_len) for i in range(region_len)])
        )
    mine = run(inner, local_event[:, 0], partner_event[:, 0], station_mask[:, 0])
    return jnp.stack([mine, jnp.concatenate(back, axis=0)], axis=1)


def solution(mesh):
    placed = (
        P(("region", "sub"), None, None, None),
        P(("region", "sub"), None),
        P(("region", "sub"), None),
        P(("region", "sub"), None, None),
    )
    return jax.shard_map(
        shards,
        mesh=mesh,
        in_specs=placed,
        out_specs=P(("region", "sub"), None, None, None),
        check_vma=False,
    )
```

```python
import math

import jax
import jax.numpy as jnp
from jax import lax
from jax.experimental import pallas as pl
from jax.experimental.pallas import tpu as pltpu
from jax.sharding import PartitionSpec as P

LAG = 50


def forward_table(samples):
    half = samples // 2
    sample_index = jnp.arange(samples, dtype=jnp.int32)
    orders = jnp.arange(half, dtype=jnp.int32)
    turn = 2.0 * math.pi / samples
    phase = (orders[:, None] * sample_index[None, :] % samples).astype(jnp.float32) * turn
    top = (half * sample_index % samples).astype(jnp.float32) * turn
    lower = jnp.concatenate([jnp.cos(top)[None, :], -jnp.sin(phase[1:])], axis=0)
    return jnp.concatenate([jnp.cos(phase), lower], axis=0)


def inverse_table(samples, reach):
    half = samples // 2
    orders = jnp.arange(half, dtype=jnp.int32)
    offsets = (jnp.arange(2 * reach + 1, dtype=jnp.int32) - reach + samples) % samples
    phase = (offsets[:, None] * orders[None, :] % samples).astype(jnp.float32) * (
        2.0 * math.pi / samples
    )
    parity = jnp.where(offsets % 2 == 0, 1.0, -1.0).astype(jnp.float32)
    scale = 2.0 / samples
    even = ((1.0 + parity) / (2.0 * samples))[:, None]
    odd = ((1.0 - parity) / (2.0 * samples))[:, None]
    cos_part = jnp.concatenate([even, scale * jnp.cos(phase[:, 1:])], axis=1)
    sin_part = jnp.concatenate([odd, -scale * jnp.sin(phase[:, 1:])], axis=1)
    table = jnp.concatenate([cos_part, sin_part], axis=1)
    rows = -(-table.shape[0] // 8) * 8
    return jnp.pad(table, ((0, rows - table.shape[0]), (0, 0)))


def split_exact(value):
    hi = lax.reduce_precision(value, exponent_bits=8, mantissa_bits=7)
    rest = value - hi
    mid = lax.reduce_precision(rest, exponent_bits=8, mantissa_bits=7)
    low = rest - mid
    return jnp.stack([hi, mid, low], axis=1).astype(jnp.bfloat16)


def round_kernel(a_ref, b_ref, u_ref, own_ref, oen_ref, mask_ref, inv_ref, inv_low_ref, *rest):
    pieces = rest[:-6]
    out_ref, buf, sem, x_ref, high_ref, low_ref = rest[-6:]
    events, comps, samples, stations = own_ref.shape
    half = samples // 2
    body_rows = comps * samples
    count, lags = out_ref.shape[0], out_ref.shape[1]
    sub_at = u_ref[0]

    def start(q, slot):
        b = b_ref[q]
        piece = jnp.bitwise_xor(b // events, sub_at)
        event = b % events
        for j, source in enumerate(pieces):
            @pl.when(piece == j)
            def _():
                pltpu.make_async_copy(source.at[event], buf.at[slot], sem.at[slot]).start()

    start(0, 0)

    def step(q, carry):
        slot = q % 2

        @pl.when(q + 1 < count)
        def _():
            start(q + 1, 1 - slot)

        pltpu.make_async_copy(pieces[0].at[0], buf.at[slot], sem.at[slot]).wait()
        ai = a_ref[q]
        first = lax.broadcasted_iota(jnp.int32, (8, stations), 0) == 0
        for r in range(0, half, 8):
            u = None
            v = None
            w = None
            for c in range(comps):
                base = c * samples
                oa = own_ref[ai, c, r:r + 8, :]
                ob = own_ref[ai, c, half + r:half + r + 8, :]
                fa = buf[slot, base + r:base + r + 8, :].astype(jnp.float32)
                fb = buf[slot, base + half + r:base + half + r + 8, :].astype(jnp.float32)
                uc = oa * fa + ob * fb
                vc = oa * fb - ob * fa
                u = uc if u is None else u + uc
                v = vc if v is None else v + vc
                if r == 0:
                    wc = oa * fa - ob * fb
                    w = wc if w is None else w + wc
            if r == 0:
                v = jnp.where(first, w, v)
            x_ref[r:r + 8, :] = u
            x_ref[half + r:half + r + 8, :] = v
        for r in range(0, samples, 16):
            x = x_ref[r:r + 16, :]
            x_high = x.astype(jnp.bfloat16)
            high_ref[r:r + 16, :] = x_high
            low_ref[r:r + 16, :] = (x - x_high.astype(jnp.float32)).astype(jnp.bfloat16)
        inv_high = inv_ref[...]
        x_high = high_ref[...]
        raw = jnp.dot(inv_high, x_high, preferred_element_type=jnp.float32)
        raw = raw + jnp.dot(inv_high, low_ref[...], preferred_element_type=jnp.float32)
        raw = raw + jnp.dot(inv_low_ref[...], x_high, preferred_element_type=jnp.float32)
        energy = jnp.sum(buf[slot, body_rows:body_rows + 16, :].astype(jnp.float32), axis=0,
                         keepdims=True)
        denom = jnp.sqrt(oen_ref[ai] * energy + 1e-06)
        out_ref[q] = raw[:lags] / denom * mask_ref[q]
        return carry

    lax.fori_loop(0, count, step, 0)


def correlate_round(own_spec, own_energy, pieces, inverse, mask, own_pick, far_pick, sub_at):
    count = own_pick.shape[0]
    events, comps, samples, stations = own_spec.shape
    rows = pieces[0].shape[1]
    lags = 2 * LAG + 1
    smem = pl.BlockSpec(memory_space=pltpu.SMEM)
    vmem = pl.BlockSpec(memory_space=pltpu.VMEM)
    hbm = pl.BlockSpec(memory_space=pl.ANY)
    return pl.pallas_call(
        round_kernel,
        in_specs=[smem, smem, smem, vmem, vmem, vmem, vmem, vmem] + [hbm] * len(pieces),
        out_specs=vmem,
        out_shape=jax.ShapeDtypeStruct((count, lags, stations), jnp.float32),
        scratch_shapes=[
            pltpu.VMEM((2, rows, stations), pieces[0].dtype),
            pltpu.SemaphoreType.DMA((2,)),
            pltpu.VMEM((samples, stations), jnp.float32),
            pltpu.VMEM((samples, stations), jnp.bfloat16),
            pltpu.VMEM((samples, stations), jnp.bfloat16),
        ],
    )(own_pick, far_pick, sub_at, own_spec, own_energy[:, None, :], mask[:, None, :], *inverse,
      *pieces)


def spectra(forward, wide):
    samples = forward.shape[1]
    return jnp.einsum(
        "jt,ects->ecjs", forward[:, LAG:samples - LAG], wide, precision=lax.Precision.HIGH
    )


def by_xor(value, axis, flip):
    length = lax.axis_size(axis)
    return lax.ppermute(value, axis, [(i, i ^ flip) for i in range(length)])


def shards(waves, local_event, partner_event, station_mask):
    events, comps, samples, stations = waves.shape
    forward = forward_table(samples)
    table = inverse_table(samples, LAG)
    table_high = lax.reduce_precision(table, exponent_bits=8, mantissa_bits=7)
    inverse = (table_high.astype(jnp.bfloat16), (table - table_high).astype(jnp.bfloat16))
    region_len = lax.axis_size("region")
    sub_at = lax.axis_index("sub")

    inner = waves[:, :, LAG:samples - LAG, :]
    meta = jnp.concatenate(
        [station_mask[:, 1], local_event[:, 1:2], partner_event[:, 1:2]], axis=1
    )
    sent_inner, sent_meta = lax.ppermute(
        (inner, meta), "region", [(i, (i - 1) % region_len) for i in range(region_len)]
    )

    wide = waves.astype(jnp.float32)
    spec = jnp.einsum("jt,ects->ecjs", forward, wide, precision=lax.Precision.HIGH)
    full_energy = jnp.sum(wide * wide, axis=(1, 2))
    body = spec.astype(jnp.bfloat16).reshape(events, comps * samples, stations)
    pieces = split_exact(full_energy)
    tail = jnp.pad(pieces, ((0, 0), (0, 16 - pieces.shape[1]), (0, 0)))
    packed = jnp.concatenate([body, tail], axis=1)

    near = by_xor(packed, "sub", 1)
    across = by_xor(packed, "sub", 2)
    corner = by_xor(across, "sub", 1)
    pieces = (packed, near, across, corner)
    sub_vec = jnp.full((1,), sub_at, jnp.int32)

    def run(own_inner, own_pick, far_pick, mask):
        own_wide = own_inner.astype(jnp.float32)
        own_spec = spectra(forward, own_wide)
        own_energy = jnp.sum(own_wide * own_wide, axis=(1, 2))
        own_pick = jnp.clip(own_pick, 0, events - 1)
        far_pick = jnp.clip(far_pick, 0, len(pieces) * events - 1)
        return correlate_round(
            own_spec, own_energy, pieces, inverse, mask.astype(jnp.float32), own_pick,
            far_pick, sub_vec,
        )

    ahead_pick = sent_meta[:, stations]
    ahead_far = sent_meta[:, stations + 1]
    ahead_mask = sent_meta[:, :stations]
    count = ahead_pick.shape[0]
    split = count // 2
    back = []
    for lo, hi in ((0, split), (split, count)):
        part = run(sent_inner, ahead_pick[lo:hi], ahead_far[lo:hi], ahead_mask[lo:hi])
        back.append(
            lax.ppermute(part, "region", [(i, (i + 1) % region_len) for i in range(region_len)])
        )
    mine = run(inner, local_event[:, 0], partner_event[:, 0], station_mask[:, 0])
    return jnp.stack([mine, jnp.concatenate(back, axis=0)], axis=1)


def solution(mesh):
    placed = (
        P(("region", "sub"), None, None, None),
        P(("region", "sub"), None),
        P(("region", "sub"), None),
        P(("region", "sub"), None, None),
    )
    return jax.shard_map(
        shards,
        mesh=mesh,
        in_specs=placed,
        out_specs=P(("region", "sub"), None, None, None),
        check_vma=False,
    )
```

```python
import math

import jax
import jax.numpy as jnp
from jax import lax
from jax.experimental import pallas as pl
from jax.experimental.pallas import tpu as pltpu
from jax.sharding import PartitionSpec as P

LAG = 50


def forward_table(samples):
    half = samples // 2
    sample_index = jnp.arange(samples, dtype=jnp.int32)
    orders = jnp.arange(half, dtype=jnp.int32)
    turn = 2.0 * math.pi / samples
    phase = (orders[:, None] * sample_index[None, :] % samples).astype(jnp.float32) * turn
    top = (half * sample_index % samples).astype(jnp.float32) * turn
    lower = jnp.concatenate([jnp.cos(top)[None, :], -jnp.sin(phase[1:])], axis=0)
    return jnp.concatenate([jnp.cos(phase), lower], axis=0)


def inverse_table(samples, reach):
    half = samples // 2
    orders = jnp.arange(half, dtype=jnp.int32)
    offsets = (jnp.arange(2 * reach + 1, dtype=jnp.int32) - reach + samples) % samples
    phase = (offsets[:, None] * orders[None, :] % samples).astype(jnp.float32) * (
        2.0 * math.pi / samples
    )
    parity = jnp.where(offsets % 2 == 0, 1.0, -1.0).astype(jnp.float32)
    scale = 2.0 / samples
    even = ((1.0 + parity) / (2.0 * samples))[:, None]
    odd = ((1.0 - parity) / (2.0 * samples))[:, None]
    cos_part = jnp.concatenate([even, scale * jnp.cos(phase[:, 1:])], axis=1)
    sin_part = jnp.concatenate([odd, -scale * jnp.sin(phase[:, 1:])], axis=1)
    table = jnp.concatenate([cos_part, sin_part], axis=1)
    rows = -(-table.shape[0] // 8) * 8
    return jnp.pad(table, ((0, rows - table.shape[0]), (0, 0)))


def split_exact(value):
    hi = lax.reduce_precision(value, exponent_bits=8, mantissa_bits=7)
    rest = value - hi
    mid = lax.reduce_precision(rest, exponent_bits=8, mantissa_bits=7)
    low = rest - mid
    return jnp.stack([hi, mid, low], axis=1).astype(jnp.bfloat16)


def round_kernel(a_ref, b_ref, u_ref, own_ref, oen_ref, mask_ref, inv_ref, inv_low_ref, *rest):
    pieces = rest[:-6]
    out_ref, buf, sem, x_ref, high_ref, low_ref = rest[-6:]
    events, comps, samples, stations = own_ref.shape
    half = samples // 2
    body_rows = comps * samples
    count, lags = out_ref.shape[0], out_ref.shape[1]
    sub_at = u_ref[0]

    bounds = [(c * samples, (c + 1) * samples) for c in range(comps)]
    bounds.append((body_rows, buf.shape[1]))

    def start(q, slot):
        b = b_ref[q]
        piece = jnp.bitwise_xor(b // events, sub_at)
        event = b % events
        for j, source in enumerate(pieces):
            @pl.when(piece == j)
            def _():
                for n, (lo, hi) in enumerate(bounds):
                    pltpu.make_async_copy(
                        source.at[event, lo:hi], buf.at[slot, lo:hi], sem.at[slot, n]
                    ).start()

    start(0, 0)

    def step(q, carry):
        slot = q % 2

        @pl.when(q + 1 < count)
        def _():
            start(q + 1, 1 - slot)

        for n, (lo, hi) in enumerate(bounds):
            pltpu.make_async_copy(
                pieces[0].at[0, lo:hi], buf.at[slot, lo:hi], sem.at[slot, n]
            ).wait()
        ai = a_ref[q]
        first = lax.broadcasted_iota(jnp.int32, (8, stations), 0) == 0
        for r in range(0, half, 8):
            u = None
            v = None
            w = None
            for c in range(comps):
                base = c * samples
                oa = own_ref[ai, c, r:r + 8, :]
                ob = own_ref[ai, c, half + r:half + r + 8, :]
                fa = buf[slot, base + r:base + r + 8, :].astype(jnp.float32)
                fb = buf[slot, base + half + r:base + half + r + 8, :].astype(jnp.float32)
                uc = oa * fa + ob * fb
                vc = oa * fb - ob * fa
                u = uc if u is None else u + uc
                v = vc if v is None else v + vc
                if r == 0:
                    wc = oa * fa - ob * fb
                    w = wc if w is None else w + wc
            if r == 0:
                v = jnp.where(first, w, v)
            x_ref[r:r + 8, :] = u
            x_ref[half + r:half + r + 8, :] = v
        for r in range(0, samples, 16):
            x = x_ref[r:r + 16, :]
            x_high = x.astype(jnp.bfloat16)
            high_ref[r:r + 16, :] = x_high
            low_ref[r:r + 16, :] = (x - x_high.astype(jnp.float32)).astype(jnp.bfloat16)
        inv_high = inv_ref[...]
        x_high = high_ref[...]
        raw = jnp.dot(inv_high, x_high, preferred_element_type=jnp.float32)
        raw = raw + jnp.dot(inv_high, low_ref[...], preferred_element_type=jnp.float32)
        raw = raw + jnp.dot(inv_low_ref[...], x_high, preferred_element_type=jnp.float32)
        energy = jnp.sum(buf[slot, body_rows:body_rows + 16, :].astype(jnp.float32), axis=0,
                         keepdims=True)
        denom = jnp.sqrt(oen_ref[ai] * energy + 1e-06)
        out_ref[q] = raw[:lags] / denom * mask_ref[q]
        return carry

    lax.fori_loop(0, count, step, 0)


def correlate_round(own_spec, own_energy, pieces, inverse, mask, own_pick, far_pick, sub_at):
    count = own_pick.shape[0]
    events, comps, samples, stations = own_spec.shape
    rows = pieces[0].shape[1]
    lags = 2 * LAG + 1
    smem = pl.BlockSpec(memory_space=pltpu.SMEM)
    vmem = pl.BlockSpec(memory_space=pltpu.VMEM)
    hbm = pl.BlockSpec(memory_space=pl.ANY)
    return pl.pallas_call(
        round_kernel,
        in_specs=[smem, smem, smem, vmem, vmem, vmem, vmem, vmem] + [hbm] * len(pieces),
        out_specs=vmem,
        out_shape=jax.ShapeDtypeStruct((count, lags, stations), jnp.float32),
        scratch_shapes=[
            pltpu.VMEM((2, rows, stations), pieces[0].dtype),
            pltpu.SemaphoreType.DMA((2, comps + 1)),
            pltpu.VMEM((samples, stations), jnp.float32),
            pltpu.VMEM((samples, stations), jnp.bfloat16),
            pltpu.VMEM((samples, stations), jnp.bfloat16),
        ],
    )(own_pick, far_pick, sub_at, own_spec, own_energy[:, None, :], mask[:, None, :], *inverse,
      *pieces)


def spectra(forward, wide):
    samples = forward.shape[1]
    return jnp.einsum(
        "jt,ects->ecjs", forward[:, LAG:samples - LAG], wide, precision=lax.Precision.HIGH
    )


def by_xor(value, axis, flip):
    length = lax.axis_size(axis)
    return lax.ppermute(value, axis, [(i, i ^ flip) for i in range(length)])


def shards(waves, local_event, partner_event, station_mask):
    events, comps, samples, stations = waves.shape
    forward = forward_table(samples)
    table = inverse_table(samples, LAG)
    table_high = lax.reduce_precision(table, exponent_bits=8, mantissa_bits=7)
    inverse = (table_high.astype(jnp.bfloat16), (table - table_high).astype(jnp.bfloat16))
    region_len = lax.axis_size("region")
    sub_at = lax.axis_index("sub")

    inner = waves[:, :, LAG:samples - LAG, :]
    meta = jnp.concatenate(
        [station_mask[:, 1], local_event[:, 1:2], partner_event[:, 1:2]], axis=1
    )
    sent_inner, sent_meta = lax.ppermute(
        (inner, meta), "region", [(i, (i - 1) % region_len) for i in range(region_len)]
    )

    wide = waves.astype(jnp.float32)
    spec = jnp.einsum("jt,ects->ecjs", forward, wide, precision=lax.Precision.HIGH)
    full_energy = jnp.sum(wide * wide, axis=(1, 2))
    body = spec.astype(jnp.bfloat16).reshape(events, comps * samples, stations)
    pieces = split_exact(full_energy)
    tail = jnp.pad(pieces, ((0, 0), (0, 16 - pieces.shape[1]), (0, 0)))
    packed = jnp.concatenate([body, tail], axis=1)

    near = by_xor(packed, "sub", 1)
    across = by_xor(packed, "sub", 2)
    corner = by_xor(across, "sub", 1)
    pieces = (packed, near, across, corner)
    sub_vec = jnp.full((1,), sub_at, jnp.int32)

    def run(own_inner, own_pick, far_pick, mask):
        own_wide = own_inner.astype(jnp.float32)
        own_spec = spectra(forward, own_wide)
        own_energy = jnp.sum(own_wide * own_wide, axis=(1, 2))
        own_pick = jnp.clip(own_pick, 0, events - 1)
        far_pick = jnp.clip(far_pick, 0, len(pieces) * events - 1)
        return correlate_round(
            own_spec, own_energy, pieces, inverse, mask.astype(jnp.float32), own_pick,
            far_pick, sub_vec,
        )

    ahead_pick = sent_meta[:, stations]
    ahead_far = sent_meta[:, stations + 1]
    ahead_mask = sent_meta[:, :stations]
    count = ahead_pick.shape[0]
    split = count // 2
    back = []
    for lo, hi in ((0, split), (split, count)):
        part = run(sent_inner, ahead_pick[lo:hi], ahead_far[lo:hi], ahead_mask[lo:hi])
        back.append(
            lax.ppermute(part, "region", [(i, (i + 1) % region_len) for i in range(region_len)])
        )
    mine = run(inner, local_event[:, 0], partner_event[:, 0], station_mask[:, 0])
    return jnp.stack([mine, jnp.concatenate(back, axis=0)], axis=1)


def solution(mesh):
    placed = (
        P(("region", "sub"), None, None, None),
        P(("region", "sub"), None),
        P(("region", "sub"), None),
        P(("region", "sub"), None, None),
    )
    return jax.shard_map(
        shards,
        mesh=mesh,
        in_specs=placed,
        out_specs=P(("region", "sub"), None, None, None),
        check_vma=False,
    )
```

```python
import functools
import math

import jax
import jax.numpy as jnp
from jax import lax
from jax.experimental import pallas as pl
from jax.experimental.pallas import tpu as pltpu
from jax.sharding import PartitionSpec as P

LAG = 50


def forward_table(samples):
    half = samples // 2
    sample_index = jnp.arange(samples, dtype=jnp.int32)
    orders = jnp.arange(half, dtype=jnp.int32)
    turn = 2.0 * math.pi / samples
    phase = (orders[:, None] * sample_index[None, :] % samples).astype(jnp.float32) * turn
    top = (half * sample_index % samples).astype(jnp.float32) * turn
    lower = jnp.concatenate([jnp.cos(top)[None, :], -jnp.sin(phase[1:])], axis=0)
    return jnp.concatenate([jnp.cos(phase), lower], axis=0)


def inverse_table(samples, reach):
    half = samples // 2
    orders = jnp.arange(half, dtype=jnp.int32)
    offsets = (jnp.arange(2 * reach + 1, dtype=jnp.int32) - reach + samples) % samples
    phase = (offsets[:, None] * orders[None, :] % samples).astype(jnp.float32) * (
        2.0 * math.pi / samples
    )
    parity = jnp.where(offsets % 2 == 0, 1.0, -1.0).astype(jnp.float32)
    scale = 2.0 / samples
    even = ((1.0 + parity) / (2.0 * samples))[:, None]
    odd = ((1.0 - parity) / (2.0 * samples))[:, None]
    cos_part = jnp.concatenate([even, scale * jnp.cos(phase[:, 1:])], axis=1)
    sin_part = jnp.concatenate([odd, -scale * jnp.sin(phase[:, 1:])], axis=1)
    table = jnp.concatenate([cos_part, sin_part], axis=1)
    rows = -(-table.shape[0] // 8) * 8
    return jnp.pad(table, ((0, rows - table.shape[0]), (0, 0)))


def split_exact(value):
    hi = lax.reduce_precision(value, exponent_bits=8, mantissa_bits=7)
    rest = value - hi
    mid = lax.reduce_precision(rest, exponent_bits=8, mantissa_bits=7)
    low = rest - mid
    return jnp.stack([hi, mid, low], axis=1).astype(jnp.bfloat16)


def round_kernel(allowed, a_ref, b_ref, u_ref, own_ref, oen_ref, mask_ref, inv_ref, inv_low_ref,
                 *rest):
    pieces = rest[:-4]
    out_ref, buf, sem, x_ref = rest[-4:]
    events, comps, samples, stations = own_ref.shape
    half = samples // 2
    body_rows = comps * samples
    count, lags = out_ref.shape[0], out_ref.shape[1]
    sub_at = u_ref[0]

    def piece_of(q):
        return jnp.bitwise_xor(b_ref[q] // events, sub_at)

    def wanted(q):
        piece = piece_of(q)
        hit = piece == allowed[0]
        for j in allowed[1:]:
            hit = hit | (piece == j)
        return hit

    def start(q, slot):
        piece = piece_of(q)
        event = b_ref[q] % events
        for j, source in zip(allowed, pieces):
            @pl.when(piece == j)
            def _():
                pltpu.make_async_copy(source.at[event], buf.at[slot], sem.at[slot]).start()

    start(0, 0)

    def step(q, carry):
        slot = q % 2

        @pl.when(q + 1 < count)
        def _():
            start(q + 1, 1 - slot)

        @pl.when(wanted(q))
        def _():
            work(q, slot)

        @pl.when(jnp.logical_not(wanted(q)))
        def _():
            out_ref[q] = jnp.zeros((lags, stations), jnp.float32)

        return carry

    def work(q, slot):
        pltpu.make_async_copy(pieces[0].at[0], buf.at[slot], sem.at[slot]).wait()
        ai = a_ref[q]
        u = None
        v = None
        w = None
        for c in range(comps):
            own = own_ref[ai, c]
            far = buf[slot, c * samples:(c + 1) * samples, :].astype(jnp.float32)
            oa = own[:half]
            ob = own[half:]
            fa = far[:half]
            fb = far[half:]
            uc = oa * fa + ob * fb
            vc = oa * fb - ob * fa
            wc = oa[:8] * fa[:8] - ob[:8] * fb[:8]
            u = uc if u is None else u + uc
            v = vc if v is None else v + vc
            w = wc if w is None else w + wc
        first = lax.broadcasted_iota(jnp.int32, w.shape, 0) == 0
        x_ref[:half, :] = u
        x_ref[half:, :] = v
        x_ref[half:half + 8, :] = jnp.where(first, w, v[:8])
        x = x_ref[...]
        x_high = x.astype(jnp.bfloat16)
        x_low = (x - x_high.astype(jnp.float32)).astype(jnp.bfloat16)
        inv_high = inv_ref[...]
        raw = jnp.dot(inv_high, x_high, preferred_element_type=jnp.float32)
        raw = raw + jnp.dot(inv_high, x_low, preferred_element_type=jnp.float32)
        raw = raw + jnp.dot(inv_low_ref[...], x_high, preferred_element_type=jnp.float32)
        energy = jnp.sum(buf[slot, body_rows:body_rows + 16, :].astype(jnp.float32), axis=0,
                         keepdims=True)
        denom = jnp.sqrt(oen_ref[ai] * energy + 1e-06)
        out_ref[q] = raw[:lags] / denom * mask_ref[q]

    lax.fori_loop(0, count, step, 0)


def correlate_round(own_spec, own_energy, pieces, allowed, inverse, mask, own_pick, far_pick,
                    sub_at):
    count = own_pick.shape[0]
    events, comps, samples, stations = own_spec.shape
    rows = pieces[0].shape[1]
    lags = 2 * LAG + 1
    smem = pl.BlockSpec(memory_space=pltpu.SMEM)
    vmem = pl.BlockSpec(memory_space=pltpu.VMEM)
    hbm = pl.BlockSpec(memory_space=pl.ANY)
    return pl.pallas_call(
        functools.partial(round_kernel, allowed),
        in_specs=[smem, smem, smem, vmem, vmem, vmem, vmem, vmem] + [hbm] * len(pieces),
        out_specs=vmem,
        out_shape=jax.ShapeDtypeStruct((count, lags, stations), jnp.float32),
        cost_estimate=pl.CostEstimate(
            flops=count * 6 * 2 * 104 * samples * stations,
            transcendentals=count * stations,
            bytes_accessed=count * 8 * (rows + comps * samples) * stations,
        ),
        scratch_shapes=[
            pltpu.VMEM((2, rows, stations), pieces[0].dtype),
            pltpu.SemaphoreType.DMA((2,)),
            pltpu.VMEM((samples, stations), jnp.float32),
        ],
    )(own_pick, far_pick, sub_at, own_spec, own_energy[:, None, :], mask[:, None, :], *inverse,
      *pieces)


def spectra(forward, wide):
    samples = forward.shape[1]
    return jnp.einsum(
        "jt,ects->ecjs", forward[:, LAG:samples - LAG], wide, precision=lax.Precision.HIGH
    )


def by_xor(value, axis, flip):
    length = lax.axis_size(axis)
    return lax.ppermute(value, axis, [(i, i ^ flip) for i in range(length)])


def shards(waves, local_event, partner_event, station_mask):
    events, comps, samples, stations = waves.shape
    forward = forward_table(samples)
    table = inverse_table(samples, LAG)
    table_high = lax.reduce_precision(table, exponent_bits=8, mantissa_bits=7)
    inverse = (table_high.astype(jnp.bfloat16), (table - table_high).astype(jnp.bfloat16))
    region_len = lax.axis_size("region")
    sub_at = lax.axis_index("sub")

    inner = waves[:, :, LAG:samples - LAG, :]
    meta = jnp.concatenate(
        [station_mask[:, 1], local_event[:, 1:2], partner_event[:, 1:2]], axis=1
    )
    sent_inner, sent_meta = lax.ppermute(
        (inner, meta), "region", [(i, (i - 1) % region_len) for i in range(region_len)]
    )

    wide = waves.astype(jnp.float32)
    spec = jnp.einsum("jt,ects->ecjs", forward, wide, precision=lax.Precision.HIGH)
    full_energy = jnp.sum(wide * wide, axis=(1, 2))
    body = spec.astype(jnp.bfloat16).reshape(events, comps * samples, stations)
    pieces = split_exact(full_energy)
    tail = jnp.pad(pieces, ((0, 0), (0, 16 - pieces.shape[1]), (0, 0)))
    packed = jnp.concatenate([body, tail], axis=1)

    near = by_xor(packed, "sub", 1)
    across = by_xor(packed, "sub", 2)
    pieces = [packed, near, across, None]
    sub_vec = jnp.full((1,), sub_at, jnp.int32)

    def prepare(own_inner):
        own_wide = own_inner.astype(jnp.float32)
        return spectra(forward, own_wide), jnp.sum(own_wide * own_wide, axis=(1, 2))

    def run(prepared, own_pick, far_pick, mask, allowed=(0, 1, 2, 3)):
        own_spec, own_energy = prepared
        own_pick = jnp.clip(own_pick, 0, events - 1)
        far_pick = jnp.clip(far_pick, 0, len(pieces) * events - 1)
        return correlate_round(
            own_spec, own_energy, tuple(pieces[j] for j in allowed), allowed, inverse,
            mask.astype(jnp.float32), own_pick, far_pick, sub_vec,
        )

    own_args = (prepare(inner), local_event[:, 0], partner_event[:, 0])
    sent_meta, own_mask = lax.optimization_barrier((sent_meta, station_mask[:, 0]))
    mine = run(*own_args, own_mask, allowed=(0, 1))
    across, mine = lax.optimization_barrier((across, mine))
    pieces[2] = across
    ahead_spec = prepare(sent_inner)
    pieces[3], ahead_spec = lax.optimization_barrier((by_xor(across, "sub", 1), ahead_spec))

    ahead_pick = sent_meta[:, stations]
    ahead_far = sent_meta[:, stations + 1]
    ahead_mask = sent_meta[:, :stations]
    count = ahead_pick.shape[0]
    split = count // 2
    back = []
    for lo, hi in ((0, split), (split, count)):
        back.append(run(ahead_spec, ahead_pick[lo:hi], ahead_far[lo:hi], ahead_mask[lo:hi]))
    back[-1], own_mask = lax.optimization_barrier((back[-1], own_mask))
    back = [
        lax.ppermute(part, "region", [(i, (i + 1) % region_len) for i in range(region_len)])
        for part in back
    ]
    late = run(*own_args, own_mask, allowed=(2, 3))
    return jnp.stack([mine + late, jnp.concatenate(back, axis=0)], axis=1)


def solution(mesh):
    placed = (
        P(("region", "sub"), None, None, None),
        P(("region", "sub"), None),
        P(("region", "sub"), None),
        P(("region", "sub"), None, None),
    )
    return jax.shard_map(
        shards,
        mesh=mesh,
        in_specs=placed,
        out_specs=P(("region", "sub"), None, None, None),
        check_vma=False,
    )
```

```python
import functools
import math

import jax
import jax.numpy as jnp
from jax import lax
from jax.experimental import pallas as pl
from jax.experimental.pallas import tpu as pltpu
from jax.sharding import PartitionSpec as P

LAG = 50


def forward_table(samples):
    half = samples // 2
    sample_index = jnp.arange(samples, dtype=jnp.int32)
    orders = jnp.arange(half, dtype=jnp.int32)
    turn = 2.0 * math.pi / samples
    phase = (orders[:, None] * sample_index[None, :] % samples).astype(jnp.float32) * turn
    top = (half * sample_index % samples).astype(jnp.float32) * turn
    lower = jnp.concatenate([jnp.cos(top)[None, :], -jnp.sin(phase[1:])], axis=0)
    return jnp.concatenate([jnp.cos(phase), lower], axis=0)


def inverse_table(samples, reach):
    half = samples // 2
    orders = jnp.arange(half, dtype=jnp.int32)
    offsets = (jnp.arange(2 * reach + 1, dtype=jnp.int32) - reach + samples) % samples
    phase = (offsets[:, None] * orders[None, :] % samples).astype(jnp.float32) * (
        2.0 * math.pi / samples
    )
    parity = jnp.where(offsets % 2 == 0, 1.0, -1.0).astype(jnp.float32)
    scale = 2.0 / samples
    even = ((1.0 + parity) / (2.0 * samples))[:, None]
    odd = ((1.0 - parity) / (2.0 * samples))[:, None]
    cos_part = jnp.concatenate([even, scale * jnp.cos(phase[:, 1:])], axis=1)
    sin_part = jnp.concatenate([odd, -scale * jnp.sin(phase[:, 1:])], axis=1)
    table = jnp.concatenate([cos_part, sin_part], axis=1)
    rows = -(-table.shape[0] // 8) * 8
    return jnp.pad(table, ((0, rows - table.shape[0]), (0, 0)))


def split_exact(value):
    hi = lax.reduce_precision(value, exponent_bits=8, mantissa_bits=7)
    rest = value - hi
    mid = lax.reduce_precision(rest, exponent_bits=8, mantissa_bits=7)
    low = rest - mid
    return jnp.stack([hi, mid, low], axis=1).astype(jnp.bfloat16)


def round_kernel(allowed, a_ref, b_ref, u_ref, own_ref, oen_ref, mask_ref, inv_ref, inv_low_ref,
                 *rest):
    pieces = rest[:-4]
    out_ref, buf, sem, x_ref = rest[-4:]
    events, comps, samples, stations = own_ref.shape
    half = samples // 2
    body_rows = comps * samples
    count, lags = out_ref.shape[0], out_ref.shape[1]
    sub_at = u_ref[0]

    def piece_of(q):
        return jnp.bitwise_xor(b_ref[q] // events, sub_at)

    def wanted(q):
        piece = piece_of(q)
        hit = piece == allowed[0]
        for j in allowed[1:]:
            hit = hit | (piece == j)
        return hit

    def start(q, slot):
        piece = piece_of(q)
        event = b_ref[q] % events
        for j, source in zip(allowed, pieces):
            @pl.when(piece == j)
            def _():
                pltpu.make_async_copy(source.at[event], buf.at[slot], sem.at[slot]).start()

    start(0, 0)

    def step(q, carry):
        slot = q % 2

        @pl.when(q + 1 < count)
        def _():
            start(q + 1, 1 - slot)

        @pl.when(wanted(q))
        def _():
            work(q, slot)

        @pl.when(jnp.logical_not(wanted(q)))
        def _():
            out_ref[q] = jnp.zeros((lags, stations), jnp.float32)

        return carry

    def work(q, slot):
        pltpu.make_async_copy(pieces[0].at[0], buf.at[slot], sem.at[slot]).wait()
        ai = a_ref[q]
        u = None
        v = None
        w = None
        for c in range(comps):
            own = own_ref[ai, c]
            far = buf[slot, c * samples:(c + 1) * samples, :].astype(jnp.float32)
            oa = own[:half]
            ob = own[half:]
            fa = far[:half]
            fb = far[half:]
            uc = oa * fa + ob * fb
            vc = oa * fb - ob * fa
            wc = oa[:8] * fa[:8] - ob[:8] * fb[:8]
            u = uc if u is None else u + uc
            v = vc if v is None else v + vc
            w = wc if w is None else w + wc
        first = lax.broadcasted_iota(jnp.int32, w.shape, 0) == 0
        x_ref[:half, :] = u
        x_ref[half:, :] = v
        x_ref[half:half + 8, :] = jnp.where(first, w, v[:8])
        x = x_ref[...]
        x_high = x.astype(jnp.bfloat16)
        x_low = (x - x_high.astype(jnp.float32)).astype(jnp.bfloat16)
        inv_high = inv_ref[...]
        raw = jnp.dot(inv_high, x_high, preferred_element_type=jnp.float32)
        raw = raw + jnp.dot(inv_high, x_low, preferred_element_type=jnp.float32)
        raw = raw + jnp.dot(inv_low_ref[...], x_high, preferred_element_type=jnp.float32)
        energy = jnp.sum(buf[slot, body_rows:body_rows + 16, :].astype(jnp.float32), axis=0,
                         keepdims=True)
        denom = jnp.sqrt(oen_ref[ai] * energy + 1e-06)
        out_ref[q] = raw[:lags] / denom * mask_ref[q]

    lax.fori_loop(0, count, step, 0)


def correlate_round(own_spec, own_energy, pieces, allowed, inverse, mask, own_pick, far_pick,
                    sub_at):
    count = own_pick.shape[0]
    events, comps, samples, stations = own_spec.shape
    rows = pieces[0].shape[1]
    lags = 2 * LAG + 1
    smem = pl.BlockSpec(memory_space=pltpu.SMEM)
    vmem = pl.BlockSpec(memory_space=pltpu.VMEM)
    hbm = pl.BlockSpec(memory_space=pl.ANY)
    return pl.pallas_call(
        functools.partial(round_kernel, allowed),
        in_specs=[smem, smem, smem, vmem, vmem, vmem, vmem, vmem] + [hbm] * len(pieces),
        out_specs=vmem,
        out_shape=jax.ShapeDtypeStruct((count, lags, stations), jnp.float32),
        cost_estimate=pl.CostEstimate(
            flops=count * 6 * 2 * 104 * samples * stations,
            transcendentals=count * stations,
            bytes_accessed=count * 8 * (rows + comps * samples) * stations,
        ),
        scratch_shapes=[
            pltpu.VMEM((2, rows, stations), pieces[0].dtype),
            pltpu.SemaphoreType.DMA((2,)),
            pltpu.VMEM((samples, stations), jnp.float32),
        ],
    )(own_pick, far_pick, sub_at, own_spec, own_energy[:, None, :], mask[:, None, :], *inverse,
      *pieces)


def spectra(forward, wide):
    samples = forward.shape[1]
    return jnp.einsum(
        "jt,ects->ecjs", forward[:, LAG:samples - LAG], wide, precision=lax.Precision.HIGH
    )


def by_xor(value, axis, flip):
    length = lax.axis_size(axis)
    return lax.ppermute(value, axis, [(i, i ^ flip) for i in range(length)])


def shards(waves, local_event, partner_event, station_mask):
    events, comps, samples, stations = waves.shape
    forward = forward_table(samples)
    table = inverse_table(samples, LAG)
    table_high = lax.reduce_precision(table, exponent_bits=8, mantissa_bits=7)
    inverse = (table_high.astype(jnp.bfloat16), (table - table_high).astype(jnp.bfloat16))
    region_len = lax.axis_size("region")
    sub_at = lax.axis_index("sub")

    inner = waves[:, :, LAG:samples - LAG, :]
    meta = jnp.concatenate(
        [station_mask[:, 1], local_event[:, 1:2], partner_event[:, 1:2]], axis=1
    )
    inner_wide = inner.astype(jnp.float32)
    inner_energy = jnp.sum(inner_wide * inner_wide, axis=(1, 2))
    sent_inner, sent_meta, sent_energy = lax.ppermute(
        (inner, meta, inner_energy), "region",
        [(i, (i - 1) % region_len) for i in range(region_len)],
    )

    wide = waves.astype(jnp.float32)
    spec = jnp.einsum("jt,ects->ecjs", forward, wide, precision=lax.Precision.HIGH)
    full_energy = jnp.sum(wide * wide, axis=(1, 2))
    body = spec.astype(jnp.bfloat16).reshape(events, comps * samples, stations)
    pieces = split_exact(full_energy)
    tail = jnp.pad(pieces, ((0, 0), (0, 16 - pieces.shape[1]), (0, 0)))
    packed = jnp.concatenate([body, tail], axis=1)

    near = by_xor(packed, "sub", 1)
    across = by_xor(packed, "sub", 2)
    pieces = [packed, near, across, None]
    sub_vec = jnp.full((1,), sub_at, jnp.int32)

    def prepare(own_inner, own_energy):
        return spectra(forward, own_inner.astype(jnp.float32)), own_energy

    def run(prepared, own_pick, far_pick, mask, allowed=(0, 1, 2, 3)):
        own_spec, own_energy = prepared
        own_pick = jnp.clip(own_pick, 0, events - 1)
        far_pick = jnp.clip(far_pick, 0, len(pieces) * events - 1)
        return correlate_round(
            own_spec, own_energy, tuple(pieces[j] for j in allowed), allowed, inverse,
            mask.astype(jnp.float32), own_pick, far_pick, sub_vec,
        )

    own_args = (prepare(inner, inner_energy), local_event[:, 0], partner_event[:, 0])
    sent_meta, own_mask = lax.optimization_barrier((sent_meta, station_mask[:, 0]))
    mine = run(*own_args, own_mask, allowed=(0, 1))
    across, mine = lax.optimization_barrier((across, mine))
    pieces[2] = across
    ahead_spec = prepare(sent_inner, sent_energy)
    pieces[3], ahead_spec = lax.optimization_barrier((by_xor(across, "sub", 1), ahead_spec))

    ahead_pick = sent_meta[:, stations]
    ahead_far = sent_meta[:, stations + 1]
    ahead_mask = sent_meta[:, :stations]
    count = ahead_pick.shape[0]
    split = count // 2
    back = []
    for lo, hi in ((0, split), (split, count)):
        back.append(run(ahead_spec, ahead_pick[lo:hi], ahead_far[lo:hi], ahead_mask[lo:hi]))
    back[-1], own_mask = lax.optimization_barrier((back[-1], own_mask))
    back = [
        lax.ppermute(part, "region", [(i, (i + 1) % region_len) for i in range(region_len)])
        for part in back
    ]
    late = run(*own_args, own_mask, allowed=(2, 3))
    return jnp.stack([mine + late, jnp.concatenate(back, axis=0)], axis=1)


def solution(mesh):
    placed = (
        P(("region", "sub"), None, None, None),
        P(("region", "sub"), None),
        P(("region", "sub"), None),
        P(("region", "sub"), None, None),
    )
    return jax.shard_map(
        shards,
        mesh=mesh,
        in_specs=placed,
        out_specs=P(("region", "sub"), None, None, None),
        check_vma=False,
    )
```

```python
import functools
import math

import jax
import jax.numpy as jnp
from jax import lax
from jax.experimental import pallas as pl
from jax.experimental.pallas import tpu as pltpu
from jax.sharding import PartitionSpec as P

LAG = 50


def forward_table(samples):
    half = samples // 2
    sample_index = jnp.arange(samples, dtype=jnp.int32)
    orders = jnp.arange(half, dtype=jnp.int32)
    turn = 2.0 * math.pi / samples
    phase = (orders[:, None] * sample_index[None, :] % samples).astype(jnp.float32) * turn
    top = (half * sample_index % samples).astype(jnp.float32) * turn
    lower = jnp.concatenate([jnp.cos(top)[None, :], -jnp.sin(phase[1:])], axis=0)
    return jnp.concatenate([jnp.cos(phase), lower], axis=0)


def inverse_table(samples, reach):
    half = samples // 2
    orders = jnp.arange(half, dtype=jnp.int32)
    offsets = (jnp.arange(2 * reach + 1, dtype=jnp.int32) - reach + samples) % samples
    phase = (offsets[:, None] * orders[None, :] % samples).astype(jnp.float32) * (
        2.0 * math.pi / samples
    )
    parity = jnp.where(offsets % 2 == 0, 1.0, -1.0).astype(jnp.float32)
    scale = 2.0 / samples
    even = ((1.0 + parity) / (2.0 * samples))[:, None]
    odd = ((1.0 - parity) / (2.0 * samples))[:, None]
    cos_part = jnp.concatenate([even, scale * jnp.cos(phase[:, 1:])], axis=1)
    sin_part = jnp.concatenate([odd, -scale * jnp.sin(phase[:, 1:])], axis=1)
    table = jnp.concatenate([cos_part, sin_part], axis=1)
    rows = -(-table.shape[0] // 8) * 8
    return jnp.pad(table, ((0, rows - table.shape[0]), (0, 0)))


def split_exact(value):
    hi = lax.reduce_precision(value, exponent_bits=8, mantissa_bits=7)
    rest = value - hi
    mid = lax.reduce_precision(rest, exponent_bits=8, mantissa_bits=7)
    low = rest - mid
    return jnp.stack([hi, mid, low], axis=1).astype(jnp.bfloat16)


def round_kernel(allowed, a_ref, b_ref, u_ref, own_ref, oen_ref, mask_ref, inv_ref, inv_low_ref,
                 *rest):
    pieces = rest[:-4]
    out_ref, buf, sem, x_ref = rest[-4:]
    events, comps, samples, stations = own_ref.shape
    half = samples // 2
    body_rows = comps * samples
    count, lags = out_ref.shape[0], out_ref.shape[1]
    sub_at = u_ref[0]

    def piece_of(q):
        return jnp.bitwise_xor(b_ref[q] // events, sub_at)

    def wanted(q):
        piece = piece_of(q)
        hit = piece == allowed[0]
        for j in allowed[1:]:
            hit = hit | (piece == j)
        return hit

    def start(q, slot):
        piece = piece_of(q)
        event = b_ref[q] % events
        for j, source in zip(allowed, pieces):
            @pl.when(piece == j)
            def _():
                pltpu.make_async_copy(source.at[event], buf.at[slot], sem.at[slot]).start()

    start(0, 0)

    def step(q, carry):
        slot = q % 2

        @pl.when(q + 1 < count)
        def _():
            start(q + 1, 1 - slot)

        @pl.when(wanted(q))
        def _():
            work(q, slot)

        @pl.when(jnp.logical_not(wanted(q)))
        def _():
            out_ref[q] = jnp.zeros((lags, stations), jnp.float32)

        return carry

    def work(q, slot):
        pltpu.make_async_copy(pieces[0].at[0], buf.at[slot], sem.at[slot]).wait()
        ai = a_ref[q]
        u = None
        v = None
        w = None
        for c in range(comps):
            own = own_ref[ai, c]
            far = buf[slot, c * samples:(c + 1) * samples, :].astype(jnp.float32)
            oa = own[:half]
            ob = own[half:]
            fa = far[:half]
            fb = far[half:]
            uc = oa * fa + ob * fb
            vc = oa * fb - ob * fa
            wc = oa[:8] * fa[:8] - ob[:8] * fb[:8]
            u = uc if u is None else u + uc
            v = vc if v is None else v + vc
            w = wc if w is None else w + wc
        first = lax.broadcasted_iota(jnp.int32, w.shape, 0) == 0
        x_ref[:half, :] = u
        x_ref[half:, :] = v
        x_ref[half:half + 8, :] = jnp.where(first, w, v[:8])
        x = x_ref[...]
        x_high = x.astype(jnp.bfloat16)
        x_low = (x - x_high.astype(jnp.float32)).astype(jnp.bfloat16)
        inv_high = inv_ref[...]
        raw = jnp.dot(inv_high, x_high, preferred_element_type=jnp.float32)
        raw = raw + jnp.dot(inv_high, x_low, preferred_element_type=jnp.float32)
        raw = raw + jnp.dot(inv_low_ref[...], x_high, preferred_element_type=jnp.float32)
        energy = jnp.sum(buf[slot, body_rows:body_rows + 16, :].astype(jnp.float32), axis=0,
                         keepdims=True)
        denom = jnp.sqrt(oen_ref[ai] * energy + 1e-06)
        out_ref[q] = raw[:lags] / denom * mask_ref[q]

    lax.fori_loop(0, count, step, 0)


def correlate_round(own_spec, own_energy, pieces, allowed, inverse, mask, own_pick, far_pick,
                    sub_at):
    count = own_pick.shape[0]
    events, comps, samples, stations = own_spec.shape
    rows = pieces[0].shape[1]
    lags = 2 * LAG + 1
    smem = pl.BlockSpec(memory_space=pltpu.SMEM)
    vmem = pl.BlockSpec(memory_space=pltpu.VMEM)
    hbm = pl.BlockSpec(memory_space=pl.ANY)
    return pl.pallas_call(
        functools.partial(round_kernel, allowed),
        in_specs=[smem, smem, smem, vmem, vmem, vmem, vmem, vmem] + [hbm] * len(pieces),
        out_specs=vmem,
        out_shape=jax.ShapeDtypeStruct((count, lags, stations), jnp.float32),
        cost_estimate=pl.CostEstimate(
            flops=count * 6 * 2 * 104 * samples * stations,
            transcendentals=count * stations,
            bytes_accessed=count * 8 * (rows + comps * samples) * stations,
        ),
        scratch_shapes=[
            pltpu.VMEM((2, rows, stations), pieces[0].dtype),
            pltpu.SemaphoreType.DMA((2,)),
            pltpu.VMEM((samples, stations), jnp.float32),
        ],
    )(own_pick, far_pick, sub_at, own_spec, own_energy[:, None, :], mask[:, None, :], *inverse,
      *pieces)


def spectra(forward, wide):
    samples = forward.shape[1]
    return jnp.einsum(
        "jt,ects->ecjs", forward[:, LAG:samples - LAG], wide, precision=lax.Precision.HIGH
    )


def by_xor(value, axis, flip):
    length = lax.axis_size(axis)
    return lax.ppermute(value, axis, [(i, i ^ flip) for i in range(length)])


def shards(waves, local_event, partner_event, station_mask):
    events, comps, samples, stations = waves.shape
    forward = forward_table(samples)
    table = inverse_table(samples, LAG)
    table_high = lax.reduce_precision(table, exponent_bits=8, mantissa_bits=7)
    inverse = (table_high.astype(jnp.bfloat16), (table - table_high).astype(jnp.bfloat16))
    region_len = lax.axis_size("region")
    sub_at = lax.axis_index("sub")

    inner = waves[:, :, LAG:samples - LAG, :]
    meta = jnp.concatenate(
        [station_mask[:, 1], local_event[:, 1:2], partner_event[:, 1:2]], axis=1
    )
    inner_wide = inner.astype(jnp.float32)
    inner_energy = jnp.sum(inner_wide * inner_wide, axis=(1, 2))
    sent_inner, sent_meta, sent_energy = lax.ppermute(
        (inner, meta, inner_energy), "region",
        [(i, (i - 1) % region_len) for i in range(region_len)],
    )

    wide = waves.astype(jnp.float32)
    spec = jnp.einsum("jt,ects->ecjs", forward, wide, precision=lax.Precision.HIGH)
    full_energy = jnp.sum(wide * wide, axis=(1, 2))
    body = spec.astype(jnp.bfloat16).reshape(events, comps * samples, stations)
    pieces = split_exact(full_energy)
    tail = jnp.pad(pieces, ((0, 0), (0, 16 - pieces.shape[1]), (0, 0)))
    packed = jnp.concatenate([body, tail], axis=1)

    near = by_xor(packed, "sub", 1)
    across = by_xor(packed, "sub", 2)
    pieces = [packed, near, across, None]
    sub_vec = jnp.full((1,), sub_at, jnp.int32)

    def prepare(own_inner, own_energy):
        return spectra(forward, own_inner.astype(jnp.float32)), own_energy

    def run(prepared, own_pick, far_pick, mask, allowed=(0, 1, 2, 3)):
        own_spec, own_energy = prepared
        own_pick = jnp.clip(own_pick, 0, events - 1)
        far_pick = jnp.clip(far_pick, 0, len(pieces) * events - 1)
        return correlate_round(
            own_spec, own_energy, tuple(pieces[j] for j in allowed), allowed, inverse,
            mask.astype(jnp.float32), own_pick, far_pick, sub_vec,
        )

    own_args = (prepare(inner, inner_energy), local_event[:, 0], partner_event[:, 0])
    sent_meta, sent_energy, own_mask = lax.optimization_barrier(
        (sent_meta, sent_energy, station_mask[:, 0])
    )
    mine = run(*own_args, own_mask, allowed=(0, 1))
    across, mine = lax.optimization_barrier((across, mine))
    pieces[2] = across
    ahead_spec = prepare(sent_inner, sent_energy)
    pieces[3], ahead_spec = lax.optimization_barrier((by_xor(across, "sub", 1), ahead_spec))

    ahead_pick = sent_meta[:, stations]
    ahead_far = sent_meta[:, stations + 1]
    ahead_mask = sent_meta[:, :stations]
    count = ahead_pick.shape[0]
    split = count // 2
    back = []
    for lo, hi in ((0, split), (split, count)):
        back.append(run(ahead_spec, ahead_pick[lo:hi], ahead_far[lo:hi], ahead_mask[lo:hi]))
    back[-1], own_mask = lax.optimization_barrier((back[-1], own_mask))
    back = [
        lax.ppermute(part, "region", [(i, (i + 1) % region_len) for i in range(region_len)])
        for part in back
    ]
    late = run(*own_args, own_mask, allowed=(2, 3))
    return jnp.stack([mine + late, jnp.concatenate(back, axis=0)], axis=1)


def solution(mesh):
    placed = (
        P(("region", "sub"), None, None, None),
        P(("region", "sub"), None),
        P(("region", "sub"), None),
        P(("region", "sub"), None, None),
    )
    return jax.shard_map(
        shards,
        mesh=mesh,
        in_specs=placed,
        out_specs=P(("region", "sub"), None, None, None),
        check_vma=False,
    )
```

```python
import functools
import math

import jax
import jax.numpy as jnp
from jax import lax
from jax.experimental import pallas as pl
from jax.experimental.pallas import tpu as pltpu
from jax.sharding import PartitionSpec as P

LAG = 50


def forward_table(samples):
    half = samples // 2
    sample_index = jnp.arange(samples, dtype=jnp.int32)
    orders = jnp.arange(half, dtype=jnp.int32)
    turn = 2.0 * math.pi / samples
    phase = (orders[:, None] * sample_index[None, :] % samples).astype(jnp.float32) * turn
    top = (half * sample_index % samples).astype(jnp.float32) * turn
    lower = jnp.concatenate([jnp.cos(top)[None, :], -jnp.sin(phase[1:])], axis=0)
    return jnp.concatenate([jnp.cos(phase), lower], axis=0)


def inverse_table(samples, reach):
    half = samples // 2
    orders = jnp.arange(half, dtype=jnp.int32)
    offsets = (jnp.arange(2 * reach + 1, dtype=jnp.int32) - reach + samples) % samples
    phase = (offsets[:, None] * orders[None, :] % samples).astype(jnp.float32) * (
        2.0 * math.pi / samples
    )
    parity = jnp.where(offsets % 2 == 0, 1.0, -1.0).astype(jnp.float32)
    scale = 2.0 / samples
    even = ((1.0 + parity) / (2.0 * samples))[:, None]
    odd = ((1.0 - parity) / (2.0 * samples))[:, None]
    cos_part = jnp.concatenate([even, scale * jnp.cos(phase[:, 1:])], axis=1)
    sin_part = jnp.concatenate([odd, -scale * jnp.sin(phase[:, 1:])], axis=1)
    table = jnp.concatenate([cos_part, sin_part], axis=1)
    rows = -(-table.shape[0] // 8) * 8
    return jnp.pad(table, ((0, rows - table.shape[0]), (0, 0)))


def split_exact(value):
    hi = lax.reduce_precision(value, exponent_bits=8, mantissa_bits=7)
    rest = value - hi
    mid = lax.reduce_precision(rest, exponent_bits=8, mantissa_bits=7)
    low = rest - mid
    return jnp.stack([hi, mid, low], axis=1).astype(jnp.bfloat16)


def round_kernel(allowed, a_ref, b_ref, u_ref, own_ref, oen_ref, mask_ref, inv_ref, inv_low_ref,
                 *rest):
    pieces = rest[:-2]
    out_ref, x_ref = rest[-2:]
    events, comps, samples, stations = own_ref.shape
    half = samples // 2
    body_rows = comps * samples
    count, lags = out_ref.shape[0], out_ref.shape[1]
    sub_at = u_ref[0]

    def piece_of(q):
        return jnp.bitwise_xor(b_ref[q] // events, sub_at)

    def wanted(q):
        piece = piece_of(q)
        hit = piece == allowed[0]
        for j in allowed[1:]:
            hit = hit | (piece == j)
        return hit

    def step(q, carry):
        piece = piece_of(q)
        event = b_ref[q] % events
        for j, source in zip(allowed, pieces):
            @pl.when(piece == j)
            def _():
                work(q, source, event)

        @pl.when(jnp.logical_not(wanted(q)))
        def _():
            out_ref[q] = jnp.zeros((lags, stations), jnp.float32)

        return carry

    def work(q, source, event):
        ai = a_ref[q]
        u = None
        v = None
        w = None
        for c in range(comps):
            own = own_ref[ai, c]
            far = source[event, c * samples:(c + 1) * samples, :].astype(jnp.float32)
            oa = own[:half]
            ob = own[half:]
            fa = far[:half]
            fb = far[half:]
            uc = oa * fa + ob * fb
            vc = oa * fb - ob * fa
            wc = oa[:8] * fa[:8] - ob[:8] * fb[:8]
            u = uc if u is None else u + uc
            v = vc if v is None else v + vc
            w = wc if w is None else w + wc
        first = lax.broadcasted_iota(jnp.int32, w.shape, 0) == 0
        x_ref[:half, :] = u
        x_ref[half:, :] = v
        x_ref[half:half + 8, :] = jnp.where(first, w, v[:8])
        x = x_ref[...]
        x_high = x.astype(jnp.bfloat16)
        x_low = (x - x_high.astype(jnp.float32)).astype(jnp.bfloat16)
        inv_high = inv_ref[...]
        raw = jnp.dot(inv_high, x_high, preferred_element_type=jnp.float32)
        raw = raw + jnp.dot(inv_high, x_low, preferred_element_type=jnp.float32)
        raw = raw + jnp.dot(inv_low_ref[...], x_high, preferred_element_type=jnp.float32)
        energy = jnp.sum(source[event, body_rows:body_rows + 16, :].astype(jnp.float32), axis=0,
                         keepdims=True)
        denom = jnp.sqrt(oen_ref[ai] * energy + 1e-06)
        out_ref[q] = raw[:lags] / denom * mask_ref[q]

    lax.fori_loop(0, count, step, 0)


def correlate_round(own_spec, own_energy, pieces, allowed, inverse, mask, own_pick, far_pick,
                    sub_at):
    count = own_pick.shape[0]
    events, comps, samples, stations = own_spec.shape
    rows = pieces[0].shape[1]
    lags = 2 * LAG + 1
    smem = pl.BlockSpec(memory_space=pltpu.SMEM)
    vmem = pl.BlockSpec(memory_space=pltpu.VMEM)
    hbm = pl.BlockSpec(memory_space=pl.ANY)
    return pl.pallas_call(
        functools.partial(round_kernel, allowed),
        in_specs=[smem, smem, smem, vmem, vmem, vmem, vmem, vmem] + [vmem] * len(pieces),
        out_specs=vmem,
        out_shape=jax.ShapeDtypeStruct((count, lags, stations), jnp.float32),
        cost_estimate=pl.CostEstimate(
            flops=count * 6 * 2 * 104 * samples * stations,
            transcendentals=count * stations,
            bytes_accessed=count * 8 * (rows + comps * samples) * stations,
        ),
        scratch_shapes=[
            pltpu.VMEM((samples, stations), jnp.float32),
        ],
    )(own_pick, far_pick, sub_at, own_spec, own_energy[:, None, :], mask[:, None, :], *inverse,
      *pieces)


def spectra(forward, wide):
    samples = forward.shape[1]
    return jnp.einsum(
        "jt,ects->ecjs", forward[:, LAG:samples - LAG], wide, precision=lax.Precision.HIGH
    )


def by_xor(value, axis, flip):
    length = lax.axis_size(axis)
    return lax.ppermute(value, axis, [(i, i ^ flip) for i in range(length)])


def shards(waves, local_event, partner_event, station_mask):
    events, comps, samples, stations = waves.shape
    forward = forward_table(samples)
    table = inverse_table(samples, LAG)
    table_high = lax.reduce_precision(table, exponent_bits=8, mantissa_bits=7)
    inverse = (table_high.astype(jnp.bfloat16), (table - table_high).astype(jnp.bfloat16))
    region_len = lax.axis_size("region")
    sub_at = lax.axis_index("sub")

    inner = waves[:, :, LAG:samples - LAG, :]
    meta = jnp.concatenate(
        [station_mask[:, 1], local_event[:, 1:2], partner_event[:, 1:2]], axis=1
    )
    inner_wide = inner.astype(jnp.float32)
    inner_energy = jnp.sum(inner_wide * inner_wide, axis=(1, 2))
    sent_inner, sent_meta, sent_energy = lax.ppermute(
        (inner, meta, inner_energy), "region",
        [(i, (i - 1) % region_len) for i in range(region_len)],
    )

    wide = waves.astype(jnp.float32)
    spec = jnp.einsum("jt,ects->ecjs", forward, wide, precision=lax.Precision.HIGH)
    full_energy = jnp.sum(wide * wide, axis=(1, 2))
    body = spec.astype(jnp.bfloat16).reshape(events, comps * samples, stations)
    pieces = split_exact(full_energy)
    tail = jnp.pad(pieces, ((0, 0), (0, 16 - pieces.shape[1]), (0, 0)))
    packed = jnp.concatenate([body, tail], axis=1)

    near = by_xor(packed, "sub", 1)
    across = by_xor(packed, "sub", 2)
    pieces = [packed, near, across, None]
    sub_vec = jnp.full((1,), sub_at, jnp.int32)

    def prepare(own_inner, own_energy):
        return spectra(forward, own_inner.astype(jnp.float32)), own_energy

    def run(prepared, own_pick, far_pick, mask, allowed=(0, 1, 2, 3)):
        own_spec, own_energy = prepared
        own_pick = jnp.clip(own_pick, 0, events - 1)
        far_pick = jnp.clip(far_pick, 0, len(pieces) * events - 1)
        return correlate_round(
            own_spec, own_energy, tuple(pieces[j] for j in allowed), allowed, inverse,
            mask.astype(jnp.float32), own_pick, far_pick, sub_vec,
        )

    own_args = (prepare(inner, inner_energy), local_event[:, 0], partner_event[:, 0])
    sent_meta, sent_energy, own_mask = lax.optimization_barrier(
        (sent_meta, sent_energy, station_mask[:, 0])
    )
    mine = run(*own_args, own_mask, allowed=(0, 1))
    across, mine = lax.optimization_barrier((across, mine))
    pieces[2] = across
    ahead_spec = prepare(sent_inner, sent_energy)
    pieces[3], ahead_spec = lax.optimization_barrier((by_xor(across, "sub", 1), ahead_spec))

    ahead_pick = sent_meta[:, stations]
    ahead_far = sent_meta[:, stations + 1]
    ahead_mask = sent_meta[:, :stations]
    count = ahead_pick.shape[0]
    split = count // 2
    back = []
    for lo, hi in ((0, split), (split, count)):
        back.append(run(ahead_spec, ahead_pick[lo:hi], ahead_far[lo:hi], ahead_mask[lo:hi]))
    back[-1], own_mask = lax.optimization_barrier((back[-1], own_mask))
    back = [
        lax.ppermute(part, "region", [(i, (i + 1) % region_len) for i in range(region_len)])
        for part in back
    ]
    late = run(*own_args, own_mask, allowed=(2, 3))
    return jnp.stack([mine + late, jnp.concatenate(back, axis=0)], axis=1)


def solution(mesh):
    placed = (
        P(("region", "sub"), None, None, None),
        P(("region", "sub"), None),
        P(("region", "sub"), None),
        P(("region", "sub"), None, None),
    )
    return jax.shard_map(
        shards,
        mesh=mesh,
        in_specs=placed,
        out_specs=P(("region", "sub"), None, None, None),
        check_vma=False,
    )
```

```python
import functools
import math

import jax
import jax.numpy as jnp
from jax import lax
from jax.experimental import pallas as pl
from jax.experimental.pallas import tpu as pltpu
from jax.sharding import PartitionSpec as P

LAG = 50


def forward_table(samples):
    half = samples // 2
    sample_index = jnp.arange(samples, dtype=jnp.int32)
    orders = jnp.arange(half, dtype=jnp.int32)
    turn = 2.0 * math.pi / samples
    phase = (orders[:, None] * sample_index[None, :] % samples).astype(jnp.float32) * turn
    top = (half * sample_index % samples).astype(jnp.float32) * turn
    lower = jnp.concatenate([jnp.cos(top)[None, :], -jnp.sin(phase[1:])], axis=0)
    return jnp.concatenate([jnp.cos(phase), lower], axis=0)


def inverse_table(samples, reach):
    half = samples // 2
    orders = jnp.arange(half, dtype=jnp.int32)
    offsets = (jnp.arange(2 * reach + 1, dtype=jnp.int32) - reach + samples) % samples
    phase = (offsets[:, None] * orders[None, :] % samples).astype(jnp.float32) * (
        2.0 * math.pi / samples
    )
    parity = jnp.where(offsets % 2 == 0, 1.0, -1.0).astype(jnp.float32)
    scale = 2.0 / samples
    even = ((1.0 + parity) / (2.0 * samples))[:, None]
    odd = ((1.0 - parity) / (2.0 * samples))[:, None]
    cos_part = jnp.concatenate([even, scale * jnp.cos(phase[:, 1:])], axis=1)
    sin_part = jnp.concatenate([odd, -scale * jnp.sin(phase[:, 1:])], axis=1)
    table = jnp.concatenate([cos_part, sin_part], axis=1)
    rows = -(-table.shape[0] // 8) * 8
    return jnp.pad(table, ((0, rows - table.shape[0]), (0, 0)))


def split_exact(value):
    hi = lax.reduce_precision(value, exponent_bits=8, mantissa_bits=7)
    rest = value - hi
    mid = lax.reduce_precision(rest, exponent_bits=8, mantissa_bits=7)
    low = rest - mid
    return jnp.stack([hi, mid, low], axis=1).astype(jnp.bfloat16)


def round_kernel(allowed, a_ref, b_ref, u_ref, own_ref, oen_ref, mask_ref, inv_ref, inv_low_ref,
                 *rest):
    pieces = rest[:-2]
    out_ref, x_ref = rest[-2:]
    events, comps, samples, stations = own_ref.shape
    half = samples // 2
    body_rows = comps * samples
    count, lags = out_ref.shape[0], out_ref.shape[1]
    sub_at = u_ref[0]

    def piece_of(q):
        return jnp.bitwise_xor(b_ref[q] // events, sub_at)

    def wanted(q):
        piece = piece_of(q)
        hit = piece == allowed[0]
        for j in allowed[1:]:
            hit = hit | (piece == j)
        return hit

    def step(q, carry):
        piece = piece_of(q)
        event = b_ref[q] % events
        for j, source in zip(allowed, pieces):
            @pl.when(piece == j)
            def _():
                work(q, source, event)

        @pl.when(jnp.logical_not(wanted(q)))
        def _():
            out_ref[q] = jnp.zeros((lags, stations), jnp.float32)

        return carry

    def work(q, source, event):
        ai = a_ref[q]
        u = None
        v = None
        w = None
        for c in range(comps):
            own = own_ref[ai, c]
            far = source[event, c * samples:(c + 1) * samples, :].astype(jnp.float32)
            oa = own[:half]
            ob = own[half:]
            fa = far[:half]
            fb = far[half:]
            uc = oa * fa + ob * fb
            vc = oa * fb - ob * fa
            wc = oa[:8] * fa[:8] - ob[:8] * fb[:8]
            u = uc if u is None else u + uc
            v = vc if v is None else v + vc
            w = wc if w is None else w + wc
        first = lax.broadcasted_iota(jnp.int32, w.shape, 0) == 0
        x_ref[:half, :] = u
        x_ref[half:, :] = v
        x_ref[half:half + 8, :] = jnp.where(first, w, v[:8])
        x = x_ref[...]
        x_high = x.astype(jnp.bfloat16)
        x_low = (x - x_high.astype(jnp.float32)).astype(jnp.bfloat16)
        inv_high = inv_ref[...]
        raw = jnp.dot(inv_high, x_high, preferred_element_type=jnp.float32)
        raw = raw + jnp.dot(inv_high, x_low, preferred_element_type=jnp.float32)
        raw = raw + jnp.dot(inv_low_ref[...], x_high, preferred_element_type=jnp.float32)
        energy = jnp.sum(source[event, body_rows:body_rows + 16, :].astype(jnp.float32), axis=0,
                         keepdims=True)
        denom = jnp.sqrt(oen_ref[ai] * energy + 1e-06)
        out_ref[q] = raw[:lags] / denom * mask_ref[q]

    lax.fori_loop(0, count, step, 0)


def correlate_round(own_spec, own_energy, pieces, allowed, inverse, mask, own_pick, far_pick,
                    sub_at):
    count = own_pick.shape[0]
    events, comps, samples, stations = own_spec.shape
    rows = pieces[0].shape[1]
    lags = 2 * LAG + 1
    smem = pl.BlockSpec(memory_space=pltpu.SMEM)
    vmem = pl.BlockSpec(memory_space=pltpu.VMEM)
    hbm = pl.BlockSpec(memory_space=pl.ANY)
    return pl.pallas_call(
        functools.partial(round_kernel, allowed),
        in_specs=[smem, smem, smem, vmem, vmem, vmem, vmem, vmem] + [vmem] * len(pieces),
        out_specs=vmem,
        out_shape=jax.ShapeDtypeStruct((count, lags, stations), jnp.float32),
        cost_estimate=pl.CostEstimate(
            flops=count * 6 * 2 * 104 * samples * stations,
            transcendentals=count * stations,
            bytes_accessed=count * 8 * (rows + comps * samples) * stations,
        ),
        scratch_shapes=[
            pltpu.VMEM((samples, stations), jnp.float32),
        ],
    )(own_pick, far_pick, sub_at, own_spec, own_energy[:, None, :], mask[:, None, :], *inverse,
      *pieces)


def spectra(forward, wide):
    samples = forward.shape[1]
    return jnp.einsum(
        "jt,ects->ecjs", forward[:, LAG:samples - LAG], wide, precision=lax.Precision.HIGH
    )


def by_xor(value, axis, flip):
    length = lax.axis_size(axis)
    return lax.ppermute(value, axis, [(i, i ^ flip) for i in range(length)])


def shards(waves, local_event, partner_event, station_mask):
    events, comps, samples, stations = waves.shape
    forward = forward_table(samples)
    table = inverse_table(samples, LAG)
    table_high = lax.reduce_precision(table, exponent_bits=8, mantissa_bits=7)
    inverse = (table_high.astype(jnp.bfloat16), (table - table_high).astype(jnp.bfloat16))
    region_len = lax.axis_size("region")
    sub_at = lax.axis_index("sub")

    inner = waves[:, :, LAG:samples - LAG, :]
    meta = jnp.concatenate(
        [station_mask[:, 1], local_event[:, 1:2], partner_event[:, 1:2]], axis=1
    )
    inner_wide = inner.astype(jnp.float32)
    inner_energy = jnp.sum(inner_wide * inner_wide, axis=(1, 2))
    sent_inner, sent_meta, sent_energy = lax.ppermute(
        (inner, meta, inner_energy), "region",
        [(i, (i - 1) % region_len) for i in range(region_len)],
    )

    wide = waves.astype(jnp.float32)
    spec = jnp.einsum("jt,ects->ecjs", forward, wide, precision=lax.Precision.HIGH)
    full_energy = jnp.sum(wide * wide, axis=(1, 2))
    body = spec.astype(jnp.bfloat16).reshape(events, comps * samples, stations)
    pieces = split_exact(full_energy)
    tail = jnp.pad(pieces, ((0, 0), (0, 16 - pieces.shape[1]), (0, 0)))
    packed = jnp.concatenate([body, tail], axis=1)

    near = by_xor(packed, "sub", 1)
    across = by_xor(packed, "sub", 2)
    pieces = [packed, near, across, None]
    sub_vec = jnp.full((1,), sub_at, jnp.int32)

    def prepare(own_inner, own_energy):
        return spectra(forward, own_inner.astype(jnp.float32)), own_energy

    def run(prepared, own_pick, far_pick, mask, allowed=(0, 1, 2, 3)):
        own_spec, own_energy = prepared
        own_pick = jnp.clip(own_pick, 0, events - 1)
        far_pick = jnp.clip(far_pick, 0, len(pieces) * events - 1)
        return correlate_round(
            own_spec, own_energy, tuple(pieces[j] for j in allowed), allowed, inverse,
            mask.astype(jnp.float32), own_pick, far_pick, sub_vec,
        )

    own_args = (prepare(inner, inner_energy), local_event[:, 0], partner_event[:, 0])
    sent_meta, sent_energy, own_mask = lax.optimization_barrier(
        (sent_meta, sent_energy, station_mask[:, 0])
    )
    mine = run(*own_args, own_mask, allowed=(0, 1))
    across, mine = lax.optimization_barrier((across, mine))
    pieces[2] = across
    ahead_spec = prepare(sent_inner, sent_energy)
    pieces[3], ahead_spec = lax.optimization_barrier((by_xor(across, "sub", 1), ahead_spec))

    ahead_pick = sent_meta[:, stations]
    ahead_far = sent_meta[:, stations + 1]
    ahead_mask = sent_meta[:, :stations]
    count = ahead_pick.shape[0]
    split = count // 4
    back = []
    for lo, hi in ((0, split), (split, count)):
        back.append(run(ahead_spec, ahead_pick[lo:hi], ahead_far[lo:hi], ahead_mask[lo:hi]))
    back[-1], own_mask = lax.optimization_barrier((back[-1], own_mask))
    back = [
        lax.ppermute(part, "region", [(i, (i + 1) % region_len) for i in range(region_len)])
        for part in back
    ]
    late = run(*own_args, own_mask, allowed=(2, 3))
    return jnp.stack([mine + late, jnp.concatenate(back, axis=0)], axis=1)


def solution(mesh):
    placed = (
        P(("region", "sub"), None, None, None),
        P(("region", "sub"), None),
        P(("region", "sub"), None),
        P(("region", "sub"), None, None),
    )
    return jax.shard_map(
        shards,
        mesh=mesh,
        in_specs=placed,
        out_specs=P(("region", "sub"), None, None, None),
        check_vma=False,
    )
```

```python
import functools
import math

import jax
import jax.numpy as jnp
from jax import lax
from jax.experimental import pallas as pl
from jax.experimental.pallas import tpu as pltpu
from jax.sharding import PartitionSpec as P

LAG = 50


def forward_table(samples):
    half = samples // 2
    sample_index = jnp.arange(samples, dtype=jnp.int32)
    orders = jnp.arange(half, dtype=jnp.int32)
    turn = 2.0 * math.pi / samples
    phase = (orders[:, None] * sample_index[None, :] % samples).astype(jnp.float32) * turn
    top = (half * sample_index % samples).astype(jnp.float32) * turn
    lower = jnp.concatenate([jnp.cos(top)[None, :], -jnp.sin(phase[1:])], axis=0)
    return jnp.concatenate([jnp.cos(phase), lower], axis=0)


def inverse_table(samples, reach):
    half = samples // 2
    orders = jnp.arange(half, dtype=jnp.int32)
    offsets = (jnp.arange(2 * reach + 1, dtype=jnp.int32) - reach + samples) % samples
    phase = (offsets[:, None] * orders[None, :] % samples).astype(jnp.float32) * (
        2.0 * math.pi / samples
    )
    parity = jnp.where(offsets % 2 == 0, 1.0, -1.0).astype(jnp.float32)
    scale = 2.0 / samples
    even = ((1.0 + parity) / (2.0 * samples))[:, None]
    odd = ((1.0 - parity) / (2.0 * samples))[:, None]
    cos_part = jnp.concatenate([even, scale * jnp.cos(phase[:, 1:])], axis=1)
    sin_part = jnp.concatenate([odd, -scale * jnp.sin(phase[:, 1:])], axis=1)
    table = jnp.concatenate([cos_part, sin_part], axis=1)
    rows = -(-table.shape[0] // 8) * 8
    return jnp.pad(table, ((0, rows - table.shape[0]), (0, 0)))


def split_exact(value):
    hi = lax.reduce_precision(value, exponent_bits=8, mantissa_bits=7)
    rest = value - hi
    mid = lax.reduce_precision(rest, exponent_bits=8, mantissa_bits=7)
    low = rest - mid
    return jnp.stack([hi, mid, low], axis=1).astype(jnp.bfloat16)


def round_kernel(allowed, a_ref, b_ref, u_ref, own_ref, oen_ref, mask_ref, inv_ref, inv_low_ref,
                 *rest):
    pieces = rest[:-2]
    out_ref, x_ref = rest[-2:]
    events, comps, samples, stations = own_ref.shape
    half = samples // 2
    body_rows = comps * samples
    count, lags = out_ref.shape[0], out_ref.shape[1]
    sub_at = u_ref[0]

    def piece_of(q):
        return jnp.bitwise_xor(b_ref[q] // events, sub_at)

    def wanted(q):
        piece = piece_of(q)
        hit = piece == allowed[0]
        for j in allowed[1:]:
            hit = hit | (piece == j)
        return hit

    def step(q, carry):
        piece = piece_of(q)
        event = b_ref[q] % events
        for j, source in zip(allowed, pieces):
            @pl.when(piece == j)
            def _():
                work(q, source, event)

        @pl.when(jnp.logical_not(wanted(q)))
        def _():
            out_ref[q] = jnp.zeros((lags, stations), jnp.float32)

        return carry

    def work(q, source, event):
        ai = a_ref[q]
        u = None
        v = None
        w = None
        for c in range(comps):
            own = own_ref[ai, c]
            far = source[event, c * samples:(c + 1) * samples, :].astype(jnp.float32)
            oa = own[:half]
            ob = own[half:]
            fa = far[:half]
            fb = far[half:]
            uc = oa * fa + ob * fb
            vc = oa * fb - ob * fa
            wc = oa[:8] * fa[:8] - ob[:8] * fb[:8]
            u = uc if u is None else u + uc
            v = vc if v is None else v + vc
            w = wc if w is None else w + wc
        first = lax.broadcasted_iota(jnp.int32, w.shape, 0) == 0
        x_ref[:half, :] = u
        x_ref[half:, :] = v
        x_ref[half:half + 8, :] = jnp.where(first, w, v[:8])
        x = x_ref[...]
        x_high = x.astype(jnp.bfloat16)
        x_low = (x - x_high.astype(jnp.float32)).astype(jnp.bfloat16)
        inv_high = inv_ref[...]
        raw = jnp.dot(inv_high, x_high, preferred_element_type=jnp.float32)
        raw = raw + jnp.dot(inv_high, x_low, preferred_element_type=jnp.float32)
        raw = raw + jnp.dot(inv_low_ref[...], x_high, preferred_element_type=jnp.float32)
        energy = jnp.sum(source[event, body_rows:body_rows + 16, :].astype(jnp.float32), axis=0,
                         keepdims=True)
        denom = jnp.sqrt(oen_ref[ai] * energy + 1e-06)
        out_ref[q] = raw[:lags] / denom * mask_ref[q]

    lax.fori_loop(0, count, step, 0)


def correlate_round(own_spec, own_energy, pieces, allowed, inverse, mask, own_pick, far_pick,
                    sub_at):
    count = own_pick.shape[0]
    events, comps, samples, stations = own_spec.shape
    rows = pieces[0].shape[1]
    lags = 2 * LAG + 1
    smem = pl.BlockSpec(memory_space=pltpu.SMEM)
    vmem = pl.BlockSpec(memory_space=pltpu.VMEM)
    hbm = pl.BlockSpec(memory_space=pl.ANY)
    return pl.pallas_call(
        functools.partial(round_kernel, allowed),
        in_specs=[smem, smem, smem, vmem, vmem, vmem, vmem, vmem] + [vmem] * len(pieces),
        out_specs=vmem,
        out_shape=jax.ShapeDtypeStruct((count, lags, stations), jnp.float32),
        cost_estimate=pl.CostEstimate(
            flops=count * 6 * 2 * 104 * samples * stations,
            transcendentals=count * stations,
            bytes_accessed=count * 8 * (rows + comps * samples) * stations,
        ),
        scratch_shapes=[
            pltpu.VMEM((samples, stations), jnp.float32),
        ],
    )(own_pick, far_pick, sub_at, own_spec, own_energy[:, None, :], mask[:, None, :], *inverse,
      *pieces)


def spectra(forward, wide):
    samples = forward.shape[1]
    return jnp.einsum(
        "jt,ects->ecjs", forward[:, LAG:samples - LAG], wide, precision=lax.Precision.HIGH
    )


def by_xor(value, axis, flip):
    length = lax.axis_size(axis)
    return lax.ppermute(value, axis, [(i, i ^ flip) for i in range(length)])


def shards(waves, local_event, partner_event, station_mask):
    events, comps, samples, stations = waves.shape
    forward = forward_table(samples)
    table = inverse_table(samples, LAG)
    table_high = lax.reduce_precision(table, exponent_bits=8, mantissa_bits=7)
    inverse = (table_high.astype(jnp.bfloat16), (table - table_high).astype(jnp.bfloat16))
    region_len = lax.axis_size("region")
    sub_at = lax.axis_index("sub")

    inner = waves[:, :, LAG:samples - LAG, :]
    meta = jnp.concatenate(
        [station_mask[:, 1], local_event[:, 1:2], partner_event[:, 1:2]], axis=1
    )
    inner_wide = inner.astype(jnp.float32)
    inner_energy = jnp.sum(inner_wide * inner_wide, axis=(1, 2))
    sent_inner, sent_meta, sent_energy = lax.ppermute(
        (inner, meta, inner_energy), "region",
        [(i, (i - 1) % region_len) for i in range(region_len)],
    )

    wide = waves.astype(jnp.float32)
    spec = jnp.einsum("jt,ects->ecjs", forward, wide, precision=lax.Precision.HIGH)
    full_energy = jnp.sum(wide * wide, axis=(1, 2))
    body = spec.astype(jnp.bfloat16).reshape(events, comps * samples, stations)
    pieces = split_exact(full_energy)
    tail = jnp.pad(pieces, ((0, 0), (0, 16 - pieces.shape[1]), (0, 0)))
    packed = jnp.concatenate([body, tail], axis=1)

    near = by_xor(packed, "sub", 1)
    across = by_xor(packed, "sub", 2)
    pieces = [packed, near, across, None]
    sub_vec = jnp.full((1,), sub_at, jnp.int32)

    def prepare(own_inner, own_energy):
        return spectra(forward, own_inner.astype(jnp.float32)), own_energy

    def run(prepared, own_pick, far_pick, mask, allowed=(0, 1, 2, 3)):
        own_spec, own_energy = prepared
        own_pick = jnp.clip(own_pick, 0, events - 1)
        far_pick = jnp.clip(far_pick, 0, len(pieces) * events - 1)
        return correlate_round(
            own_spec, own_energy, tuple(pieces[j] for j in allowed), allowed, inverse,
            mask.astype(jnp.float32), own_pick, far_pick, sub_vec,
        )

    own_args = (prepare(inner, inner_energy), local_event[:, 0], partner_event[:, 0])
    sent_meta, sent_energy, own_mask = lax.optimization_barrier(
        (sent_meta, sent_energy, station_mask[:, 0])
    )
    mine = run(*own_args, own_mask, allowed=(0, 1))
    across, mine = lax.optimization_barrier((across, mine))
    pieces[2] = across
    ahead_spec = prepare(sent_inner, sent_energy)
    pieces[3], ahead_spec = lax.optimization_barrier((by_xor(across, "sub", 1), ahead_spec))

    ahead_pick = sent_meta[:, stations]
    ahead_far = sent_meta[:, stations + 1]
    ahead_mask = sent_meta[:, :stations]
    count = ahead_pick.shape[0]
    split = count // 4
    back = []
    rest_mask = ahead_mask[split:]
    for lo, hi in ((0, split), (split, count)):
        part_mask = ahead_mask[:split] if lo == 0 else rest_mask
        part = run(ahead_spec, ahead_pick[lo:hi], ahead_far[lo:hi], part_mask)
        if lo == 0:
            part, rest_mask = lax.optimization_barrier((part, rest_mask))
        else:
            part, own_mask = lax.optimization_barrier((part, own_mask))
        back.append(
            lax.ppermute(part, "region", [(i, (i + 1) % region_len) for i in range(region_len)])
        )
    late = run(*own_args, own_mask, allowed=(2, 3))
    return jnp.stack([mine + late, jnp.concatenate(back, axis=0)], axis=1)


def solution(mesh):
    placed = (
        P(("region", "sub"), None, None, None),
        P(("region", "sub"), None),
        P(("region", "sub"), None),
        P(("region", "sub"), None, None),
    )
    return jax.shard_map(
        shards,
        mesh=mesh,
        in_specs=placed,
        out_specs=P(("region", "sub"), None, None, None),
        check_vma=False,
    )
```

```python
import functools
import math

import jax
import jax.numpy as jnp
from jax import lax
from jax.experimental import pallas as pl
from jax.experimental.pallas import tpu as pltpu
from jax.sharding import PartitionSpec as P

LAG = 50


def forward_table(samples):
    half = samples // 2
    sample_index = jnp.arange(samples, dtype=jnp.int32)
    orders = jnp.arange(half, dtype=jnp.int32)
    turn = 2.0 * math.pi / samples
    phase = (orders[:, None] * sample_index[None, :] % samples).astype(jnp.float32) * turn
    top = (half * sample_index % samples).astype(jnp.float32) * turn
    lower = jnp.concatenate([jnp.cos(top)[None, :], -jnp.sin(phase[1:])], axis=0)
    return jnp.concatenate([jnp.cos(phase), lower], axis=0)


def inverse_table(samples, reach):
    half = samples // 2
    orders = jnp.arange(half, dtype=jnp.int32)
    offsets = (jnp.arange(2 * reach + 1, dtype=jnp.int32) - reach + samples) % samples
    phase = (offsets[:, None] * orders[None, :] % samples).astype(jnp.float32) * (
        2.0 * math.pi / samples
    )
    parity = jnp.where(offsets % 2 == 0, 1.0, -1.0).astype(jnp.float32)
    scale = 2.0 / samples
    even = ((1.0 + parity) / (2.0 * samples))[:, None]
    odd = ((1.0 - parity) / (2.0 * samples))[:, None]
    cos_part = jnp.concatenate([even, scale * jnp.cos(phase[:, 1:])], axis=1)
    sin_part = jnp.concatenate([odd, -scale * jnp.sin(phase[:, 1:])], axis=1)
    table = jnp.concatenate([cos_part, sin_part], axis=1)
    rows = -(-table.shape[0] // 8) * 8
    return jnp.pad(table, ((0, rows - table.shape[0]), (0, 0)))


def split_exact(value):
    hi = lax.reduce_precision(value, exponent_bits=8, mantissa_bits=7)
    rest = value - hi
    mid = lax.reduce_precision(rest, exponent_bits=8, mantissa_bits=7)
    low = rest - mid
    return jnp.stack([hi, mid, low], axis=1).astype(jnp.bfloat16)


def round_kernel(allowed, a_ref, b_ref, u_ref, own_ref, oen_ref, mask_ref, inv_ref, inv_low_ref,
                 *rest):
    pieces = rest[:-2]
    out_ref, x_ref = rest[-2:]
    events, comps, samples, stations = own_ref.shape
    half = samples // 2
    body_rows = comps * samples
    count, lags = out_ref.shape[0], out_ref.shape[1]
    sub_at = u_ref[0]

    def piece_of(q):
        return jnp.bitwise_xor(b_ref[q] // events, sub_at)

    def wanted(q):
        piece = piece_of(q)
        hit = piece == allowed[0]
        for j in allowed[1:]:
            hit = hit | (piece == j)
        return hit

    def step(q, carry):
        piece = piece_of(q)
        event = b_ref[q] % events
        for j, source in zip(allowed, pieces):
            @pl.when(piece == j)
            def _():
                work(q, source, event)

        @pl.when(jnp.logical_not(wanted(q)))
        def _():
            out_ref[q] = jnp.zeros((lags, stations), jnp.float32)

        return carry

    def work(q, source, event):
        ai = a_ref[q]
        u = None
        v = None
        w = None
        for c in range(comps):
            own = own_ref[ai, c]
            far = source[event, c * samples:(c + 1) * samples, :].astype(jnp.float32)
            oa = own[:half]
            ob = own[half:]
            fa = far[:half]
            fb = far[half:]
            uc = oa * fa + ob * fb
            vc = oa * fb - ob * fa
            wc = oa[:8] * fa[:8] - ob[:8] * fb[:8]
            u = uc if u is None else u + uc
            v = vc if v is None else v + vc
            w = wc if w is None else w + wc
        first = lax.broadcasted_iota(jnp.int32, w.shape, 0) == 0
        x_ref[:half, :] = u
        x_ref[half:, :] = v
        x_ref[half:half + 8, :] = jnp.where(first, w, v[:8])
        x = x_ref[...]
        x_high = x.astype(jnp.bfloat16)
        x_low = (x - x_high.astype(jnp.float32)).astype(jnp.bfloat16)
        inv_high = inv_ref[...]
        raw = jnp.dot(inv_high, x_high, preferred_element_type=jnp.float32)
        raw = raw + jnp.dot(inv_high, x_low, preferred_element_type=jnp.float32)
        raw = raw + jnp.dot(inv_low_ref[...], x_high, preferred_element_type=jnp.float32)
        energy = jnp.sum(source[event, body_rows:body_rows + 16, :].astype(jnp.float32), axis=0,
                         keepdims=True)
        denom = jnp.sqrt(oen_ref[ai] * energy + 1e-06)
        out_ref[q] = raw[:lags] / denom * mask_ref[q]

    lax.fori_loop(0, count, step, 0)


def correlate_round(own_spec, own_energy, pieces, allowed, inverse, mask, own_pick, far_pick,
                    sub_at):
    count = own_pick.shape[0]
    events, comps, samples, stations = own_spec.shape
    rows = pieces[0].shape[1]
    lags = 2 * LAG + 1
    smem = pl.BlockSpec(memory_space=pltpu.SMEM)
    vmem = pl.BlockSpec(memory_space=pltpu.VMEM)
    hbm = pl.BlockSpec(memory_space=pl.ANY)
    return pl.pallas_call(
        functools.partial(round_kernel, allowed),
        in_specs=[smem, smem, smem, vmem, vmem, vmem, vmem, vmem] + [vmem] * len(pieces),
        out_specs=vmem,
        out_shape=jax.ShapeDtypeStruct((count, lags, stations), jnp.float32),
        cost_estimate=pl.CostEstimate(
            flops=count * 6 * 2 * 104 * samples * stations,
            transcendentals=count * stations,
            bytes_accessed=count * 8 * (rows + comps * samples) * stations,
        ),
        scratch_shapes=[
            pltpu.VMEM((samples, stations), jnp.float32),
        ],
    )(own_pick, far_pick, sub_at, own_spec, own_energy[:, None, :], mask[:, None, :], *inverse,
      *pieces)


def spectra(forward, wide):
    samples = forward.shape[1]
    return jnp.einsum(
        "jt,ects->ecjs", forward[:, LAG:samples - LAG], wide, precision=lax.Precision.HIGH
    )


def by_xor(value, axis, flip):
    length = lax.axis_size(axis)
    return lax.ppermute(value, axis, [(i, i ^ flip) for i in range(length)])


def shards(waves, local_event, partner_event, station_mask):
    events, comps, samples, stations = waves.shape
    forward = forward_table(samples)
    table = inverse_table(samples, LAG)
    table_high = lax.reduce_precision(table, exponent_bits=8, mantissa_bits=7)
    inverse = (table_high.astype(jnp.bfloat16), (table - table_high).astype(jnp.bfloat16))
    region_len = lax.axis_size("region")
    sub_at = lax.axis_index("sub")

    inner = waves[:, :, LAG:samples - LAG, :]
    meta = jnp.concatenate(
        [station_mask[:, 1], local_event[:, 1:2], partner_event[:, 1:2]], axis=1
    )
    inner_wide = inner.astype(jnp.float32)
    inner_energy = jnp.sum(inner_wide * inner_wide, axis=(1, 2))
    sent_inner, sent_meta, sent_energy = lax.ppermute(
        (inner, meta, inner_energy), "region",
        [(i, (i - 1) % region_len) for i in range(region_len)],
    )

    wide = waves.astype(jnp.float32)
    spec = jnp.einsum("jt,ects->ecjs", forward, wide, precision=lax.Precision.HIGH)
    full_energy = jnp.sum(wide * wide, axis=(1, 2))
    body = spec.astype(jnp.bfloat16).reshape(events, comps * samples, stations)
    pieces = split_exact(full_energy)
    tail = jnp.pad(pieces, ((0, 0), (0, 16 - pieces.shape[1]), (0, 0)))
    packed = jnp.concatenate([body, tail], axis=1)

    near = by_xor(packed, "sub", 1)
    across = by_xor(packed, "sub", 2)
    pieces = [packed, near, across, None]
    sub_vec = jnp.full((1,), sub_at, jnp.int32)

    def prepare(own_inner, own_energy):
        return spectra(forward, own_inner.astype(jnp.float32)), own_energy

    def run(prepared, own_pick, far_pick, mask, allowed=(0, 1, 2, 3)):
        own_spec, own_energy = prepared
        own_pick = jnp.clip(own_pick, 0, events - 1)
        far_pick = jnp.clip(far_pick, 0, len(pieces) * events - 1)
        return correlate_round(
            own_spec, own_energy, tuple(pieces[j] for j in allowed), allowed, inverse,
            mask.astype(jnp.float32), own_pick, far_pick, sub_vec,
        )

    own_args = (prepare(inner, inner_energy), local_event[:, 0], partner_event[:, 0])
    sent_meta, sent_energy, own_mask = lax.optimization_barrier(
        (sent_meta, sent_energy, station_mask[:, 0])
    )
    mine = run(*own_args, own_mask, allowed=(0, 1))
    across, mine = lax.optimization_barrier((across, mine))
    pieces[2] = across
    ahead_spec = prepare(sent_inner, sent_energy)
    pieces[3], ahead_spec = lax.optimization_barrier((by_xor(across, "sub", 1), ahead_spec))

    ahead_pick = sent_meta[:, stations]
    ahead_far = sent_meta[:, stations + 1]
    ahead_mask = sent_meta[:, :stations]
    count = ahead_pick.shape[0]
    split = count // 2
    back = []
    for lo, hi in ((0, split), (split, count)):
        back.append(run(ahead_spec, ahead_pick[lo:hi], ahead_far[lo:hi], ahead_mask[lo:hi]))
    back[-1], own_mask = lax.optimization_barrier((back[-1], own_mask))
    back = [
        lax.ppermute(
            part.astype(jnp.bfloat16), "region",
            [(i, (i + 1) % region_len) for i in range(region_len)],
        ).astype(jnp.float32)
        for part in back
    ]
    late = run(*own_args, own_mask, allowed=(2, 3))
    return jnp.stack([mine + late, jnp.concatenate(back, axis=0)], axis=1)


def solution(mesh):
    placed = (
        P(("region", "sub"), None, None, None),
        P(("region", "sub"), None),
        P(("region", "sub"), None),
        P(("region", "sub"), None, None),
    )
    return jax.shard_map(
        shards,
        mesh=mesh,
        in_specs=placed,
        out_specs=P(("region", "sub"), None, None, None),
        check_vma=False,
    )
```

```python
import functools
import math

import jax
import jax.numpy as jnp
from jax import lax
from jax.experimental import pallas as pl
from jax.experimental.pallas import tpu as pltpu
from jax.sharding import PartitionSpec as P

LAG = 50


def forward_table(samples):
    half = samples // 2
    sample_index = jnp.arange(samples, dtype=jnp.int32)
    orders = jnp.arange(half, dtype=jnp.int32)
    turn = 2.0 * math.pi / samples
    phase = (orders[:, None] * sample_index[None, :] % samples).astype(jnp.float32) * turn
    top = (half * sample_index % samples).astype(jnp.float32) * turn
    lower = jnp.concatenate([jnp.cos(top)[None, :], -jnp.sin(phase[1:])], axis=0)
    return jnp.concatenate([jnp.cos(phase), lower], axis=0)


def inverse_table(samples, reach):
    half = samples // 2
    orders = jnp.arange(half, dtype=jnp.int32)
    offsets = (jnp.arange(2 * reach + 1, dtype=jnp.int32) - reach + samples) % samples
    phase = (offsets[:, None] * orders[None, :] % samples).astype(jnp.float32) * (
        2.0 * math.pi / samples
    )
    parity = jnp.where(offsets % 2 == 0, 1.0, -1.0).astype(jnp.float32)
    scale = 2.0 / samples
    even = ((1.0 + parity) / (2.0 * samples))[:, None]
    odd = ((1.0 - parity) / (2.0 * samples))[:, None]
    cos_part = jnp.concatenate([even, scale * jnp.cos(phase[:, 1:])], axis=1)
    sin_part = jnp.concatenate([odd, -scale * jnp.sin(phase[:, 1:])], axis=1)
    table = jnp.concatenate([cos_part, sin_part], axis=1)
    rows = -(-table.shape[0] // 8) * 8
    return jnp.pad(table, ((0, rows - table.shape[0]), (0, 0)))


def split_exact(value):
    hi = lax.reduce_precision(value, exponent_bits=8, mantissa_bits=7)
    rest = value - hi
    mid = lax.reduce_precision(rest, exponent_bits=8, mantissa_bits=7)
    low = rest - mid
    return jnp.stack([hi, mid, low], axis=1).astype(jnp.bfloat16)


def round_kernel(allowed, a_ref, b_ref, u_ref, own_ref, oen_ref, mask_ref, inv_ref, inv_low_ref,
                 *rest):
    pieces = rest[:-2]
    out_ref, x_ref = rest[-2:]
    events, comps, samples, stations = own_ref.shape
    half = samples // 2
    body_rows = comps * samples
    count, lags = out_ref.shape[0], out_ref.shape[1]
    sub_at = u_ref[0]

    def piece_of(q):
        return jnp.bitwise_xor(b_ref[q] // events, sub_at)

    def wanted(q):
        piece = piece_of(q)
        hit = piece == allowed[0]
        for j in allowed[1:]:
            hit = hit | (piece == j)
        return hit

    def step(q, carry):
        piece = piece_of(q)
        event = b_ref[q] % events
        for j, source in zip(allowed, pieces):
            @pl.when(piece == j)
            def _():
                work(q, source, event)

        @pl.when(jnp.logical_not(wanted(q)))
        def _():
            out_ref[q] = jnp.zeros((lags, stations), jnp.float32)

        return carry

    def work(q, source, event):
        ai = a_ref[q]
        u = None
        v = None
        w = None
        for c in range(comps):
            own = own_ref[ai, c]
            far = source[event, c * samples:(c + 1) * samples, :].astype(jnp.float32)
            oa = own[:half]
            ob = own[half:]
            fa = far[:half]
            fb = far[half:]
            uc = oa * fa + ob * fb
            vc = oa * fb - ob * fa
            wc = oa[:8] * fa[:8] - ob[:8] * fb[:8]
            u = uc if u is None else u + uc
            v = vc if v is None else v + vc
            w = wc if w is None else w + wc
        first = lax.broadcasted_iota(jnp.int32, w.shape, 0) == 0
        x_ref[:half, :] = u
        x_ref[half:, :] = v
        x_ref[half:half + 8, :] = jnp.where(first, w, v[:8])
        x = x_ref[...]
        x_high = x.astype(jnp.bfloat16)
        x_low = (x - x_high.astype(jnp.float32)).astype(jnp.bfloat16)
        inv_high = inv_ref[...]
        raw = jnp.dot(inv_high, x_high, preferred_element_type=jnp.float32)
        raw = raw + jnp.dot(inv_high, x_low, preferred_element_type=jnp.float32)
        raw = raw + jnp.dot(inv_low_ref[...], x_high, preferred_element_type=jnp.float32)
        energy = jnp.sum(source[event, body_rows:body_rows + 16, :].astype(jnp.float32), axis=0,
                         keepdims=True)
        denom = jnp.sqrt(oen_ref[ai] * energy + 1e-06)
        out_ref[q] = raw[:lags] / denom * mask_ref[q]

    lax.fori_loop(0, count, step, 0)


def correlate_round(own_spec, own_energy, pieces, allowed, inverse, mask, own_pick, far_pick,
                    sub_at):
    count = own_pick.shape[0]
    events, comps, samples, stations = own_spec.shape
    rows = pieces[0].shape[1]
    lags = 2 * LAG + 1
    smem = pl.BlockSpec(memory_space=pltpu.SMEM)
    vmem = pl.BlockSpec(memory_space=pltpu.VMEM)
    hbm = pl.BlockSpec(memory_space=pl.ANY)
    return pl.pallas_call(
        functools.partial(round_kernel, allowed),
        in_specs=[smem, smem, smem, vmem, vmem, vmem, vmem, vmem] + [vmem] * len(pieces),
        out_specs=vmem,
        out_shape=jax.ShapeDtypeStruct((count, lags, stations), jnp.float32),
        cost_estimate=pl.CostEstimate(
            flops=count * 6 * 2 * 104 * samples * stations,
            transcendentals=count * stations,
            bytes_accessed=count * 8 * (rows + comps * samples) * stations,
        ),
        scratch_shapes=[
            pltpu.VMEM((samples, stations), jnp.float32),
        ],
    )(own_pick, far_pick, sub_at, own_spec, own_energy[:, None, :], mask[:, None, :], *inverse,
      *pieces)


def spectra(forward, waves, start=0, stop=None):
    samples = forward.shape[1]
    stop = samples if stop is None else stop
    table = forward[:, start:stop]
    high = lax.reduce_precision(table, exponent_bits=8, mantissa_bits=7)
    low = (table - high).astype(jnp.bfloat16)
    high = high.astype(jnp.bfloat16)
    waves = waves.astype(jnp.bfloat16)
    first = jnp.einsum("jt,ects->ecjs", high, waves, preferred_element_type=jnp.float32)
    return first + jnp.einsum("jt,ects->ecjs", low, waves, preferred_element_type=jnp.float32)


def by_xor(value, axis, flip):
    length = lax.axis_size(axis)
    return lax.ppermute(value, axis, [(i, i ^ flip) for i in range(length)])


def shards(waves, local_event, partner_event, station_mask):
    events, comps, samples, stations = waves.shape
    forward = forward_table(samples)
    table = inverse_table(samples, LAG)
    table_high = lax.reduce_precision(table, exponent_bits=8, mantissa_bits=7)
    inverse = (table_high.astype(jnp.bfloat16), (table - table_high).astype(jnp.bfloat16))
    region_len = lax.axis_size("region")
    sub_at = lax.axis_index("sub")

    inner = waves[:, :, LAG:samples - LAG, :]
    meta = jnp.concatenate(
        [station_mask[:, 1], local_event[:, 1:2], partner_event[:, 1:2]], axis=1
    )
    inner_wide = inner.astype(jnp.float32)
    inner_energy = jnp.sum(inner_wide * inner_wide, axis=(1, 2))
    sent_inner, sent_meta, sent_energy = lax.ppermute(
        (inner, meta, inner_energy), "region",
        [(i, (i - 1) % region_len) for i in range(region_len)],
    )

    wide = waves.astype(jnp.float32)
    spec = spectra(forward, waves)
    full_energy = jnp.sum(wide * wide, axis=(1, 2))
    body = spec.astype(jnp.bfloat16).reshape(events, comps * samples, stations)
    pieces = split_exact(full_energy)
    tail = jnp.pad(pieces, ((0, 0), (0, 16 - pieces.shape[1]), (0, 0)))
    packed = jnp.concatenate([body, tail], axis=1)

    near = by_xor(packed, "sub", 1)
    across = by_xor(packed, "sub", 2)
    pieces = [packed, near, across, None]
    sub_vec = jnp.full((1,), sub_at, jnp.int32)

    def prepare(own_inner, own_energy):
        return spectra(forward, own_inner, LAG, samples - LAG), own_energy

    def run(prepared, own_pick, far_pick, mask, allowed=(0, 1, 2, 3)):
        own_spec, own_energy = prepared
        own_pick = jnp.clip(own_pick, 0, events - 1)
        far_pick = jnp.clip(far_pick, 0, len(pieces) * events - 1)
        return correlate_round(
            own_spec, own_energy, tuple(pieces[j] for j in allowed), allowed, inverse,
            mask.astype(jnp.float32), own_pick, far_pick, sub_vec,
        )

    own_args = (prepare(inner, inner_energy), local_event[:, 0], partner_event[:, 0])
    sent_meta, sent_energy, own_mask = lax.optimization_barrier(
        (sent_meta, sent_energy, station_mask[:, 0])
    )
    mine = run(*own_args, own_mask, allowed=(0, 1))
    across, mine = lax.optimization_barrier((across, mine))
    pieces[2] = across
    ahead_spec = prepare(sent_inner, sent_energy)
    pieces[3], ahead_spec = lax.optimization_barrier((by_xor(across, "sub", 1), ahead_spec))

    ahead_pick = sent_meta[:, stations]
    ahead_far = sent_meta[:, stations + 1]
    ahead_mask = sent_meta[:, :stations]
    count = ahead_pick.shape[0]
    split = count // 2
    back = []
    for lo, hi in ((0, split), (split, count)):
        back.append(run(ahead_spec, ahead_pick[lo:hi], ahead_far[lo:hi], ahead_mask[lo:hi]))
    back[-1], own_mask = lax.optimization_barrier((back[-1], own_mask))
    back = [
        lax.ppermute(part, "region", [(i, (i + 1) % region_len) for i in range(region_len)])
        for part in back
    ]
    late = run(*own_args, own_mask, allowed=(2, 3))
    return jnp.stack([mine + late, jnp.concatenate(back, axis=0)], axis=1)


def solution(mesh):
    placed = (
        P(("region", "sub"), None, None, None),
        P(("region", "sub"), None),
        P(("region", "sub"), None),
        P(("region", "sub"), None, None),
    )
    return jax.shard_map(
        shards,
        mesh=mesh,
        in_specs=placed,
        out_specs=P(("region", "sub"), None, None, None),
        check_vma=False,
    )
```

```python
import functools
import math

import jax
import jax.numpy as jnp
from jax import lax
from jax.experimental import pallas as pl
from jax.experimental.pallas import tpu as pltpu
from jax.sharding import PartitionSpec as P

LAG = 50


def forward_table(samples):
    half = samples // 2
    sample_index = jnp.arange(samples, dtype=jnp.int32)
    orders = jnp.arange(half, dtype=jnp.int32)
    turn = 2.0 * math.pi / samples
    phase = (orders[:, None] * sample_index[None, :] % samples).astype(jnp.float32) * turn
    top = (half * sample_index % samples).astype(jnp.float32) * turn
    lower = jnp.concatenate([jnp.cos(top)[None, :], -jnp.sin(phase[1:])], axis=0)
    return jnp.concatenate([jnp.cos(phase), lower], axis=0)


def inverse_table(samples, reach):
    half = samples // 2
    orders = jnp.arange(half, dtype=jnp.int32)
    offsets = (jnp.arange(2 * reach + 1, dtype=jnp.int32) - reach + samples) % samples
    phase = (offsets[:, None] * orders[None, :] % samples).astype(jnp.float32) * (
        2.0 * math.pi / samples
    )
    parity = jnp.where(offsets % 2 == 0, 1.0, -1.0).astype(jnp.float32)
    scale = 2.0 / samples
    even = ((1.0 + parity) / (2.0 * samples))[:, None]
    odd = ((1.0 - parity) / (2.0 * samples))[:, None]
    cos_part = jnp.concatenate([even, scale * jnp.cos(phase[:, 1:])], axis=1)
    sin_part = jnp.concatenate([odd, -scale * jnp.sin(phase[:, 1:])], axis=1)
    table = jnp.concatenate([cos_part, sin_part], axis=1)
    rows = -(-table.shape[0] // 8) * 8
    return jnp.pad(table, ((0, rows - table.shape[0]), (0, 0)))


def split_exact(value):
    hi = lax.reduce_precision(value, exponent_bits=8, mantissa_bits=7)
    rest = value - hi
    mid = lax.reduce_precision(rest, exponent_bits=8, mantissa_bits=7)
    low = rest - mid
    return jnp.stack([hi, mid, low], axis=1).astype(jnp.bfloat16)


def round_kernel(allowed, a_ref, b_ref, u_ref, own_ref, oen_ref, mask_ref, inv_ref, inv_low_ref,
                 *rest):
    pieces = rest[:-2]
    out_ref, x_ref = rest[-2:]
    events, comps, samples, stations = own_ref.shape
    half = samples // 2
    body_rows = comps * samples
    count, lags = out_ref.shape[0], out_ref.shape[1]
    sub_at = u_ref[0]

    def piece_of(q):
        return jnp.bitwise_xor(b_ref[q] // events, sub_at)

    def wanted(q):
        piece = piece_of(q)
        hit = piece == allowed[0]
        for j in allowed[1:]:
            hit = hit | (piece == j)
        return hit

    def step(q, carry):
        piece = piece_of(q)
        event = b_ref[q] % events
        for j, source in zip(allowed, pieces):
            @pl.when(piece == j)
            def _():
                work(q, source, event)

        @pl.when(jnp.logical_not(wanted(q)))
        def _():
            out_ref[q] = jnp.zeros((lags, stations), jnp.float32)

        return carry

    def work(q, source, event):
        ai = a_ref[q]
        u = None
        v = None
        w = None
        for c in range(comps):
            own = own_ref[ai, c]
            far = source[event, c * samples:(c + 1) * samples, :].astype(jnp.float32)
            oa = own[:half]
            ob = own[half:]
            fa = far[:half]
            fb = far[half:]
            uc = oa * fa + ob * fb
            vc = oa * fb - ob * fa
            wc = oa[:8] * fa[:8] - ob[:8] * fb[:8]
            u = uc if u is None else u + uc
            v = vc if v is None else v + vc
            w = wc if w is None else w + wc
        first = lax.broadcasted_iota(jnp.int32, w.shape, 0) == 0
        x_ref[:half, :] = u
        x_ref[half:, :] = v
        x_ref[half:half + 8, :] = jnp.where(first, w, v[:8])
        x = x_ref[...]
        x_high = x.astype(jnp.bfloat16)
        x_low = (x - x_high.astype(jnp.float32)).astype(jnp.bfloat16)
        inv_high = inv_ref[...]
        raw = jnp.dot(inv_high, x_high, preferred_element_type=jnp.float32)
        raw = raw + jnp.dot(inv_high, x_low, preferred_element_type=jnp.float32)
        raw = raw + jnp.dot(inv_low_ref[...], x_high, preferred_element_type=jnp.float32)
        energy = jnp.sum(source[event, body_rows:body_rows + 16, :].astype(jnp.float32), axis=0,
                         keepdims=True)
        denom = jnp.sqrt(oen_ref[ai] * energy + 1e-06)
        out_ref[q] = raw[:lags] / denom * mask_ref[q]

    lax.fori_loop(0, count, step, 0)


def correlate_round(own_spec, own_energy, pieces, allowed, inverse, mask, own_pick, far_pick,
                    sub_at):
    count = own_pick.shape[0]
    events, comps, samples, stations = own_spec.shape
    rows = pieces[0].shape[1]
    lags = 2 * LAG + 1
    smem = pl.BlockSpec(memory_space=pltpu.SMEM)
    vmem = pl.BlockSpec(memory_space=pltpu.VMEM)
    hbm = pl.BlockSpec(memory_space=pl.ANY)
    return pl.pallas_call(
        functools.partial(round_kernel, allowed),
        in_specs=[smem, smem, smem, vmem, vmem, vmem, vmem, vmem] + [vmem] * len(pieces),
        out_specs=vmem,
        out_shape=jax.ShapeDtypeStruct((count, lags, stations), jnp.float32),
        cost_estimate=pl.CostEstimate(
            flops=count * 6 * 2 * 104 * samples * stations,
            transcendentals=count * stations,
            bytes_accessed=count * 8 * (rows + comps * samples) * stations,
        ),
        scratch_shapes=[
            pltpu.VMEM((samples, stations), jnp.float32),
        ],
    )(own_pick, far_pick, sub_at, own_spec, own_energy[:, None, :], mask[:, None, :], *inverse,
      *pieces)


def spectra(forward, wide):
    samples = forward.shape[1]
    return jnp.einsum(
        "jt,ects->ecjs", forward[:, LAG:samples - LAG], wide, precision=lax.Precision.HIGH
    )


def by_xor(value, axis, flip):
    length = lax.axis_size(axis)
    return lax.ppermute(value, axis, [(i, i ^ flip) for i in range(length)])


def shards(waves, local_event, partner_event, station_mask):
    events, comps, samples, stations = waves.shape
    forward = forward_table(samples)
    table = inverse_table(samples, LAG)
    table_high = lax.reduce_precision(table, exponent_bits=8, mantissa_bits=7)
    inverse = (table_high.astype(jnp.bfloat16), (table - table_high).astype(jnp.bfloat16))
    region_len = lax.axis_size("region")
    sub_at = lax.axis_index("sub")

    inner = waves[:, :, LAG:samples - LAG, :]
    meta = jnp.concatenate(
        [station_mask[:, 1], local_event[:, 1:2], partner_event[:, 1:2]], axis=1
    )
    inner_wide = inner.astype(jnp.float32)
    inner_energy = jnp.sum(inner_wide * inner_wide, axis=(1, 2))
    sent_waves, sent_meta, sent_energy = lax.ppermute(
        (waves, meta, inner_energy), "region",
        [(i, (i - 1) % region_len) for i in range(region_len)],
    )

    wide = waves.astype(jnp.float32)
    spec = jnp.einsum("jt,ects->ecjs", forward, wide, precision=lax.Precision.HIGH)
    full_energy = jnp.sum(wide * wide, axis=(1, 2))
    body = spec.astype(jnp.bfloat16).reshape(events, comps * samples, stations)
    pieces = split_exact(full_energy)
    tail = jnp.pad(pieces, ((0, 0), (0, 16 - pieces.shape[1]), (0, 0)))
    packed = jnp.concatenate([body, tail], axis=1)

    near = by_xor(packed, "sub", 1)
    across = by_xor(packed, "sub", 2)
    pieces = [packed, near, across, None]
    sub_vec = jnp.full((1,), sub_at, jnp.int32)

    def prepare(own_inner, own_energy):
        return spectra(forward, own_inner.astype(jnp.float32)), own_energy

    def run(prepared, own_pick, far_pick, mask, allowed=(0, 1, 2, 3)):
        own_spec, own_energy = prepared
        own_pick = jnp.clip(own_pick, 0, events - 1)
        far_pick = jnp.clip(far_pick, 0, len(pieces) * events - 1)
        return correlate_round(
            own_spec, own_energy, tuple(pieces[j] for j in allowed), allowed, inverse,
            mask.astype(jnp.float32), own_pick, far_pick, sub_vec,
        )

    own_args = (prepare(inner, inner_energy), local_event[:, 0], partner_event[:, 0])
    sent_meta, sent_energy, own_mask = lax.optimization_barrier(
        (sent_meta, sent_energy, station_mask[:, 0])
    )
    mine = run(*own_args, own_mask, allowed=(0, 1))
    sent_waves, mine = lax.optimization_barrier((sent_waves, mine))
    ahead_spec = prepare(sent_waves[:, :, LAG:samples - LAG, :], sent_energy)
    across, mine, ahead_spec = lax.optimization_barrier((across, mine, ahead_spec))
    pieces[2] = across
    pieces[3] = by_xor(across, "sub", 1)

    ahead_pick = sent_meta[:, stations]
    ahead_far = sent_meta[:, stations + 1]
    ahead_mask = sent_meta[:, :stations]
    count = ahead_pick.shape[0]
    split = count // 2
    back = []
    for lo, hi in ((0, split), (split, count)):
        back.append(run(ahead_spec, ahead_pick[lo:hi], ahead_far[lo:hi], ahead_mask[lo:hi]))
    back[-1], own_mask = lax.optimization_barrier((back[-1], own_mask))
    back = [
        lax.ppermute(part, "region", [(i, (i + 1) % region_len) for i in range(region_len)])
        for part in back
    ]
    late = run(*own_args, own_mask, allowed=(2, 3))
    return jnp.stack([mine + late, jnp.concatenate(back, axis=0)], axis=1)


def solution(mesh):
    placed = (
        P(("region", "sub"), None, None, None),
        P(("region", "sub"), None),
        P(("region", "sub"), None),
        P(("region", "sub"), None, None),
    )
    return jax.shard_map(
        shards,
        mesh=mesh,
        in_specs=placed,
        out_specs=P(("region", "sub"), None, None, None),
        check_vma=False,
    )
```

```python
import functools
import math

import jax
import jax.numpy as jnp
from jax import lax
from jax.experimental import pallas as pl
from jax.experimental.pallas import tpu as pltpu
from jax.sharding import PartitionSpec as P

LAG = 50


def forward_table(samples):
    half = samples // 2
    sample_index = jnp.arange(samples, dtype=jnp.int32)
    orders = jnp.arange(half, dtype=jnp.int32)
    turn = 2.0 * math.pi / samples
    phase = (orders[:, None] * sample_index[None, :] % samples).astype(jnp.float32) * turn
    top = (half * sample_index % samples).astype(jnp.float32) * turn
    lower = jnp.concatenate([jnp.cos(top)[None, :], -jnp.sin(phase[1:])], axis=0)
    return jnp.concatenate([jnp.cos(phase), lower], axis=0)


def inverse_table(samples, reach):
    half = samples // 2
    orders = jnp.arange(half, dtype=jnp.int32)
    offsets = (jnp.arange(2 * reach + 1, dtype=jnp.int32) - reach + samples) % samples
    phase = (offsets[:, None] * orders[None, :] % samples).astype(jnp.float32) * (
        2.0 * math.pi / samples
    )
    parity = jnp.where(offsets % 2 == 0, 1.0, -1.0).astype(jnp.float32)
    scale = 2.0 / samples
    even = ((1.0 + parity) / (2.0 * samples))[:, None]
    odd = ((1.0 - parity) / (2.0 * samples))[:, None]
    cos_part = jnp.concatenate([even, scale * jnp.cos(phase[:, 1:])], axis=1)
    sin_part = jnp.concatenate([odd, -scale * jnp.sin(phase[:, 1:])], axis=1)
    table = jnp.concatenate([cos_part, sin_part], axis=1)
    rows = -(-table.shape[0] // 8) * 8
    return jnp.pad(table, ((0, rows - table.shape[0]), (0, 0)))


def split_exact(value):
    hi = lax.reduce_precision(value, exponent_bits=8, mantissa_bits=7)
    rest = value - hi
    mid = lax.reduce_precision(rest, exponent_bits=8, mantissa_bits=7)
    low = rest - mid
    return jnp.stack([hi, mid, low], axis=1).astype(jnp.bfloat16)


def round_kernel(allowed, keep, a_ref, b_ref, u_ref, own_ref, oen_ref, mask_ref, inv_ref,
                 inv_low_ref, *rest):
    pieces = rest[:len(allowed)]
    out_ref, x_ref = rest[-2:]
    events, comps, samples, stations = own_ref.shape
    half = samples // 2
    body_rows = comps * samples
    count, lags = out_ref.shape[0], out_ref.shape[1]
    sub_at = u_ref[0]

    def piece_of(q):
        return jnp.bitwise_xor(b_ref[q] // events, sub_at)

    def wanted(q):
        piece = piece_of(q)
        hit = piece == allowed[0]
        for j in allowed[1:]:
            hit = hit | (piece == j)
        return hit

    def step(q, carry):
        piece = piece_of(q)
        event = b_ref[q] % events
        for j, source in zip(allowed, pieces):
            @pl.when(piece == j)
            def _():
                work(q, source, event)

        @pl.when(jnp.logical_not(wanted(q)))
        def _():
            if keep:
                out_ref[q] = rest[len(allowed)][q]
            else:
                out_ref[q] = jnp.zeros((lags, stations), jnp.float32)

        return carry

    def work(q, source, event):
        ai = a_ref[q]
        u = None
        v = None
        w = None
        for c in range(comps):
            own = own_ref[ai, c]
            far = source[event, c * samples:(c + 1) * samples, :].astype(jnp.float32)
            oa = own[:half]
            ob = own[half:]
            fa = far[:half]
            fb = far[half:]
            uc = oa * fa + ob * fb
            vc = oa * fb - ob * fa
            wc = oa[:8] * fa[:8] - ob[:8] * fb[:8]
            u = uc if u is None else u + uc
            v = vc if v is None else v + vc
            w = wc if w is None else w + wc
        first = lax.broadcasted_iota(jnp.int32, w.shape, 0) == 0
        x_ref[:half, :] = u
        x_ref[half:, :] = v
        x_ref[half:half + 8, :] = jnp.where(first, w, v[:8])
        x = x_ref[...]
        x_high = x.astype(jnp.bfloat16)
        x_low = (x - x_high.astype(jnp.float32)).astype(jnp.bfloat16)
        inv_high = inv_ref[...]
        raw = jnp.dot(inv_high, x_high, preferred_element_type=jnp.float32)
        raw = raw + jnp.dot(inv_high, x_low, preferred_element_type=jnp.float32)
        raw = raw + jnp.dot(inv_low_ref[...], x_high, preferred_element_type=jnp.float32)
        energy = jnp.sum(source[event, body_rows:body_rows + 16, :].astype(jnp.float32), axis=0,
                         keepdims=True)
        denom = jnp.sqrt(oen_ref[ai] * energy + 1e-06)
        out_ref[q] = raw[:lags] / denom * mask_ref[q]

    lax.fori_loop(0, count, step, 0)


def correlate_round(own_spec, own_energy, pieces, allowed, inverse, mask, own_pick, far_pick,
                    sub_at, prior=None):
    count = own_pick.shape[0]
    events, comps, samples, stations = own_spec.shape
    rows = pieces[0].shape[1]
    lags = 2 * LAG + 1
    smem = pl.BlockSpec(memory_space=pltpu.SMEM)
    vmem = pl.BlockSpec(memory_space=pltpu.VMEM)
    hbm = pl.BlockSpec(memory_space=pl.ANY)
    return pl.pallas_call(
        functools.partial(round_kernel, allowed, prior is not None),
        in_specs=[smem, smem, smem, vmem, vmem, vmem, vmem, vmem] + [vmem] * len(pieces)
        + ([vmem] if prior is not None else []),
        out_specs=vmem,
        out_shape=jax.ShapeDtypeStruct((count, lags, stations), jnp.float32),
        cost_estimate=pl.CostEstimate(
            flops=count * 6 * 2 * 104 * samples * stations,
            transcendentals=count * stations,
            bytes_accessed=count * 8 * (rows + comps * samples) * stations,
        ),
        scratch_shapes=[
            pltpu.VMEM((samples, stations), jnp.float32),
        ],
    )(own_pick, far_pick, sub_at, own_spec, own_energy[:, None, :], mask[:, None, :], *inverse,
      *pieces, *([prior] if prior is not None else []))


def spectra(forward, wide):
    samples = forward.shape[1]
    return jnp.einsum(
        "jt,ects->ecjs", forward[:, LAG:samples - LAG], wide, precision=lax.Precision.HIGH
    )


def by_xor(value, axis, flip):
    length = lax.axis_size(axis)
    return lax.ppermute(value, axis, [(i, i ^ flip) for i in range(length)])


def shards(waves, local_event, partner_event, station_mask):
    events, comps, samples, stations = waves.shape
    forward = forward_table(samples)
    table = inverse_table(samples, LAG)
    table_high = lax.reduce_precision(table, exponent_bits=8, mantissa_bits=7)
    inverse = (table_high.astype(jnp.bfloat16), (table - table_high).astype(jnp.bfloat16))
    region_len = lax.axis_size("region")
    sub_at = lax.axis_index("sub")

    inner = waves[:, :, LAG:samples - LAG, :]
    meta = jnp.concatenate(
        [station_mask[:, 1], local_event[:, 1:2], partner_event[:, 1:2]], axis=1
    )
    inner_wide = inner.astype(jnp.float32)
    inner_energy = jnp.sum(inner_wide * inner_wide, axis=(1, 2))
    sent_inner, sent_meta, sent_energy = lax.ppermute(
        (inner, meta, inner_energy), "region",
        [(i, (i - 1) % region_len) for i in range(region_len)],
    )

    wide = waves.astype(jnp.float32)
    spec = jnp.einsum("jt,ects->ecjs", forward, wide, precision=lax.Precision.HIGH)
    full_energy = jnp.sum(wide * wide, axis=(1, 2))
    body = spec.astype(jnp.bfloat16).reshape(events, comps * samples, stations)
    pieces = split_exact(full_energy)
    tail = jnp.pad(pieces, ((0, 0), (0, 16 - pieces.shape[1]), (0, 0)))
    packed = jnp.concatenate([body, tail], axis=1)

    near = by_xor(packed, "sub", 1)
    across = by_xor(packed, "sub", 2)
    pieces = [packed, near, across, None]
    sub_vec = jnp.full((1,), sub_at, jnp.int32)

    def prepare(own_inner, own_energy):
        return spectra(forward, own_inner.astype(jnp.float32)), own_energy

    def run(prepared, own_pick, far_pick, mask, allowed=(0, 1, 2, 3), prior=None):
        own_spec, own_energy = prepared
        own_pick = jnp.clip(own_pick, 0, events - 1)
        far_pick = jnp.clip(far_pick, 0, len(pieces) * events - 1)
        return correlate_round(
            own_spec, own_energy, tuple(pieces[j] for j in allowed), allowed, inverse,
            mask.astype(jnp.float32), own_pick, far_pick, sub_vec, prior,
        )

    own_args = (prepare(inner, inner_energy), local_event[:, 0], partner_event[:, 0])
    sent_meta, sent_energy, own_mask = lax.optimization_barrier(
        (sent_meta, sent_energy, station_mask[:, 0])
    )
    mine = run(*own_args, own_mask, allowed=(0, 1))
    across, mine = lax.optimization_barrier((across, mine))
    pieces[2] = across
    ahead_spec = prepare(sent_inner, sent_energy)
    pieces[3], ahead_spec = lax.optimization_barrier((by_xor(across, "sub", 1), ahead_spec))

    ahead_pick = sent_meta[:, stations]
    ahead_far = sent_meta[:, stations + 1]
    ahead_mask = sent_meta[:, :stations]
    count = ahead_pick.shape[0]
    split = count // 2
    back = []
    for lo, hi in ((0, split), (split, count)):
        back.append(run(ahead_spec, ahead_pick[lo:hi], ahead_far[lo:hi], ahead_mask[lo:hi]))
    back[-1], own_mask = lax.optimization_barrier((back[-1], own_mask))
    back = [
        lax.ppermute(part, "region", [(i, (i + 1) % region_len) for i in range(region_len)])
        for part in back
    ]
    mine = run(*own_args, own_mask, allowed=(2, 3), prior=mine)
    return jnp.stack([mine, jnp.concatenate(back, axis=0)], axis=1)


def solution(mesh):
    placed = (
        P(("region", "sub"), None, None, None),
        P(("region", "sub"), None),
        P(("region", "sub"), None),
        P(("region", "sub"), None, None),
    )
    return jax.shard_map(
        shards,
        mesh=mesh,
        in_specs=placed,
        out_specs=P(("region", "sub"), None, None, None),
        check_vma=False,
    )
```

```python
import functools
import math

import jax
import jax.numpy as jnp
from jax import lax
from jax.experimental import pallas as pl
from jax.experimental.pallas import tpu as pltpu
from jax.sharding import PartitionSpec as P

LAG = 50


def forward_table(samples):
    half = samples // 2
    sample_index = jnp.arange(samples, dtype=jnp.int32)
    orders = jnp.arange(half, dtype=jnp.int32)
    turn = 2.0 * math.pi / samples
    phase = (orders[:, None] * sample_index[None, :] % samples).astype(jnp.float32) * turn
    top = (half * sample_index % samples).astype(jnp.float32) * turn
    lower = jnp.concatenate([jnp.cos(top)[None, :], -jnp.sin(phase[1:])], axis=0)
    return jnp.concatenate([jnp.cos(phase), lower], axis=0)


def inverse_table(samples, reach):
    half = samples // 2
    orders = jnp.arange(half, dtype=jnp.int32)
    offsets = (jnp.arange(2 * reach + 1, dtype=jnp.int32) - reach + samples) % samples
    phase = (offsets[:, None] * orders[None, :] % samples).astype(jnp.float32) * (
        2.0 * math.pi / samples
    )
    parity = jnp.where(offsets % 2 == 0, 1.0, -1.0).astype(jnp.float32)
    scale = 2.0 / samples
    even = ((1.0 + parity) / (2.0 * samples))[:, None]
    odd = ((1.0 - parity) / (2.0 * samples))[:, None]
    cos_part = jnp.concatenate([even, scale * jnp.cos(phase[:, 1:])], axis=1)
    sin_part = jnp.concatenate([odd, -scale * jnp.sin(phase[:, 1:])], axis=1)
    table = jnp.concatenate([cos_part, sin_part], axis=1)
    rows = -(-table.shape[0] // 8) * 8
    return jnp.pad(table, ((0, rows - table.shape[0]), (0, 0)))


def split_exact(value):
    hi = lax.reduce_precision(value, exponent_bits=8, mantissa_bits=7)
    rest = value - hi
    mid = lax.reduce_precision(rest, exponent_bits=8, mantissa_bits=7)
    low = rest - mid
    return jnp.stack([hi, mid, low], axis=1).astype(jnp.bfloat16)


def round_kernel(allowed, keep, a_ref, b_ref, u_ref, own_ref, oen_ref, mask_ref, inv_ref,
                 inv_low_ref, *rest):
    pieces = rest[:len(allowed)]
    out_ref, x_ref = rest[-2:]
    events, comps, samples, stations = own_ref.shape
    half = samples // 2
    body_rows = comps * samples
    count, lags = out_ref.shape[0], out_ref.shape[1]
    sub_at = u_ref[0]

    def piece_of(q):
        return jnp.bitwise_xor(b_ref[q] // events, sub_at)

    def wanted(q):
        piece = piece_of(q)
        hit = piece == allowed[0]
        for j in allowed[1:]:
            hit = hit | (piece == j)
        return hit

    def step(q, carry):
        piece = piece_of(q)
        event = b_ref[q] % events
        for j, source in zip(allowed, pieces):
            @pl.when(piece == j)
            def _():
                work(q, source, event)

        @pl.when(jnp.logical_not(wanted(q)))
        def _():
            if keep:
                out_ref[q] = rest[len(allowed)][q]
            else:
                out_ref[q] = jnp.zeros((lags, stations), out_ref.dtype)

        return carry

    def work(q, source, event):
        ai = a_ref[q]
        u = None
        v = None
        w = None
        for c in range(comps):
            own = own_ref[ai, c]
            far = source[event, c * samples:(c + 1) * samples, :].astype(jnp.float32)
            oa = own[:half]
            ob = own[half:]
            fa = far[:half]
            fb = far[half:]
            uc = oa * fa + ob * fb
            vc = oa * fb - ob * fa
            wc = oa[:8] * fa[:8] - ob[:8] * fb[:8]
            u = uc if u is None else u + uc
            v = vc if v is None else v + vc
            w = wc if w is None else w + wc
        first = lax.broadcasted_iota(jnp.int32, w.shape, 0) == 0
        x_ref[:half, :] = u
        x_ref[half:, :] = v
        x_ref[half:half + 8, :] = jnp.where(first, w, v[:8])
        x = x_ref[...]
        x_high = x.astype(jnp.bfloat16)
        x_low = (x - x_high.astype(jnp.float32)).astype(jnp.bfloat16)
        inv_high = inv_ref[...]
        raw = jnp.dot(inv_high, x_high, preferred_element_type=jnp.float32)
        raw = raw + jnp.dot(inv_high, x_low, preferred_element_type=jnp.float32)
        raw = raw + jnp.dot(inv_low_ref[...], x_high, preferred_element_type=jnp.float32)
        energy = jnp.sum(source[event, body_rows:body_rows + 16, :].astype(jnp.float32), axis=0,
                         keepdims=True)
        denom = jnp.sqrt(oen_ref[ai] * energy + 1e-06)
        out_ref[q] = (raw[:lags] / denom * mask_ref[q]).astype(out_ref.dtype)

    lax.fori_loop(0, count, step, 0)


def correlate_round(own_spec, own_energy, pieces, allowed, inverse, mask, own_pick, far_pick,
                    sub_at, prior=None, out_dtype=jnp.float32):
    count = own_pick.shape[0]
    events, comps, samples, stations = own_spec.shape
    rows = pieces[0].shape[1]
    lags = 2 * LAG + 1
    smem = pl.BlockSpec(memory_space=pltpu.SMEM)
    vmem = pl.BlockSpec(memory_space=pltpu.VMEM)
    hbm = pl.BlockSpec(memory_space=pl.ANY)
    return pl.pallas_call(
        functools.partial(round_kernel, allowed, prior is not None),
        in_specs=[smem, smem, smem, vmem, vmem, vmem, vmem, vmem] + [vmem] * len(pieces)
        + ([vmem] if prior is not None else []),
        out_specs=vmem,
        out_shape=jax.ShapeDtypeStruct((count, lags, stations), out_dtype),
        cost_estimate=pl.CostEstimate(
            flops=count * 6 * 2 * 104 * samples * stations,
            transcendentals=count * stations,
            bytes_accessed=count * 8 * (rows + comps * samples) * stations,
        ),
        scratch_shapes=[
            pltpu.VMEM((samples, stations), jnp.float32),
        ],
    )(own_pick, far_pick, sub_at, own_spec, own_energy[:, None, :], mask[:, None, :], *inverse,
      *pieces, *([prior] if prior is not None else []))


def spectra(forward, wide):
    samples = forward.shape[1]
    return jnp.einsum(
        "jt,ects->ecjs", forward[:, LAG:samples - LAG], wide, precision=lax.Precision.HIGH
    )


def by_xor(value, axis, flip):
    length = lax.axis_size(axis)
    return lax.ppermute(value, axis, [(i, i ^ flip) for i in range(length)])


def shards(waves, local_event, partner_event, station_mask):
    events, comps, samples, stations = waves.shape
    forward = forward_table(samples)
    table = inverse_table(samples, LAG)
    table_high = lax.reduce_precision(table, exponent_bits=8, mantissa_bits=7)
    inverse = (table_high.astype(jnp.bfloat16), (table - table_high).astype(jnp.bfloat16))
    region_len = lax.axis_size("region")
    sub_at = lax.axis_index("sub")

    inner = waves[:, :, LAG:samples - LAG, :]
    meta = jnp.concatenate(
        [station_mask[:, 1], local_event[:, 1:2], partner_event[:, 1:2]], axis=1
    )
    inner_wide = inner.astype(jnp.float32)
    inner_energy = jnp.sum(inner_wide * inner_wide, axis=(1, 2))
    sent_inner, sent_meta, sent_energy = lax.ppermute(
        (inner, meta, inner_energy), "region",
        [(i, (i - 1) % region_len) for i in range(region_len)],
    )

    wide = waves.astype(jnp.float32)
    spec = jnp.einsum("jt,ects->ecjs", forward, wide, precision=lax.Precision.HIGH)
    full_energy = jnp.sum(wide * wide, axis=(1, 2))
    body = spec.astype(jnp.bfloat16).reshape(events, comps * samples, stations)
    pieces = split_exact(full_energy)
    tail = jnp.pad(pieces, ((0, 0), (0, 16 - pieces.shape[1]), (0, 0)))
    packed = jnp.concatenate([body, tail], axis=1)

    near = by_xor(packed, "sub", 1)
    across = by_xor(packed, "sub", 2)
    pieces = [packed, near, across, None]
    sub_vec = jnp.full((1,), sub_at, jnp.int32)

    def prepare(own_inner, own_energy):
        return spectra(forward, own_inner.astype(jnp.float32)), own_energy

    def run(prepared, own_pick, far_pick, mask, allowed=(0, 1, 2, 3), prior=None,
            out_dtype=jnp.float32):
        own_spec, own_energy = prepared
        own_pick = jnp.clip(own_pick, 0, events - 1)
        far_pick = jnp.clip(far_pick, 0, len(pieces) * events - 1)
        return correlate_round(
            own_spec, own_energy, tuple(pieces[j] for j in allowed), allowed, inverse,
            mask.astype(jnp.float32), own_pick, far_pick, sub_vec, prior, out_dtype,
        )

    own_args = (prepare(inner, inner_energy), local_event[:, 0], partner_event[:, 0])
    sent_meta, sent_energy, own_mask = lax.optimization_barrier(
        (sent_meta, sent_energy, station_mask[:, 0])
    )
    mine = run(*own_args, own_mask, allowed=(0, 1))
    across, mine = lax.optimization_barrier((across, mine))
    pieces[2] = across
    ahead_spec = prepare(sent_inner, sent_energy)
    pieces[3], ahead_spec = lax.optimization_barrier((by_xor(across, "sub", 1), ahead_spec))

    ahead_pick = sent_meta[:, stations]
    ahead_far = sent_meta[:, stations + 1]
    ahead_mask = sent_meta[:, :stations]
    count = ahead_pick.shape[0]
    split = count // 2
    back = []
    for lo, hi in ((0, split), (split, count)):
        back.append(run(ahead_spec, ahead_pick[lo:hi], ahead_far[lo:hi], ahead_mask[lo:hi],
                        out_dtype=jnp.bfloat16))
    back[-1], own_mask = lax.optimization_barrier((back[-1], own_mask))
    back = [
        lax.ppermute(part, "region", [(i, (i + 1) % region_len) for i in range(region_len)])
        for part in back
    ]
    mine = run(*own_args, own_mask, allowed=(2, 3), prior=mine)
    return jnp.stack([mine, jnp.concatenate(back, axis=0).astype(jnp.float32)], axis=1)


def solution(mesh):
    placed = (
        P(("region", "sub"), None, None, None),
        P(("region", "sub"), None),
        P(("region", "sub"), None),
        P(("region", "sub"), None, None),
    )
    return jax.shard_map(
        shards,
        mesh=mesh,
        in_specs=placed,
        out_specs=P(("region", "sub"), None, None, None),
        check_vma=False,
    )
```

```python
import functools
import math

import jax
import jax.numpy as jnp
from jax import lax
from jax.experimental import pallas as pl
from jax.experimental.pallas import tpu as pltpu
from jax.sharding import PartitionSpec as P

LAG = 50


def forward_table(samples):
    half = samples // 2
    sample_index = jnp.arange(samples, dtype=jnp.int32)
    orders = jnp.arange(half, dtype=jnp.int32)
    turn = 2.0 * math.pi / samples
    phase = (orders[:, None] * sample_index[None, :] % samples).astype(jnp.float32) * turn
    top = (half * sample_index % samples).astype(jnp.float32) * turn
    lower = jnp.concatenate([jnp.cos(top)[None, :], -jnp.sin(phase[1:])], axis=0)
    return jnp.concatenate([jnp.cos(phase), lower], axis=0)


def inverse_table(samples, reach):
    half = samples // 2
    orders = jnp.arange(half, dtype=jnp.int32)
    offsets = (jnp.arange(2 * reach + 1, dtype=jnp.int32) - reach + samples) % samples
    phase = (offsets[:, None] * orders[None, :] % samples).astype(jnp.float32) * (
        2.0 * math.pi / samples
    )
    parity = jnp.where(offsets % 2 == 0, 1.0, -1.0).astype(jnp.float32)
    scale = 2.0 / samples
    even = ((1.0 + parity) / (2.0 * samples))[:, None]
    odd = ((1.0 - parity) / (2.0 * samples))[:, None]
    cos_part = jnp.concatenate([even, scale * jnp.cos(phase[:, 1:])], axis=1)
    sin_part = jnp.concatenate([odd, -scale * jnp.sin(phase[:, 1:])], axis=1)
    table = jnp.concatenate([cos_part, sin_part], axis=1)
    rows = -(-table.shape[0] // 8) * 8
    return jnp.pad(table, ((0, rows - table.shape[0]), (0, 0)))


def split_exact(value):
    hi = lax.reduce_precision(value, exponent_bits=8, mantissa_bits=7)
    rest = value - hi
    mid = lax.reduce_precision(rest, exponent_bits=8, mantissa_bits=7)
    low = rest - mid
    return jnp.stack([hi, mid, low], axis=1).astype(jnp.bfloat16)


def round_kernel(allowed, keep, a_ref, b_ref, u_ref, own_ref, oen_ref, mask_ref, inv_ref,
                 inv_low_ref, *rest):
    pieces = rest[:len(allowed)]
    out_ref, x_ref = rest[-2:]
    events, comps, samples, stations = own_ref.shape
    half = samples // 2
    body_rows = comps * samples
    count, lags = out_ref.shape[0], out_ref.shape[1]
    sub_at = u_ref[0]

    def piece_of(q):
        return jnp.bitwise_xor(b_ref[q] // events, sub_at)

    def wanted(q):
        piece = piece_of(q)
        hit = piece == allowed[0]
        for j in allowed[1:]:
            hit = hit | (piece == j)
        return hit

    def step(q, carry):
        piece = piece_of(q)
        event = b_ref[q] % events
        for j, source in zip(allowed, pieces):
            @pl.when(piece == j)
            def _():
                work(q, source, event)

        @pl.when(jnp.logical_not(wanted(q)))
        def _():
            if keep:
                out_ref[q] = rest[len(allowed)][q]
            else:
                out_ref[q] = jnp.zeros((lags, stations), out_ref.dtype)

        return carry

    def work(q, source, event):
        ai = a_ref[q]
        u = None
        v = None
        w = None
        for c in range(comps):
            own = own_ref[ai, c]
            far = source[event, c * samples:(c + 1) * samples, :].astype(jnp.float32)
            oa = own[:half]
            ob = own[half:]
            fa = far[:half]
            fb = far[half:]
            uc = oa * fa + ob * fb
            vc = oa * fb - ob * fa
            wc = oa[:8] * fa[:8] - ob[:8] * fb[:8]
            u = uc if u is None else u + uc
            v = vc if v is None else v + vc
            w = wc if w is None else w + wc
        first = lax.broadcasted_iota(jnp.int32, w.shape, 0) == 0
        x_ref[:half, :] = u
        x_ref[half:, :] = v
        x_ref[half:half + 8, :] = jnp.where(first, w, v[:8])
        x = x_ref[...]
        x_high = x.astype(jnp.bfloat16)
        x_low = (x - x_high.astype(jnp.float32)).astype(jnp.bfloat16)
        inv_high = inv_ref[...]
        raw = jnp.dot(inv_high, x_high, preferred_element_type=jnp.float32)
        raw = raw + jnp.dot(inv_high, x_low, preferred_element_type=jnp.float32)
        raw = raw + jnp.dot(inv_low_ref[...], x_high, preferred_element_type=jnp.float32)
        energy = jnp.sum(source[event, body_rows:body_rows + 16, :].astype(jnp.float32), axis=0,
                         keepdims=True)
        denom = jnp.sqrt(oen_ref[ai] * energy + 1e-06)
        out_ref[q] = (raw[:lags] / denom * mask_ref[q]).astype(out_ref.dtype)

    lax.fori_loop(0, count, step, 0)


def correlate_round(own_spec, own_energy, pieces, allowed, inverse, mask, own_pick, far_pick,
                    sub_at, prior=None, out_dtype=jnp.float32):
    count = own_pick.shape[0]
    events, comps, samples, stations = own_spec.shape
    rows = pieces[0].shape[1]
    lags = 2 * LAG + 1
    smem = pl.BlockSpec(memory_space=pltpu.SMEM)
    vmem = pl.BlockSpec(memory_space=pltpu.VMEM)
    hbm = pl.BlockSpec(memory_space=pl.ANY)
    return pl.pallas_call(
        functools.partial(round_kernel, allowed, prior is not None),
        in_specs=[smem, smem, smem, vmem, vmem, vmem, vmem, vmem] + [vmem] * len(pieces)
        + ([vmem] if prior is not None else []),
        out_specs=vmem,
        out_shape=jax.ShapeDtypeStruct((count, lags, stations), out_dtype),
        cost_estimate=pl.CostEstimate(
            flops=count * 6 * 2 * 104 * samples * stations,
            transcendentals=count * stations,
            bytes_accessed=count * 8 * (rows + comps * samples) * stations,
        ),
        scratch_shapes=[
            pltpu.VMEM((samples, stations), jnp.float32),
        ],
    )(own_pick, far_pick, sub_at, own_spec, own_energy[:, None, :], mask[:, None, :], *inverse,
      *pieces, *([prior] if prior is not None else []))


def spectra(forward, wide):
    samples = forward.shape[1]
    return jnp.einsum(
        "jt,ects->ecjs", forward[:, LAG:samples - LAG], wide, precision=lax.Precision.HIGH
    )


def by_xor(value, axis, flip):
    length = lax.axis_size(axis)
    return lax.ppermute(value, axis, [(i, i ^ flip) for i in range(length)])


def shards(waves, local_event, partner_event, station_mask):
    events, comps, samples, stations = waves.shape
    forward = forward_table(samples)
    table = inverse_table(samples, LAG)
    table_high = lax.reduce_precision(table, exponent_bits=8, mantissa_bits=7)
    inverse = (table_high.astype(jnp.bfloat16), (table - table_high).astype(jnp.bfloat16))
    region_len = lax.axis_size("region")
    sub_at = lax.axis_index("sub")

    inner = waves[:, :, LAG:samples - LAG, :]
    meta = jnp.concatenate(
        [station_mask[:, 1], local_event[:, 1:2], partner_event[:, 1:2]], axis=1
    )
    inner_wide = inner.astype(jnp.float32)
    inner_energy = jnp.sum(inner_wide * inner_wide, axis=(1, 2))
    sent_inner, sent_meta, sent_energy = lax.ppermute(
        (inner, meta, inner_energy), "region",
        [(i, (i - 1) % region_len) for i in range(region_len)],
    )

    wide = waves.astype(jnp.float32)
    spec = jnp.einsum("jt,ects->ecjs", forward, wide, precision=lax.Precision.HIGH)
    full_energy = jnp.sum(wide * wide, axis=(1, 2))
    body = spec.astype(jnp.bfloat16).reshape(events, comps * samples, stations)
    pieces = split_exact(full_energy)
    tail = jnp.pad(pieces, ((0, 0), (0, 16 - pieces.shape[1]), (0, 0)))
    packed = jnp.concatenate([body, tail], axis=1)

    near = by_xor(packed, "sub", 1)
    across = by_xor(packed, "sub", 2)
    pieces = [packed, near, across, None]
    sub_vec = jnp.full((1,), sub_at, jnp.int32)

    def prepare(own_inner, own_energy):
        return spectra(forward, own_inner.astype(jnp.float32)), own_energy

    def run(prepared, own_pick, far_pick, mask, allowed=(0, 1, 2, 3), prior=None,
            out_dtype=jnp.float32):
        own_spec, own_energy = prepared
        own_pick = jnp.clip(own_pick, 0, events - 1)
        far_pick = jnp.clip(far_pick, 0, len(pieces) * events - 1)
        return correlate_round(
            own_spec, own_energy, tuple(pieces[j] for j in allowed), allowed, inverse,
            mask.astype(jnp.float32), own_pick, far_pick, sub_vec, prior, out_dtype,
        )

    own_args = (prepare(inner, inner_energy), local_event[:, 0], partner_event[:, 0])
    sent_meta, sent_energy, own_mask = lax.optimization_barrier(
        (sent_meta, sent_energy, station_mask[:, 0])
    )
    mine = run(*own_args, own_mask, allowed=(0, 1))
    across, mine = lax.optimization_barrier((across, mine))
    pieces[2] = across
    ahead_spec = prepare(sent_inner, sent_energy)
    pieces[3], ahead_spec = lax.optimization_barrier((by_xor(across, "sub", 1), ahead_spec))

    ahead_pick = sent_meta[:, stations]
    ahead_far = sent_meta[:, stations + 1]
    ahead_mask = sent_meta[:, :stations]
    count = ahead_pick.shape[0]
    split = count * 5 // 8
    back = []
    for lo, hi in ((0, split), (split, count)):
        back.append(run(ahead_spec, ahead_pick[lo:hi], ahead_far[lo:hi], ahead_mask[lo:hi],
                        out_dtype=jnp.bfloat16))
    back[-1], own_mask = lax.optimization_barrier((back[-1], own_mask))
    back = [
        lax.ppermute(part, "region", [(i, (i + 1) % region_len) for i in range(region_len)])
        for part in back
    ]
    mine = run(*own_args, own_mask, allowed=(2, 3), prior=mine)
    return jnp.stack([mine, jnp.concatenate(back, axis=0).astype(jnp.float32)], axis=1)


def solution(mesh):
    placed = (
        P(("region", "sub"), None, None, None),
        P(("region", "sub"), None),
        P(("region", "sub"), None),
        P(("region", "sub"), None, None),
    )
    return jax.shard_map(
        shards,
        mesh=mesh,
        in_specs=placed,
        out_specs=P(("region", "sub"), None, None, None),
        check_vma=False,
    )
```
